32 devices in a mesh: gx: 8 (over y, x, core), gy: 4 (over z).
Axes of the slice: x: 2, y: 2, z: 4, core: 2. Of those that a mesh axis runs over, the one named last changes fastest.
Arguments:
- temp_start: float32 [8, 1024, 2048], P(None, ('gx', 'gy')), may hold values from -6 to 6
- heat_input: float32 [8, 1024, 2048], P(None, ('gx', 'gy')), may hold values from -3 to 3
- lateral: float32 [8], replicated, may hold values from 0.03 to 0.15
- vertical: float32 [7], replicated, may hold values from 0.03 to 0.15
- weighting: float32 [8], replicated, may hold values from -1 to 1
- modulus: float32 [1024, 2048], P('gx', 'gy'), may hold values from 0.3 to 3
- warp_prev: float32 [1024, 2048], P('gx', 'gy'), may hold values from -6 to 6
- joint_cell: int32 [65536], P(('gx', 'gy')), may hold values from 0 to 65535
- joint_owner: int32 [65536, 1], P(('gx', 'gy')), may hold values from 0 to 31; in each aligned block of 2048 rows (0 to 2047, 2048 to 4095, ...) at most 192 rows name the same one
- joint_strain: float32 [2, 32, 6144], P(None, ('gx', 'gy')), may hold values from -4 to 4
- joint_resist: float32 [32, 6144], P(('gx', 'gy')), may hold values from 1 to 2
Outputs:
- warpage: float32 [1024, 2048], P('gx', 'gy')
- strain_next: float32 [2, 32, 6144], P(None, ('gx', 'gy'))
- resist_next: float32 [32, 6144], P(('gx', 'gy'))
The draws below stay inside these ranges and needn't reach their ends.
Inputs may be any that keep to these rules, and one draw needn't show every extreme that they name: `joint_owner`: among the 2048 joints of one device at most 192 have the same owner, and on some device exactly 192 do.
All inputs are finite; a program needn't handle non-finite values.
Results may differ from the reference program's by a relative error of at most 0.0003.
Values sent between devices are 32-bit elements; how exact they have to be, the bound alone decides.
No kernel may reach another device: no remote copies, remote signals or barrier semaphores. Data moves between devices by JAX's collectives and lax.ppermute only.
A program may use at most 320 MiB of HBM per device.

```python
import math
import jax
import jax.numpy as jnp
import numpy as np
from jax import lax

CM = 512
LAYERS = 8
STEPS = 2
SWEEPS = 3
JPD = 2048
RM = 128
NR = 1024
C = 2048
JOINTS = 65536
CAP = 192
N_GX = 8
N_GY = 4


def place_ends(values, own_key, low, high):
    shape = values.shape
    place = [jax.random.randint(jax.random.fold_in(own_key, axis), (), 0, shape[axis]) for axis in range(len(shape))]
    values = values.at[tuple(place)].set(low)
    longest = shape.index(max(shape))
    place[longest] = (place[longest] + 1) % shape[longest]
    return values.at[tuple(place)].set(high)


def levels(key, dims, pieces, smallest, largest):
    level, own = 1.0, jax.random.fold_in(key, 6)
    for axis_at, parts in pieces:
        heights = jnp.exp(jax.random.uniform(jax.random.fold_in(own, axis_at), (parts,), jnp.float32, smallest / len(pieces), largest / len(pieces)))
        level = level * jnp.repeat(heights, dims[axis_at] // parts).reshape([-1 if axis == axis_at else 1 for axis in range(len(dims))])
    return level


def deal_out(key, own, number, rows, amount, top, most, lean):
    order = jax.random.permutation(key, amount)
    crowded, ordinary = portions_of(amount, rows * top, most, lean, True), portions_of(amount, rows * top, most, lean, False)
    places = jnp.arange(amount)

    def named(lengths, offset_by):
        used = int((lengths > 0).sum())
        fixed = max(1, used // 4)
        shifted = fixed + (places - fixed + offset_by * (used - fixed)) % max(1, amount - fixed)
        return jnp.zeros((amount,), jnp.int32).at[order[jnp.where(places < fixed, places, shifted)]].set(jnp.asarray(lengths, jnp.int32))

    lengths = jnp.where(number % 4 == 0, named(crowded, number // 4), named(ordinary, number - number // 4 - 1))
    mixed = jax.random.permutation(jax.random.fold_in(own, 3), amount)
    giver, taker = mixed[0:amount // 2 * 2:2], mixed[1:amount // 2 * 2:2]
    slack = jnp.minimum(lengths[giver] - 1, most - lengths[taker]) // 2
    slack = jnp.where((giver == order[0]) | (taker == order[0]) | (lengths[taker] == 0), 0, jnp.maximum(slack, 0))
    shifted = jax.random.randint(jax.random.fold_in(own, 4), (amount // 2,), 0, 1 << 20) % (slack + 1)
    lengths = lengths.at[giver].add(-shifted).at[taker].add(shifted)
    labels = jnp.searchsorted(jnp.cumsum(lengths), jnp.arange(rows * top), side="right").astype(jnp.int32)
    table = labels.reshape(top, rows).T
    table = table[jax.random.permutation(jax.random.fold_in(own, 1), rows)]
    offset_by = jax.random.randint(jax.random.fold_in(own, 2), (rows, 1), 0, top)
    return jnp.take_along_axis(table, (jnp.arange(top)[None, :] + offset_by) % top, axis=1)


def portions_of(number_of, total, most, lean, full):
    portions = [(1 << 20) // math.isqrt(rank ** lean) + 1 for rank in range(1, number_of + 1)]
    largest = most if full else min(most, max(-(-total // number_of), total * portions[0] // sum(portions)))
    least = 1 if total - largest >= number_of - 1 else 0
    given, surplus = [largest] + [least] * (number_of - 1), total - largest - least * (number_of - 1)
    while surplus > 0:
        free = [i for i in range(1, number_of) if given[i] < largest] or [i for i in range(1, number_of) if given[i] < most]
        pool, remaining = sum([portions[i] for i in free]), surplus
        for i in free:
            addition = min(most - given[i], max(1, remaining * portions[i] // pool), surplus)
            given[i] = given[i] + addition
            surplus = surplus - addition
    return np.array(given)


def gaussian(own_key, shape, scale, bound, split=(), held_as=jnp.bfloat16):
    entries = scale * jax.random.normal(own_key, shape, jnp.float32)
    if split:
        entries = entries * levels(own_key, shape, split, -0.22, 0.18)
    return jnp.clip(entries, -bound, bound).astype(held_as)


def setup_inputs(seed: int = 0) -> dict:
    streams_of = jax.random.split(jax.random.key(seed), 12)
    temp_start = gaussian(streams_of[0], (LAYERS, NR, C), 1.0, 6.0, ((1, 32),), jnp.float32)
    heat_input = gaussian(streams_of[1], (LAYERS, NR, C), 0.2, 3.0, ((1, 32),), jnp.float32)
    lateral = jnp.clip(jnp.exp(jax.random.uniform(streams_of[2], (LAYERS,), jnp.float32, math.log(0.03), math.log(0.15))), 0.03, 0.15)
    vertical = jnp.clip(jnp.exp(jax.random.uniform(streams_of[3], (LAYERS - 1,), jnp.float32, math.log(0.03), math.log(0.15))), 0.03, 0.15)
    weighting = jnp.clip(jax.random.uniform(streams_of[4], (LAYERS,), jnp.float32, -1.0, 1.0), -1.0, 1.0)
    modulus = jnp.clip(jnp.exp(math.log(3.0) - 2.3025851 * jax.random.uniform(streams_of[5], (NR, C), jnp.float32) ** levels(streams_of[5], (NR, C), ((0, 8), (1, 4)), -0.2, 0.2)), 0.3, 3.0)
    warp_prev = gaussian(streams_of[6], (NR, C), 0.5, 6.0, ((0, 8), (1, 4)), jnp.float32)
    joint_cell = place_ends(jax.random.randint(streams_of[7], (JOINTS,), 0, RM * CM), jax.random.fold_in(streams_of[7], 1), 0, (RM * CM) - 1).astype(jnp.int32)
    joint_owner_keys = jax.random.split(jax.random.fold_in(streams_of[8], 1), JOINTS // JPD)
    joint_owner_turns = jax.random.permutation(jax.random.fold_in(streams_of[8], 3), JOINTS // JPD)
    joint_owner = jax.vmap(lambda own, number: deal_out(jax.random.fold_in(streams_of[8], 2), own, number, JPD, N_GX * N_GY, 1, CAP, 2))(joint_owner_keys, joint_owner_turns).reshape((JOINTS, 1))
    joint_strain = gaussian(streams_of[9], (2, N_GX * N_GY, N_GX * N_GY * CAP), 0.3, 4.0, ((1, 32),), jnp.float32)
    joint_resist = jnp.clip(1.0 + 1.0 * jax.random.uniform(streams_of[10], (N_GX * N_GY, N_GX * N_GY * CAP), jnp.float32) ** levels(streams_of[10], (N_GX * N_GY, N_GX * N_GY * CAP), ((0, 32),), -0.2, 0.2), 1.0, 2.0)
    return dict(temp_start=temp_start, heat_input=heat_input, lateral=lateral, vertical=vertical, weighting=weighting, modulus=modulus, warp_prev=warp_prev, joint_cell=joint_cell, joint_owner=joint_owner, joint_strain=joint_strain, joint_resist=joint_resist)


stiffness = 0.2
shear_mod = 0.6
rate_scale = 0.5
sat_level = 2.5
sat_power = 0.3
harden = 2.0


def thermal_step(ext, heat_rows, lateral, vertical):
    cols = jnp.pad(ext, ((0, 0), (0, 0), (1, 1)))
    center = ext[:, 1:-1]
    lap = ext[:, 2:] + ext[:, :-2] + cols[:, 1:-1, 2:] + cols[:, 1:-1, :-2] - 4.0 * center
    flux = vertical[:, None, None] * (center[1:] - center[:-1])
    vert = jnp.pad(flux, ((0, 1), (0, 0), (0, 0))) - jnp.pad(flux, ((1, 0), (0, 0), (0, 0)))
    return center + lateral[:, None, None] * lap + vert + heat_rows


def moment_of(field, weighting):
    total = weighting[0] * field[0]
    for layer in range(1, field.shape[0]):
        total = total + weighting[layer] * field[layer]
    return total


def sweep(w_pad, e_pad, load):
    center = e_pad[1:-1, 1:-1]
    e_up = 0.5 * (center + e_pad[:-2, 1:-1])
    e_down = 0.5 * (center + e_pad[2:, 1:-1])
    e_left = 0.5 * (center + e_pad[1:-1, :-2])
    e_right = 0.5 * (center + e_pad[1:-1, 2:])
    numer = load + e_up * w_pad[:-2, 1:-1] + e_down * w_pad[2:, 1:-1] + e_left * w_pad[1:-1, :-2] + e_right * w_pad[1:-1, 2:]
    denom = stiffness + e_up + e_down + e_left + e_right
    return numer / denom


def pack_joints(cells, owners, warp_flat, prev_flat, top_flat, devices, cap):
    increment = warp_flat[cells] - prev_flat[cells]
    theta = top_flat[cells]
    values = jnp.stack([increment, theta, jnp.ones_like(theta)])
    onehot = (owners[:, None] == jnp.arange(devices, dtype=jnp.int32)[None, :]).astype(jnp.int32)
    ranks = jnp.sum(jnp.cumsum(onehot, axis=0) * onehot, axis=1) - 1
    slots = (owners * cap + ranks).astype(jnp.int32)
    return jnp.zeros((3, devices * cap), jnp.float32).at[:, slots].set(values)


def anand(strain, resist, recv):
    total, inelastic = strain[0], strain[1]
    increment, theta, live = recv[0], recv[1], recv[2]
    total_new = total + increment
    arrhen = jnp.exp(2.0 - 2.0 / (1.0 + 0.1 * theta * theta))
    hyper = jnp.sinh(shear_mod * (total_new - inelastic) / resist)
    rate = rate_scale * arrhen * hyper * jnp.abs(hyper)
    inelastic_new = inelastic + rate
    target = sat_level * jnp.power(1.0 + jnp.abs(rate) / arrhen, sat_power)
    resist_new = resist + harden * (1.0 - resist / target) * jnp.abs(rate)
    keep = live > 0.5
    strain_out = jnp.stack([jnp.where(keep, total_new, total), jnp.where(keep, inelastic_new, inelastic)])
    return strain_out, jnp.where(keep, resist_new, resist)


def as_tiles(field):
    return field.reshape(N_GX, RM, N_GY, CM).transpose(0, 2, 1, 3).reshape(N_GX * N_GY, RM * CM)


def reference(temp_start, heat_input, lateral, vertical, weighting, modulus, warp_prev, joint_cell, joint_owner, joint_strain, joint_resist):
    temp = temp_start
    for step in range(STEPS):
        ext = jnp.pad(temp, ((0, 0), (1, 1), (0, 0)))
        temp = thermal_step(ext, heat_input, lateral, vertical)
    load = moment_of(temp, weighting)
    top = temp[-1]
    e_pad = jnp.pad(modulus, 1)
    warp = warp_prev
    for step in range(SWEEPS):
        warp = sweep(jnp.pad(warp, 1), e_pad, load)
    devices = N_GX * N_GY
    warp_tiles = as_tiles(warp)
    prev_tiles = as_tiles(warp_prev)
    top_tiles = as_tiles(top)
    cells = joint_cell.reshape(devices, JPD)
    owners = joint_owner.reshape(devices, JPD)

    def one_source(args):
        return pack_joints(args[0], args[1], args[2], args[3], args[4], devices, CAP)

    sent = lax.map(one_source, (cells, owners, warp_tiles, prev_tiles, top_tiles))
    recv = sent.reshape(devices, 3, devices, CAP).transpose(1, 2, 0, 3).reshape(3, devices, devices * CAP)
    strain_next, resist_next = anand(joint_strain, joint_resist, recv)
    return warp, strain_next, resist_next
```

```python
import jax
import jax.numpy as jnp
from jax import lax
from jax.sharding import PartitionSpec as P

STEPS = 2
SWEEPS = 3


stiffness = 0.2
shear_mod = 0.6
rate_scale = 0.5
sat_level = 2.5
sat_power = 0.3
harden = 2.0

FLAT = ("gx", "gy")


def exchange(last, leading, axis):
    count = lax.axis_size(axis)
    up = [(i, i + 1) for i in range(count - 1)]
    down = [(j, i) for i, j in up]
    return lax.ppermute(last, axis, up), lax.ppermute(leading, axis, down)


def with_halo(array, sides, width):
    for axis, dim in sides:
        length = array.shape[dim]
        last = lax.slice_in_dim(array, length - width, length, axis=dim)
        leading = lax.slice_in_dim(array, 0, width, axis=dim)
        before, after = exchange(last, leading, axis)
        array = jnp.concatenate([before, array, after], axis=dim)
    return array


def thermal_step(ext, heat_rows, lateral, vertical):
    cols = jnp.pad(ext, ((0, 0), (0, 0), (1, 1)))
    center = ext[:, 1:-1]
    lap = ext[:, 2:] + ext[:, :-2] + cols[:, 1:-1, 2:] + cols[:, 1:-1, :-2] - 4.0 * center
    flux = vertical[:, None, None] * (center[1:] - center[:-1])
    vert = jnp.pad(flux, ((0, 1), (0, 0), (0, 0))) - jnp.pad(flux, ((1, 0), (0, 0), (0, 0)))
    return center + lateral[:, None, None] * lap + vert + heat_rows


def moment_of(field, weighting):
    total = weighting[0] * field[0]
    for layer in range(1, field.shape[0]):
        total = total + weighting[layer] * field[layer]
    return total


def sweep(w_pad, e_pad, load):
    center = e_pad[1:-1, 1:-1]
    e_up = 0.5 * (center + e_pad[:-2, 1:-1])
    e_down = 0.5 * (center + e_pad[2:, 1:-1])
    e_left = 0.5 * (center + e_pad[1:-1, :-2])
    e_right = 0.5 * (center + e_pad[1:-1, 2:])
    numer = (
        load
        + e_up * w_pad[:-2, 1:-1]
        + e_down * w_pad[2:, 1:-1]
        + e_left * w_pad[1:-1, :-2]
        + e_right * w_pad[1:-1, 2:]
    )
    denom = stiffness + e_up + e_down + e_left + e_right
    return numer / denom


def anand(strain, resist, recv):
    total, inelastic = (strain[0], strain[1])
    increment, theta, live = (recv[0], recv[1], recv[2])
    total_new = total + increment
    arrhen = jnp.exp(2.0 - 2.0 / (1.0 + 0.1 * theta * theta))
    hyper = jnp.sinh(shear_mod * (total_new - inelastic) / resist)
    rate = rate_scale * arrhen * hyper * jnp.abs(hyper)
    inelastic_new = inelastic + rate
    target = sat_level * jnp.power(1.0 + jnp.abs(rate) / arrhen, sat_power)
    resist_new = resist + harden * (1.0 - resist / target) * jnp.abs(rate)
    keep = live > 0.5
    strain_out = jnp.stack(
        [jnp.where(keep, total_new, total), jnp.where(keep, inelastic_new, inelastic)]
    )
    return (strain_out, jnp.where(keep, resist_new, resist))


def thermal(temp, heat, lateral, vertical):
    devices = lax.axis_size(FLAT)
    t = lax.axis_index(FLAT)
    rows = temp.shape[1]
    h = STEPS
    last = jnp.concatenate([temp[:, rows - h:], heat[:, rows - (h - 1):]], axis=1)
    leading = jnp.concatenate([temp[:, :h], heat[:, : h - 1]], axis=1)
    before, after = exchange(last, leading, FLAT)
    ext = jnp.concatenate([before[:, :h], temp, after[:, :h]], axis=1)
    heat_ext = jnp.concatenate([before[:, h:], heat, after[:, h:]], axis=1)
    for step in range(1, STEPS + 1):
        r = STEPS - step
        heat_rows = heat_ext[:, h - 1 - r: h - 1 - r + rows + 2 * r]
        ext = thermal_step(ext, heat_rows, lateral, vertical)
        if r > 0:
            g = t * rows + jnp.arange(-r, rows + r)
            inside = (g >= 0) & (g < devices * rows)
            ext = jnp.where(inside[None, :, None], ext, 0.0)
    return ext


def relay(load, top, width):
    n_gy = lax.axis_size("gy")
    rows, cols = load.shape
    cm = cols // n_gy
    before, after = exchange(load[rows - width:], load[:width], FLAT)
    load_ext = jnp.concatenate([before, load, after], axis=0)
    lp = jnp.pad(load_ext, ((0, 0), (width, width)))
    tp = jnp.pad(top, ((width, width), (width, width)))
    both = jnp.stack([lp, tp])
    send = jnp.stack([both[:, :, k * cm: k * cm + cm + 2 * width] for k in range(n_gy)])
    recv = lax.all_to_all(send, "gy", split_axis=0, concat_axis=0, tiled=True)
    parts = []
    for k in range(n_gy):
        lo = 0 if k == 0 else width
        hi = rows + 2 * width if k == n_gy - 1 else rows + width
        parts.append(recv[k, 0, lo:hi])
    load_m = jnp.concatenate(parts, axis=0)
    top_m = jnp.concatenate(
        [recv[k, 1, width: rows + width, width: cm + width] for k in range(n_gy)], axis=0
    )
    return load_m, top_m


def joint_ranks(owners, devices):
    count = owners.shape[0]
    block = 128 if count % 128 == 0 else count
    nb = count // block
    onehot = (owners[:, None] == jnp.arange(devices, dtype=jnp.int32)[None, :]).astype(jnp.float32)
    oh = onehot.reshape(nb, block, devices)
    ar = jnp.arange(block)
    tri = (ar[:, None] >= ar[None, :]).astype(jnp.float32)
    within = jnp.einsum("ij,bjd->bid", tri, oh, precision=lax.Precision.HIGHEST)
    totals = within[:, -1, :]
    ab = jnp.arange(nb)
    stri = (ab[:, None] > ab[None, :]).astype(jnp.float32)
    offs = jnp.dot(stri, totals, precision=lax.Precision.HIGHEST)
    cum = (within + offs[:, None, :]).reshape(count, devices)
    return jnp.sum(cum * onehot, axis=1).astype(jnp.int32) - 1


def body(
    temp_start,
    heat_input,
    lateral,
    vertical,
    weighting,
    modulus,
    warp_prev,
    joint_cell,
    joint_owner,
    joint_strain,
    joint_resist,
):
    devices = lax.axis_size(FLAT)
    n_gx, n_gy = lax.axis_size("gx"), lax.axis_size("gy")
    gi, gj = lax.axis_index("gx"), lax.axis_index("gy")
    rm, cm = warp_prev.shape

    wm = with_halo(jnp.stack([warp_prev, modulus]), (("gx", 1), ("gy", 2)), SWEEPS)
    owners = joint_owner[:, 0]
    capacity = joint_resist.shape[1] // devices
    slots = owners * capacity + joint_ranks(owners, devices)

    temp = thermal(temp_start, heat_input, lateral, vertical)
    load_t = moment_of(temp, weighting)
    load, top = relay(load_t, temp[-1], SWEEPS - 1)

    warp = wm[0]
    mod_ext = wm[1]
    for step in range(1, SWEEPS + 1):
        r = SWEEPS - step
        off = SWEEPS - (r + 1)
        e_pad = mod_ext[off: off + rm + 2 * r + 2, off: off + cm + 2 * r + 2]
        lo = SWEEPS - 1 - r
        ld = load[lo: lo + rm + 2 * r, lo: lo + cm + 2 * r]
        warp = sweep(warp, e_pad, ld)
        if r > 0:
            gr = gi * rm + jnp.arange(-r, rm + r)
            gc = gj * cm + jnp.arange(-r, cm + r)
            inside = ((gr >= 0) & (gr < n_gx * rm))[:, None] & ((gc >= 0) & (gc < n_gy * cm))[None, :]
            warp = jnp.where(inside, warp, 0.0)

    fields = jnp.stack([(warp - warp_prev).reshape(-1), top.reshape(-1)])
    picked = fields[:, joint_cell]
    values = jnp.concatenate([picked, jnp.ones_like(picked[:1])], axis=0)
    outgoing = jnp.zeros((3, devices * capacity), jnp.float32).at[:, slots].set(values)
    incoming = lax.all_to_all(outgoing, FLAT, split_axis=1, concat_axis=1, tiled=True)
    strain_next, resist_next = anand(joint_strain, joint_resist, incoming[:, None, :])
    return (warp, strain_next, resist_next)


def solution(mesh):
    return jax.shard_map(
        body,
        mesh=mesh,
        in_specs=(
            P(None, FLAT, None),
            P(None, FLAT, None),
            P(),
            P(),
            P(),
            P("gx", "gy"),
            P("gx", "gy"),
            P(FLAT),
            P(FLAT, None),
            P(None, FLAT, None),
            P(FLAT, None),
        ),
        out_specs=(P("gx", "gy"), P(None, FLAT, None), P(FLAT, None)),
        check_vma=False,
    )
```

```python
import jax
import jax.numpy as jnp
from jax import lax
from jax.sharding import PartitionSpec as P
from jax.experimental import pallas as pl

STEPS = 2
SWEEPS = 3


stiffness = 0.2
shear_mod = 0.6
rate_scale = 0.5
sat_level = 2.5
sat_power = 0.3
harden = 2.0

FLAT = ("gx", "gy")


def exchange(last, leading, axis):
    count = lax.axis_size(axis)
    up = [(i, i + 1) for i in range(count - 1)]
    down = [(j, i) for i, j in up]
    return lax.ppermute(last, axis, up), lax.ppermute(leading, axis, down)


def with_halo(array, sides, width):
    for axis, dim in sides:
        length = array.shape[dim]
        last = lax.slice_in_dim(array, length - width, length, axis=dim)
        leading = lax.slice_in_dim(array, 0, width, axis=dim)
        before, after = exchange(last, leading, axis)
        array = jnp.concatenate([before, array, after], axis=dim)
    return array


def thermal_step(ext, heat_rows, lateral, vertical):
    cols = jnp.pad(ext, ((0, 0), (0, 0), (1, 1)))
    center = ext[:, 1:-1]
    lap = ext[:, 2:] + ext[:, :-2] + cols[:, 1:-1, 2:] + cols[:, 1:-1, :-2] - 4.0 * center
    flux = vertical[:, None, None] * (center[1:] - center[:-1])
    vert = jnp.pad(flux, ((0, 1), (0, 0), (0, 0))) - jnp.pad(flux, ((1, 0), (0, 0), (0, 0)))
    return center + lateral[:, None, None] * lap + vert + heat_rows


def moment_of(field, weighting):
    total = weighting[0] * field[0]
    for layer in range(1, field.shape[0]):
        total = total + weighting[layer] * field[layer]
    return total


def sweep(w_pad, e_pad, load):
    center = e_pad[1:-1, 1:-1]
    e_up = 0.5 * (center + e_pad[:-2, 1:-1])
    e_down = 0.5 * (center + e_pad[2:, 1:-1])
    e_left = 0.5 * (center + e_pad[1:-1, :-2])
    e_right = 0.5 * (center + e_pad[1:-1, 2:])
    numer = (
        load
        + e_up * w_pad[:-2, 1:-1]
        + e_down * w_pad[2:, 1:-1]
        + e_left * w_pad[1:-1, :-2]
        + e_right * w_pad[1:-1, 2:]
    )
    denom = stiffness + e_up + e_down + e_left + e_right
    return numer / denom


def anand(strain, resist, recv):
    total, inelastic = (strain[0], strain[1])
    increment, theta, live = (recv[0], recv[1], recv[2])
    total_new = total + increment
    arrhen = jnp.exp(2.0 - 2.0 / (1.0 + 0.1 * theta * theta))
    hyper = jnp.sinh(shear_mod * (total_new - inelastic) / resist)
    rate = rate_scale * arrhen * hyper * jnp.abs(hyper)
    inelastic_new = inelastic + rate
    target = sat_level * jnp.power(1.0 + jnp.abs(rate) / arrhen, sat_power)
    resist_new = resist + harden * (1.0 - resist / target) * jnp.abs(rate)
    keep = live > 0.5
    strain_out = jnp.stack(
        [jnp.where(keep, total_new, total), jnp.where(keep, inelastic_new, inelastic)]
    )
    return (strain_out, jnp.where(keep, resist_new, resist))


def thermal(temp, heat, lateral, vertical):
    devices = lax.axis_size(FLAT)
    t = lax.axis_index(FLAT)
    rows = temp.shape[1]
    h = STEPS
    last = jnp.concatenate([temp[:, rows - h:], heat[:, rows - (h - 1):]], axis=1)
    leading = jnp.concatenate([temp[:, :h], heat[:, : h - 1]], axis=1)
    before, after = exchange(last, leading, FLAT)
    ext = jnp.concatenate([before[:, :h], temp, after[:, :h]], axis=1)
    heat_ext = jnp.concatenate([before[:, h:], heat, after[:, h:]], axis=1)
    for step in range(1, STEPS + 1):
        r = STEPS - step
        heat_rows = heat_ext[:, h - 1 - r: h - 1 - r + rows + 2 * r]
        ext = thermal_step(ext, heat_rows, lateral, vertical)
        if r > 0:
            g = t * rows + jnp.arange(-r, rows + r)
            inside = (g >= 0) & (g < devices * rows)
            ext = jnp.where(inside[None, :, None], ext, 0.0)
    return ext


def relay(load, top, width):
    n_gy = lax.axis_size("gy")
    rows, cols = load.shape
    cm = cols // n_gy
    before, after = exchange(load[rows - width:], load[:width], FLAT)
    load_ext = jnp.concatenate([before, load, after], axis=0)
    lp = jnp.pad(load_ext, ((0, 0), (width, width)))
    tp = jnp.pad(top, ((width, width), (width, width)))
    both = jnp.stack([lp, tp])
    send = jnp.stack([both[:, :, k * cm: k * cm + cm + 2 * width] for k in range(n_gy)])
    recv = lax.all_to_all(send, "gy", split_axis=0, concat_axis=0, tiled=True)
    parts = []
    for k in range(n_gy):
        lo = 0 if k == 0 else width
        hi = rows + 2 * width if k == n_gy - 1 else rows + width
        parts.append(recv[k, 0, lo:hi])
    load_m = jnp.concatenate(parts, axis=0)
    top_m = jnp.concatenate(
        [recv[k, 1, width: rows + width, width: cm + width] for k in range(n_gy)], axis=0
    )
    return load_m, top_m


def joint_ranks(owners, devices):
    count = owners.shape[0]
    block = 128 if count % 128 == 0 else count
    nb = count // block
    onehot = (owners[:, None] == jnp.arange(devices, dtype=jnp.int32)[None, :]).astype(jnp.float32)
    oh = onehot.reshape(nb, block, devices)
    ar = jnp.arange(block)
    tri = (ar[:, None] >= ar[None, :]).astype(jnp.float32)
    within = jnp.einsum("ij,bjd->bid", tri, oh, precision=lax.Precision.HIGHEST)
    totals = within[:, -1, :]
    ab = jnp.arange(nb)
    stri = (ab[:, None] > ab[None, :]).astype(jnp.float32)
    offs = jnp.dot(stri, totals, precision=lax.Precision.HIGHEST)
    cum = (within + offs[:, None, :]).reshape(count, devices)
    return jnp.sum(cum * onehot, axis=1).astype(jnp.int32) - 1


def pick_kernel(rc_ref, parts_ref, out_ref):
    rc = rc_ref[...]
    rows = rc[:, 0:1]
    cols = rc[:, 1:2]
    block = rc.shape[0]
    _, rm, width = parts_ref.shape
    fields = out_ref.shape[1]
    cm = width // fields
    hit = rows == lax.broadcasted_iota(jnp.int32, (block, rm), 1)
    onehot = jnp.where(hit, 1.0, 0.0).astype(jnp.bfloat16)
    acc = jnp.dot(onehot, parts_ref[0], preferred_element_type=jnp.float32)
    acc = acc + jnp.dot(onehot, parts_ref[1], preferred_element_type=jnp.float32)
    acc = acc + jnp.dot(onehot, parts_ref[2], preferred_element_type=jnp.float32)
    lane = cols == lax.broadcasted_iota(jnp.int32, (block, cm), 1)
    for f in range(fields):
        seg = acc[:, f * cm: (f + 1) * cm]
        out_ref[:, f: f + 1] = jnp.sum(jnp.where(lane, seg, 0.0), axis=1, keepdims=True)


def pick_cells(fields, cells):
    count = cells.shape[0]
    nf, rm, cm = fields.shape
    wide = jnp.concatenate(list(fields), axis=1)
    hi = lax.reduce_precision(wide, exponent_bits=8, mantissa_bits=7)
    rest = wide - hi
    mid = lax.reduce_precision(rest, exponent_bits=8, mantissa_bits=7)
    lo = rest - mid
    parts = jnp.stack([hi, mid, lo]).astype(jnp.bfloat16)
    rc = jnp.stack([cells // cm, cells % cm], axis=1).astype(jnp.int32)
    block = 256 if count % 256 == 0 else count
    picked = pl.pallas_call(
        pick_kernel,
        grid=(count // block,),
        in_specs=[
            pl.BlockSpec((block, 2), lambda i: (i, 0)),
            pl.BlockSpec((3, rm, nf * cm), lambda i: (0, 0, 0)),
        ],
        out_specs=pl.BlockSpec((block, nf), lambda i: (i, 0)),
        out_shape=jax.ShapeDtypeStruct((count, nf), jnp.float32),
    )(rc, parts)
    return picked.T


def body(
    temp_start,
    heat_input,
    lateral,
    vertical,
    weighting,
    modulus,
    warp_prev,
    joint_cell,
    joint_owner,
    joint_strain,
    joint_resist,
):
    devices = lax.axis_size(FLAT)
    n_gx, n_gy = lax.axis_size("gx"), lax.axis_size("gy")
    gi, gj = lax.axis_index("gx"), lax.axis_index("gy")
    rm, cm = warp_prev.shape

    wm = with_halo(jnp.stack([warp_prev, modulus]), (("gx", 1), ("gy", 2)), SWEEPS)
    owners = joint_owner[:, 0]
    capacity = joint_resist.shape[1] // devices
    slots = owners * capacity + joint_ranks(owners, devices)

    temp = thermal(temp_start, heat_input, lateral, vertical)
    load_t = moment_of(temp, weighting)
    load, top = relay(load_t, temp[-1], SWEEPS - 1)

    warp = wm[0]
    mod_ext = wm[1]
    for step in range(1, SWEEPS + 1):
        r = SWEEPS - step
        off = SWEEPS - (r + 1)
        e_pad = mod_ext[off: off + rm + 2 * r + 2, off: off + cm + 2 * r + 2]
        lo = SWEEPS - 1 - r
        ld = load[lo: lo + rm + 2 * r, lo: lo + cm + 2 * r]
        warp = sweep(warp, e_pad, ld)
        if r > 0:
            gr = gi * rm + jnp.arange(-r, rm + r)
            gc = gj * cm + jnp.arange(-r, cm + r)
            inside = ((gr >= 0) & (gr < n_gx * rm))[:, None] & ((gc >= 0) & (gc < n_gy * cm))[None, :]
            warp = jnp.where(inside, warp, 0.0)

    picked = pick_cells(jnp.stack([warp - warp_prev, top]), joint_cell)
    values = jnp.concatenate([picked, jnp.ones_like(picked[:1])], axis=0)
    outgoing = jnp.zeros((3, devices * capacity), jnp.float32).at[:, slots].set(values)
    incoming = lax.all_to_all(outgoing, FLAT, split_axis=1, concat_axis=1, tiled=True)
    strain_next, resist_next = anand(joint_strain, joint_resist, incoming[:, None, :])
    return (warp, strain_next, resist_next)


def solution(mesh):
    return jax.shard_map(
        body,
        mesh=mesh,
        in_specs=(
            P(None, FLAT, None),
            P(None, FLAT, None),
            P(),
            P(),
            P(),
            P("gx", "gy"),
            P("gx", "gy"),
            P(FLAT),
            P(FLAT, None),
            P(None, FLAT, None),
            P(FLAT, None),
        ),
        out_specs=(P("gx", "gy"), P(None, FLAT, None), P(FLAT, None)),
        check_vma=False,
    )
```

```python
import jax
import jax.numpy as jnp
from jax import lax
from jax.sharding import PartitionSpec as P
from jax.experimental import pallas as pl

STEPS = 2
SWEEPS = 3


stiffness = 0.2
shear_mod = 0.6
rate_scale = 0.5
sat_level = 2.5
sat_power = 0.3
harden = 2.0

FLAT = ("gx", "gy")


def exchange(last, leading, axis):
    count = lax.axis_size(axis)
    up = [(i, i + 1) for i in range(count - 1)]
    down = [(j, i) for i, j in up]
    return lax.ppermute(last, axis, up), lax.ppermute(leading, axis, down)


def with_halo(array, sides, width):
    for axis, dim in sides:
        length = array.shape[dim]
        last = lax.slice_in_dim(array, length - width, length, axis=dim)
        leading = lax.slice_in_dim(array, 0, width, axis=dim)
        before, after = exchange(last, leading, axis)
        array = jnp.concatenate([before, array, after], axis=dim)
    return array


def thermal_step(ext, heat_rows, lateral, vertical):
    cols = jnp.pad(ext, ((0, 0), (0, 0), (1, 1)))
    center = ext[:, 1:-1]
    lap = ext[:, 2:] + ext[:, :-2] + cols[:, 1:-1, 2:] + cols[:, 1:-1, :-2] - 4.0 * center
    flux = vertical[:, None, None] * (center[1:] - center[:-1])
    vert = jnp.pad(flux, ((0, 1), (0, 0), (0, 0))) - jnp.pad(flux, ((1, 0), (0, 0), (0, 0)))
    return center + lateral[:, None, None] * lap + vert + heat_rows


def moment_of(field, weighting):
    total = weighting[0] * field[0]
    for layer in range(1, field.shape[0]):
        total = total + weighting[layer] * field[layer]
    return total


def sweep(w_pad, e_pad, load):
    center = e_pad[1:-1, 1:-1]
    e_up = 0.5 * (center + e_pad[:-2, 1:-1])
    e_down = 0.5 * (center + e_pad[2:, 1:-1])
    e_left = 0.5 * (center + e_pad[1:-1, :-2])
    e_right = 0.5 * (center + e_pad[1:-1, 2:])
    numer = (
        load
        + e_up * w_pad[:-2, 1:-1]
        + e_down * w_pad[2:, 1:-1]
        + e_left * w_pad[1:-1, :-2]
        + e_right * w_pad[1:-1, 2:]
    )
    denom = stiffness + e_up + e_down + e_left + e_right
    return numer / denom


def anand(strain, resist, recv):
    total, inelastic = (strain[0], strain[1])
    increment, theta, live = (recv[0], recv[1], recv[2])
    total_new = total + increment
    arrhen = jnp.exp(2.0 - 2.0 / (1.0 + 0.1 * theta * theta))
    hyper = jnp.sinh(shear_mod * (total_new - inelastic) / resist)
    rate = rate_scale * arrhen * hyper * jnp.abs(hyper)
    inelastic_new = inelastic + rate
    target = sat_level * jnp.power(1.0 + jnp.abs(rate) / arrhen, sat_power)
    resist_new = resist + harden * (1.0 - resist / target) * jnp.abs(rate)
    keep = live > 0.5
    strain_out = jnp.stack(
        [jnp.where(keep, total_new, total), jnp.where(keep, inelastic_new, inelastic)]
    )
    return (strain_out, jnp.where(keep, resist_new, resist))


def thermal(temp, heat, lateral, vertical, extra):
    devices = lax.axis_size(FLAT)
    t = lax.axis_index(FLAT)
    rows = temp.shape[1]
    h = STEPS + extra
    hh = h - 1
    last = jnp.concatenate([temp[:, rows - h:], heat[:, rows - hh:]], axis=1)
    leading = jnp.concatenate([temp[:, :h], heat[:, :hh]], axis=1)
    before, after = exchange(last, leading, FLAT)
    ext = jnp.concatenate([before[:, :h], temp, after[:, :h]], axis=1)
    heat_ext = jnp.concatenate([before[:, h:], heat, after[:, h:]], axis=1)
    for step in range(1, STEPS + 1):
        r = STEPS - step + extra
        heat_rows = heat_ext[:, hh - r: hh - r + rows + 2 * r]
        ext = thermal_step(ext, heat_rows, lateral, vertical)
        if step < STEPS:
            g = t * rows + jnp.arange(-r, rows + r)
            inside = (g >= 0) & (g < devices * rows)
            ext = jnp.where(inside[None, :, None], ext, 0.0)
    return ext


def halo_2d(array, width):
    n_gx, n_gy = lax.axis_size("gx"), lax.axis_size("gy")
    rm, cm = array.shape[-2:]
    w = width
    pieces = {}
    for di in (-1, 0, 1):
        for dj in (-1, 0, 1):
            if di == 0 and dj == 0:
                continue
            rs = slice(rm - w, rm) if di == 1 else (slice(0, w) if di == -1 else slice(0, rm))
            cs = slice(cm - w, cm) if dj == 1 else (slice(0, w) if dj == -1 else slice(0, cm))
            pairs = [
                (i * n_gy + j, (i + di) * n_gy + (j + dj))
                for i in range(n_gx)
                for j in range(n_gy)
                if 0 <= i + di < n_gx and 0 <= j + dj < n_gy
            ]
            pieces[(di, dj)] = lax.ppermute(array[..., rs, cs], FLAT, pairs)
    top = jnp.concatenate([pieces[(1, 1)], pieces[(1, 0)], pieces[(1, -1)]], axis=-1)
    mid = jnp.concatenate([pieces[(0, 1)], array, pieces[(0, -1)]], axis=-1)
    bottom = jnp.concatenate([pieces[(-1, 1)], pieces[(-1, 0)], pieces[(-1, -1)]], axis=-1)
    return jnp.concatenate([top, mid, bottom], axis=-2)


def relay(load, top, width):
    n_gy = lax.axis_size("gy")
    rows, cols = load.shape
    cm = cols // n_gy
    rows = rows - 2 * width
    lp = jnp.pad(load, ((0, 0), (width, width)))
    tp = jnp.pad(top, ((width, width), (width, width)))
    both = jnp.stack([lp, tp])
    send = jnp.stack([both[:, :, k * cm: k * cm + cm + 2 * width] for k in range(n_gy)])
    recv = lax.all_to_all(send, "gy", split_axis=0, concat_axis=0, tiled=True)
    parts = []
    for k in range(n_gy):
        lo = 0 if k == 0 else width
        hi = rows + 2 * width if k == n_gy - 1 else rows + width
        parts.append(recv[k, 0, lo:hi])
    load_m = jnp.concatenate(parts, axis=0)
    top_m = jnp.concatenate(
        [recv[k, 1, width: rows + width, width: cm + width] for k in range(n_gy)], axis=0
    )
    return load_m, top_m


def joint_ranks(owners, devices):
    count = owners.shape[0]
    block = 128 if count % 128 == 0 else count
    nb = count // block
    onehot = (owners[:, None] == jnp.arange(devices, dtype=jnp.int32)[None, :]).astype(jnp.float32)
    oh = onehot.reshape(nb, block, devices)
    ar = jnp.arange(block)
    tri = (ar[:, None] >= ar[None, :]).astype(jnp.float32)
    within = jnp.einsum("ij,bjd->bid", tri, oh, precision=lax.Precision.HIGHEST)
    totals = within[:, -1, :]
    ab = jnp.arange(nb)
    stri = (ab[:, None] > ab[None, :]).astype(jnp.float32)
    offs = jnp.dot(stri, totals, precision=lax.Precision.HIGHEST)
    cum = (within + offs[:, None, :]).reshape(count, devices)
    return jnp.sum(cum * onehot, axis=1).astype(jnp.int32) - 1


def pick_kernel(rc_ref, parts_ref, out_ref):
    rc = rc_ref[...]
    rows = rc[:, 0:1]
    cols = rc[:, 1:2]
    block = rc.shape[0]
    _, rm, width = parts_ref.shape
    fields = out_ref.shape[1]
    cm = width // fields
    hit = rows == lax.broadcasted_iota(jnp.int32, (block, rm), 1)
    onehot = jnp.where(hit, 1.0, 0.0).astype(jnp.bfloat16)
    acc = jnp.dot(onehot, parts_ref[0], preferred_element_type=jnp.float32)
    acc = acc + jnp.dot(onehot, parts_ref[1], preferred_element_type=jnp.float32)
    acc = acc + jnp.dot(onehot, parts_ref[2], preferred_element_type=jnp.float32)
    lane = cols == lax.broadcasted_iota(jnp.int32, (block, cm), 1)
    for f in range(fields):
        seg = acc[:, f * cm: (f + 1) * cm]
        out_ref[:, f: f + 1] = jnp.sum(jnp.where(lane, seg, 0.0), axis=1, keepdims=True)


def pick_cells(fields, cells):
    count = cells.shape[0]
    nf, rm, cm = fields.shape
    wide = jnp.concatenate(list(fields), axis=1)
    hi = lax.reduce_precision(wide, exponent_bits=8, mantissa_bits=7)
    rest = wide - hi
    mid = lax.reduce_precision(rest, exponent_bits=8, mantissa_bits=7)
    lo = rest - mid
    parts = jnp.stack([hi, mid, lo]).astype(jnp.bfloat16)
    rc = jnp.stack([cells // cm, cells % cm], axis=1).astype(jnp.int32)
    block = 256 if count % 256 == 0 else count
    picked = pl.pallas_call(
        pick_kernel,
        grid=(count // block,),
        in_specs=[
            pl.BlockSpec((block, 2), lambda i: (i, 0)),
            pl.BlockSpec((3, rm, nf * cm), lambda i: (0, 0, 0)),
        ],
        out_specs=pl.BlockSpec((block, nf), lambda i: (i, 0)),
        out_shape=jax.ShapeDtypeStruct((count, nf), jnp.float32),
    )(rc, parts)
    return picked.T


def body(
    temp_start,
    heat_input,
    lateral,
    vertical,
    weighting,
    modulus,
    warp_prev,
    joint_cell,
    joint_owner,
    joint_strain,
    joint_resist,
):
    devices = lax.axis_size(FLAT)
    n_gx, n_gy = lax.axis_size("gx"), lax.axis_size("gy")
    gi, gj = lax.axis_index("gx"), lax.axis_index("gy")
    rm, cm = warp_prev.shape

    wm = halo_2d(jnp.stack([warp_prev, modulus]), SWEEPS)
    owners = joint_owner[:, 0]
    capacity = joint_resist.shape[1] // devices
    slots = owners * capacity + joint_ranks(owners, devices)

    extra = SWEEPS - 1
    temp = thermal(temp_start, heat_input, lateral, vertical, extra)
    load_t = moment_of(temp, weighting)
    load, top = relay(load_t, temp[-1, extra: temp.shape[1] - extra], extra)

    warp = wm[0]
    mod_ext = wm[1]
    for step in range(1, SWEEPS + 1):
        r = SWEEPS - step
        off = SWEEPS - (r + 1)
        e_pad = mod_ext[off: off + rm + 2 * r + 2, off: off + cm + 2 * r + 2]
        lo = SWEEPS - 1 - r
        ld = load[lo: lo + rm + 2 * r, lo: lo + cm + 2 * r]
        warp = sweep(warp, e_pad, ld)
        if r > 0:
            gr = gi * rm + jnp.arange(-r, rm + r)
            gc = gj * cm + jnp.arange(-r, cm + r)
            inside = ((gr >= 0) & (gr < n_gx * rm))[:, None] & ((gc >= 0) & (gc < n_gy * cm))[None, :]
            warp = jnp.where(inside, warp, 0.0)

    picked = pick_cells(jnp.stack([warp - warp_prev, top]), joint_cell)
    values = jnp.concatenate([picked, jnp.ones_like(picked[:1])], axis=0)
    outgoing = jnp.zeros((3, devices * capacity), jnp.float32).at[:, slots].set(values)
    incoming = lax.all_to_all(outgoing, FLAT, split_axis=1, concat_axis=1, tiled=True)
    strain_next, resist_next = anand(joint_strain, joint_resist, incoming[:, None, :])
    return (warp, strain_next, resist_next)


def solution(mesh):
    return jax.shard_map(
        body,
        mesh=mesh,
        in_specs=(
            P(None, FLAT, None),
            P(None, FLAT, None),
            P(),
            P(),
            P(),
            P("gx", "gy"),
            P("gx", "gy"),
            P(FLAT),
            P(FLAT, None),
            P(None, FLAT, None),
            P(FLAT, None),
        ),
        out_specs=(P("gx", "gy"), P(None, FLAT, None), P(FLAT, None)),
        check_vma=False,
    )
```

```python
import jax
import jax.numpy as jnp
from jax import lax
from jax.sharding import PartitionSpec as P
from jax.experimental import pallas as pl

STEPS = 2
SWEEPS = 3


stiffness = 0.2
shear_mod = 0.6
rate_scale = 0.5
sat_level = 2.5
sat_power = 0.3
harden = 2.0

FLAT = ("gx", "gy")


def exchange(last, leading, axis):
    count = lax.axis_size(axis)
    up = [(i, i + 1) for i in range(count - 1)]
    down = [(j, i) for i, j in up]
    return lax.ppermute(last, axis, up), lax.ppermute(leading, axis, down)


def with_halo(array, sides, width):
    for axis, dim in sides:
        length = array.shape[dim]
        last = lax.slice_in_dim(array, length - width, length, axis=dim)
        leading = lax.slice_in_dim(array, 0, width, axis=dim)
        before, after = exchange(last, leading, axis)
        array = jnp.concatenate([before, array, after], axis=dim)
    return array


def thermal_step(ext, heat_rows, lateral, vertical):
    cols = jnp.pad(ext, ((0, 0), (0, 0), (1, 1)))
    center = ext[:, 1:-1]
    lap = ext[:, 2:] + ext[:, :-2] + cols[:, 1:-1, 2:] + cols[:, 1:-1, :-2] - 4.0 * center
    flux = vertical[:, None, None] * (center[1:] - center[:-1])
    vert = jnp.pad(flux, ((0, 1), (0, 0), (0, 0))) - jnp.pad(flux, ((1, 0), (0, 0), (0, 0)))
    return center + lateral[:, None, None] * lap + vert + heat_rows


def moment_of(field, weighting):
    total = weighting[0] * field[0]
    for layer in range(1, field.shape[0]):
        total = total + weighting[layer] * field[layer]
    return total


def sweep(w_pad, e_pad, load):
    center = e_pad[1:-1, 1:-1]
    e_up = 0.5 * (center + e_pad[:-2, 1:-1])
    e_down = 0.5 * (center + e_pad[2:, 1:-1])
    e_left = 0.5 * (center + e_pad[1:-1, :-2])
    e_right = 0.5 * (center + e_pad[1:-1, 2:])
    numer = (
        load
        + e_up * w_pad[:-2, 1:-1]
        + e_down * w_pad[2:, 1:-1]
        + e_left * w_pad[1:-1, :-2]
        + e_right * w_pad[1:-1, 2:]
    )
    denom = stiffness + e_up + e_down + e_left + e_right
    return numer / denom


def anand(strain, resist, recv):
    total, inelastic = (strain[0], strain[1])
    increment, theta, live = (recv[0], recv[1], recv[2])
    total_new = total + increment
    arrhen = jnp.exp(2.0 - 2.0 / (1.0 + 0.1 * theta * theta))
    hyper = jnp.sinh(shear_mod * (total_new - inelastic) / resist)
    rate = rate_scale * arrhen * hyper * jnp.abs(hyper)
    inelastic_new = inelastic + rate
    target = sat_level * jnp.power(1.0 + jnp.abs(rate) / arrhen, sat_power)
    resist_new = resist + harden * (1.0 - resist / target) * jnp.abs(rate)
    keep = live > 0.5
    strain_out = jnp.stack(
        [jnp.where(keep, total_new, total), jnp.where(keep, inelastic_new, inelastic)]
    )
    return (strain_out, jnp.where(keep, resist_new, resist))


def as_slab(piece, layers, cols):
    flat = piece.reshape(-1)
    per = layers * cols
    n = -(-flat.shape[0] // per)
    return jnp.pad(flat, (0, n * per - flat.shape[0])).reshape(n, layers, cols).transpose(1, 0, 2)


def from_slab(slab, shape):
    size = 1
    for d in shape:
        size *= d
    return slab.transpose(1, 0, 2).reshape(-1)[:size].reshape(shape)


def thermal(temp, heat, lateral, vertical, extra, side_last, side_leading):
    devices = lax.axis_size(FLAT)
    t = lax.axis_index(FLAT)
    layers, rows, cols = temp.shape
    h = STEPS + extra
    hh = h - 1
    last = jnp.concatenate(
        [temp[:, rows - h:], heat[:, rows - hh:], as_slab(side_last, layers, cols)], axis=1)
    leading = jnp.concatenate(
        [temp[:, :h], heat[:, :hh], as_slab(side_leading, layers, cols)], axis=1)
    before, after = exchange(last, leading, FLAT)
    side_before = from_slab(before[:, h + hh:], side_last.shape)
    side_after = from_slab(after[:, h + hh:], side_leading.shape)
    before, after = before[:, : h + hh], after[:, : h + hh]
    ext = jnp.concatenate([before[:, :h], temp, after[:, :h]], axis=1)
    heat_ext = jnp.concatenate([before[:, h:], heat, after[:, h:]], axis=1)
    for step in range(1, STEPS + 1):
        r = STEPS - step + extra
        heat_rows = heat_ext[:, hh - r: hh - r + rows + 2 * r]
        ext = thermal_step(ext, heat_rows, lateral, vertical)
        if step < STEPS:
            g = t * rows + jnp.arange(-r, rows + r)
            inside = (g >= 0) & (g < devices * rows)
            ext = jnp.where(inside[None, :, None], ext, 0.0)
    return ext, side_before, side_after


def relay(load, top, width):
    n_gy = lax.axis_size("gy")
    rows, cols = load.shape
    cm = cols // n_gy
    rows = rows - 2 * width
    lp = jnp.pad(load, ((0, 0), (width, width)))
    tp = jnp.pad(top, ((width, width), (width, width)))
    both = jnp.stack([lp, tp])
    send = jnp.stack([both[:, :, k * cm: k * cm + cm + 2 * width] for k in range(n_gy)])
    recv = lax.all_to_all(send, "gy", split_axis=0, concat_axis=0, tiled=True)
    parts = []
    for k in range(n_gy):
        lo = 0 if k == 0 else width
        hi = rows + 2 * width if k == n_gy - 1 else rows + width
        parts.append(recv[k, 0, lo:hi])
    load_m = jnp.concatenate(parts, axis=0)
    top_m = jnp.concatenate(
        [recv[k, 1, width: rows + width, width: cm + width] for k in range(n_gy)], axis=0
    )
    return load_m, top_m


def joint_ranks(owners, devices):
    count = owners.shape[0]
    block = 128 if count % 128 == 0 else count
    nb = count // block
    onehot = (owners[:, None] == jnp.arange(devices, dtype=jnp.int32)[None, :]).astype(jnp.float32)
    oh = onehot.reshape(nb, block, devices)
    ar = jnp.arange(block)
    tri = (ar[:, None] >= ar[None, :]).astype(jnp.float32)
    within = jnp.einsum("ij,bjd->bid", tri, oh, precision=lax.Precision.HIGHEST)
    totals = within[:, -1, :]
    ab = jnp.arange(nb)
    stri = (ab[:, None] > ab[None, :]).astype(jnp.float32)
    offs = jnp.dot(stri, totals, precision=lax.Precision.HIGHEST)
    cum = (within + offs[:, None, :]).reshape(count, devices)
    return jnp.sum(cum * onehot, axis=1).astype(jnp.int32) - 1


def pick_kernel(rc_ref, parts_ref, out_ref):
    rc = rc_ref[...]
    rows = rc[:, 0:1]
    cols = rc[:, 1:2]
    block = rc.shape[0]
    _, rm, width = parts_ref.shape
    fields = out_ref.shape[1]
    cm = width // fields
    hit = rows == lax.broadcasted_iota(jnp.int32, (block, rm), 1)
    onehot = jnp.where(hit, 1.0, 0.0).astype(jnp.bfloat16)
    acc = jnp.dot(onehot, parts_ref[0], preferred_element_type=jnp.float32)
    acc = acc + jnp.dot(onehot, parts_ref[1], preferred_element_type=jnp.float32)
    acc = acc + jnp.dot(onehot, parts_ref[2], preferred_element_type=jnp.float32)
    lane = cols == lax.broadcasted_iota(jnp.int32, (block, cm), 1)
    for f in range(fields):
        seg = acc[:, f * cm: (f + 1) * cm]
        out_ref[:, f: f + 1] = jnp.sum(jnp.where(lane, seg, 0.0), axis=1, keepdims=True)


def pick_cells(fields, cells):
    count = cells.shape[0]
    nf, rm, cm = fields.shape
    wide = jnp.concatenate(list(fields), axis=1)
    hi = lax.reduce_precision(wide, exponent_bits=8, mantissa_bits=7)
    rest = wide - hi
    mid = lax.reduce_precision(rest, exponent_bits=8, mantissa_bits=7)
    lo = rest - mid
    parts = jnp.stack([hi, mid, lo]).astype(jnp.bfloat16)
    rc = jnp.stack([cells // cm, cells % cm], axis=1).astype(jnp.int32)
    block = 256 if count % 256 == 0 else count
    picked = pl.pallas_call(
        pick_kernel,
        grid=(count // block,),
        in_specs=[
            pl.BlockSpec((block, 2), lambda i: (i, 0)),
            pl.BlockSpec((3, rm, nf * cm), lambda i: (0, 0, 0)),
        ],
        out_specs=pl.BlockSpec((block, nf), lambda i: (i, 0)),
        out_shape=jax.ShapeDtypeStruct((count, nf), jnp.float32),
    )(rc, parts)
    return picked.T


def body(
    temp_start,
    heat_input,
    lateral,
    vertical,
    weighting,
    modulus,
    warp_prev,
    joint_cell,
    joint_owner,
    joint_strain,
    joint_resist,
):
    devices = lax.axis_size(FLAT)
    n_gx, n_gy = lax.axis_size("gx"), lax.axis_size("gy")
    gi, gj = lax.axis_index("gx"), lax.axis_index("gy")
    rm, cm = warp_prev.shape

    wm = jnp.stack([warp_prev, modulus])
    owners = joint_owner[:, 0]
    capacity = joint_resist.shape[1] // devices
    slots = owners * capacity + joint_ranks(owners, devices)

    extra = SWEEPS - 1
    g = SWEEPS
    temp, left, right = thermal(
        temp_start, heat_input, lateral, vertical, extra, wm[:, :, cm - g:], wm[:, :, :g])
    left = jnp.where(gj > 0, left, 0.0)
    right = jnp.where(gj < n_gy - 1, right, 0.0)
    wm = with_halo(jnp.concatenate([left, wm, right], axis=2), (("gx", 1),), g)
    load_t = moment_of(temp, weighting)
    load, top = relay(load_t, temp[-1, extra: temp.shape[1] - extra], extra)

    warp = wm[0]
    mod_ext = wm[1]
    for step in range(1, SWEEPS + 1):
        r = SWEEPS - step
        off = SWEEPS - (r + 1)
        e_pad = mod_ext[off: off + rm + 2 * r + 2, off: off + cm + 2 * r + 2]
        lo = SWEEPS - 1 - r
        ld = load[lo: lo + rm + 2 * r, lo: lo + cm + 2 * r]
        warp = sweep(warp, e_pad, ld)
        if r > 0:
            gr = gi * rm + jnp.arange(-r, rm + r)
            gc = gj * cm + jnp.arange(-r, cm + r)
            inside = ((gr >= 0) & (gr < n_gx * rm))[:, None] & ((gc >= 0) & (gc < n_gy * cm))[None, :]
            warp = jnp.where(inside, warp, 0.0)

    picked = pick_cells(jnp.stack([warp - warp_prev, top]), joint_cell)
    values = jnp.concatenate([picked, jnp.ones_like(picked[:1])], axis=0)
    outgoing = jnp.zeros((3, devices * capacity), jnp.float32).at[:, slots].set(values)
    incoming = lax.all_to_all(outgoing, FLAT, split_axis=1, concat_axis=1, tiled=True)
    strain_next, resist_next = anand(joint_strain, joint_resist, incoming[:, None, :])
    return (warp, strain_next, resist_next)


def solution(mesh):
    return jax.shard_map(
        body,
        mesh=mesh,
        in_specs=(
            P(None, FLAT, None),
            P(None, FLAT, None),
            P(),
            P(),
            P(),
            P("gx", "gy"),
            P("gx", "gy"),
            P(FLAT),
            P(FLAT, None),
            P(None, FLAT, None),
            P(FLAT, None),
        ),
        out_specs=(P("gx", "gy"), P(None, FLAT, None), P(FLAT, None)),
        check_vma=False,
    )
```

```python
import jax
import jax.numpy as jnp
from jax import lax
from jax.sharding import PartitionSpec as P
from jax.experimental import pallas as pl

STEPS = 2
SWEEPS = 3


stiffness = 0.2
shear_mod = 0.6
rate_scale = 0.5
sat_level = 2.5
sat_power = 0.3
harden = 2.0

FLAT = ("gx", "gy")


def exchange(last, leading, axis):
    count = lax.axis_size(axis)
    up = [(i, i + 1) for i in range(count - 1)]
    down = [(j, i) for i, j in up]
    return lax.ppermute(last, axis, up), lax.ppermute(leading, axis, down)


def with_halo(array, sides, width):
    for axis, dim in sides:
        length = array.shape[dim]
        last = lax.slice_in_dim(array, length - width, length, axis=dim)
        leading = lax.slice_in_dim(array, 0, width, axis=dim)
        before, after = exchange(last, leading, axis)
        array = jnp.concatenate([before, array, after], axis=dim)
    return array


def thermal_step(ext, heat_rows, lateral, vertical):
    cols = jnp.pad(ext, ((0, 0), (0, 0), (1, 1)))
    center = ext[:, 1:-1]
    lap = ext[:, 2:] + ext[:, :-2] + cols[:, 1:-1, 2:] + cols[:, 1:-1, :-2] - 4.0 * center
    flux = vertical[:, None, None] * (center[1:] - center[:-1])
    vert = jnp.pad(flux, ((0, 1), (0, 0), (0, 0))) - jnp.pad(flux, ((1, 0), (0, 0), (0, 0)))
    return center + lateral[:, None, None] * lap + vert + heat_rows


def moment_of(field, weighting):
    total = weighting[0] * field[0]
    for layer in range(1, field.shape[0]):
        total = total + weighting[layer] * field[layer]
    return total


def sweep(w_pad, e_pad, load):
    center = e_pad[1:-1, 1:-1]
    e_up = 0.5 * (center + e_pad[:-2, 1:-1])
    e_down = 0.5 * (center + e_pad[2:, 1:-1])
    e_left = 0.5 * (center + e_pad[1:-1, :-2])
    e_right = 0.5 * (center + e_pad[1:-1, 2:])
    numer = (
        load
        + e_up * w_pad[:-2, 1:-1]
        + e_down * w_pad[2:, 1:-1]
        + e_left * w_pad[1:-1, :-2]
        + e_right * w_pad[1:-1, 2:]
    )
    denom = stiffness + e_up + e_down + e_left + e_right
    return numer / denom


def anand(strain, resist, recv):
    total, inelastic = (strain[0], strain[1])
    increment, theta, live = (recv[0], recv[1], recv[2])
    total_new = total + increment
    arrhen = jnp.exp(2.0 - 2.0 / (1.0 + 0.1 * theta * theta))
    hyper = jnp.sinh(shear_mod * (total_new - inelastic) / resist)
    rate = rate_scale * arrhen * hyper * jnp.abs(hyper)
    inelastic_new = inelastic + rate
    target = sat_level * jnp.power(1.0 + jnp.abs(rate) / arrhen, sat_power)
    resist_new = resist + harden * (1.0 - resist / target) * jnp.abs(rate)
    keep = live > 0.5
    strain_out = jnp.stack(
        [jnp.where(keep, total_new, total), jnp.where(keep, inelastic_new, inelastic)]
    )
    return (strain_out, jnp.where(keep, resist_new, resist))


def as_slab(piece, layers, cols):
    flat = piece.reshape(-1)
    per = layers * cols
    n = -(-flat.shape[0] // per)
    return jnp.pad(flat, (0, n * per - flat.shape[0])).reshape(n, layers, cols).transpose(1, 0, 2)


def from_slab(slab, shape):
    size = 1
    for d in shape:
        size *= d
    return slab.transpose(1, 0, 2).reshape(-1)[:size].reshape(shape)


def thermal(temp, heat, lateral, vertical, extra, side_last, side_leading):
    devices = lax.axis_size(FLAT)
    t = lax.axis_index(FLAT)
    layers, rows, cols = temp.shape
    h = STEPS + extra
    hh = h - 1
    last = jnp.concatenate(
        [temp[:, rows - h:], heat[:, rows - hh:], as_slab(side_last, layers, cols)], axis=1)
    leading = jnp.concatenate(
        [temp[:, :h], heat[:, :hh], as_slab(side_leading, layers, cols)], axis=1)
    before, after = exchange(last, leading, FLAT)
    side_before = from_slab(before[:, h + hh:], side_last.shape)
    side_after = from_slab(after[:, h + hh:], side_leading.shape)
    before, after = before[:, : h + hh], after[:, : h + hh]
    ext = jnp.concatenate([before[:, :h], temp, after[:, :h]], axis=1)
    heat_ext = jnp.concatenate([before[:, h:], heat, after[:, h:]], axis=1)
    for step in range(1, STEPS + 1):
        r = STEPS - step + extra
        heat_rows = heat_ext[:, hh - r: hh - r + rows + 2 * r]
        ext = thermal_step(ext, heat_rows, lateral, vertical)
        if step < STEPS:
            g = t * rows + jnp.arange(-r, rows + r)
            inside = (g >= 0) & (g < devices * rows)
            ext = jnp.where(inside[None, :, None], ext, 0.0)
    return ext, side_before, side_after


def relay(load, top, width):
    n_gy = lax.axis_size("gy")
    rows, cols = load.shape
    cm = cols // n_gy
    rows = rows - 2 * width
    lp = jnp.pad(load, ((0, 0), (width, width)))
    tp = jnp.pad(top, ((width, width), (width, width)))
    both = jnp.stack([lp, tp])
    send = jnp.stack([both[:, :, k * cm: k * cm + cm + 2 * width] for k in range(n_gy)])
    gj = lax.axis_index("gy")
    got = [lax.dynamic_index_in_dim(send, gj, 0, keepdims=False)]
    for shift in range(1, n_gy):
        piece = lax.dynamic_index_in_dim(send, (gj + shift) % n_gy, 0, keepdims=False)
        got.append(lax.ppermute(piece, "gy", [(j, (j + shift) % n_gy) for j in range(n_gy)]))
    recv = jnp.take(jnp.stack(got), (gj - jnp.arange(n_gy)) % n_gy, axis=0)
    parts = []
    for k in range(n_gy):
        lo = 0 if k == 0 else width
        hi = rows + 2 * width if k == n_gy - 1 else rows + width
        parts.append(recv[k, 0, lo:hi])
    load_m = jnp.concatenate(parts, axis=0)
    top_m = jnp.concatenate(
        [recv[k, 1, width: rows + width, width: cm + width] for k in range(n_gy)], axis=0
    )
    return load_m, top_m


def joint_ranks(owners, devices):
    count = owners.shape[0]
    block = 128 if count % 128 == 0 else count
    nb = count // block
    onehot = (owners[:, None] == jnp.arange(devices, dtype=jnp.int32)[None, :]).astype(jnp.float32)
    oh = onehot.reshape(nb, block, devices)
    ar = jnp.arange(block)
    tri = (ar[:, None] >= ar[None, :]).astype(jnp.float32)
    within = jnp.einsum("ij,bjd->bid", tri, oh, precision=lax.Precision.HIGHEST)
    totals = within[:, -1, :]
    ab = jnp.arange(nb)
    stri = (ab[:, None] > ab[None, :]).astype(jnp.float32)
    offs = jnp.dot(stri, totals, precision=lax.Precision.HIGHEST)
    cum = (within + offs[:, None, :]).reshape(count, devices)
    return jnp.sum(cum * onehot, axis=1).astype(jnp.int32) - 1


def pick_kernel(rc_ref, parts_ref, out_ref):
    rc = rc_ref[...]
    rows = rc[:, 0:1]
    cols = rc[:, 1:2]
    block = rc.shape[0]
    _, rm, width = parts_ref.shape
    fields = out_ref.shape[1]
    cm = width // fields
    hit = rows == lax.broadcasted_iota(jnp.int32, (block, rm), 1)
    onehot = jnp.where(hit, 1.0, 0.0).astype(jnp.bfloat16)
    acc = jnp.dot(onehot, parts_ref[0], preferred_element_type=jnp.float32)
    acc = acc + jnp.dot(onehot, parts_ref[1], preferred_element_type=jnp.float32)
    acc = acc + jnp.dot(onehot, parts_ref[2], preferred_element_type=jnp.float32)
    lane = cols == lax.broadcasted_iota(jnp.int32, (block, cm), 1)
    for f in range(fields):
        seg = acc[:, f * cm: (f + 1) * cm]
        out_ref[:, f: f + 1] = jnp.sum(jnp.where(lane, seg, 0.0), axis=1, keepdims=True)


def pick_cells(fields, cells):
    count = cells.shape[0]
    nf, rm, cm = fields.shape
    wide = jnp.concatenate(list(fields), axis=1)
    hi = lax.reduce_precision(wide, exponent_bits=8, mantissa_bits=7)
    rest = wide - hi
    mid = lax.reduce_precision(rest, exponent_bits=8, mantissa_bits=7)
    lo = rest - mid
    parts = jnp.stack([hi, mid, lo]).astype(jnp.bfloat16)
    rc = jnp.stack([cells // cm, cells % cm], axis=1).astype(jnp.int32)
    block = 256 if count % 256 == 0 else count
    picked = pl.pallas_call(
        pick_kernel,
        grid=(count // block,),
        in_specs=[
            pl.BlockSpec((block, 2), lambda i: (i, 0)),
            pl.BlockSpec((3, rm, nf * cm), lambda i: (0, 0, 0)),
        ],
        out_specs=pl.BlockSpec((block, nf), lambda i: (i, 0)),
        out_shape=jax.ShapeDtypeStruct((count, nf), jnp.float32),
    )(rc, parts)
    return picked.T


def body(
    temp_start,
    heat_input,
    lateral,
    vertical,
    weighting,
    modulus,
    warp_prev,
    joint_cell,
    joint_owner,
    joint_strain,
    joint_resist,
):
    devices = lax.axis_size(FLAT)
    n_gx, n_gy = lax.axis_size("gx"), lax.axis_size("gy")
    gi, gj = lax.axis_index("gx"), lax.axis_index("gy")
    rm, cm = warp_prev.shape

    wm = jnp.stack([warp_prev, modulus])
    owners = joint_owner[:, 0]
    capacity = joint_resist.shape[1] // devices
    slots = owners * capacity + joint_ranks(owners, devices)

    extra = SWEEPS - 1
    g = SWEEPS
    temp, left, right = thermal(
        temp_start, heat_input, lateral, vertical, extra, wm[:, :, cm - g:], wm[:, :, :g])
    left = jnp.where(gj > 0, left, 0.0)
    right = jnp.where(gj < n_gy - 1, right, 0.0)
    wm = with_halo(jnp.concatenate([left, wm, right], axis=2), (("gx", 1),), g)
    load_t = moment_of(temp, weighting)
    load, top = relay(load_t, temp[-1, extra: temp.shape[1] - extra], extra)

    warp = wm[0]
    mod_ext = wm[1]
    for step in range(1, SWEEPS + 1):
        r = SWEEPS - step
        off = SWEEPS - (r + 1)
        e_pad = mod_ext[off: off + rm + 2 * r + 2, off: off + cm + 2 * r + 2]
        lo = SWEEPS - 1 - r
        ld = load[lo: lo + rm + 2 * r, lo: lo + cm + 2 * r]
        warp = sweep(warp, e_pad, ld)
        if r > 0:
            gr = gi * rm + jnp.arange(-r, rm + r)
            gc = gj * cm + jnp.arange(-r, cm + r)
            inside = ((gr >= 0) & (gr < n_gx * rm))[:, None] & ((gc >= 0) & (gc < n_gy * cm))[None, :]
            warp = jnp.where(inside, warp, 0.0)

    picked = pick_cells(jnp.stack([warp - warp_prev, top]), joint_cell)
    values = jnp.concatenate([picked, jnp.ones_like(picked[:1])], axis=0)
    outgoing = jnp.zeros((3, devices * capacity), jnp.float32).at[:, slots].set(values)
    incoming = lax.all_to_all(outgoing, FLAT, split_axis=1, concat_axis=1, tiled=True)
    strain_next, resist_next = anand(joint_strain, joint_resist, incoming[:, None, :])
    return (warp, strain_next, resist_next)


def solution(mesh):
    return jax.shard_map(
        body,
        mesh=mesh,
        in_specs=(
            P(None, FLAT, None),
            P(None, FLAT, None),
            P(),
            P(),
            P(),
            P("gx", "gy"),
            P("gx", "gy"),
            P(FLAT),
            P(FLAT, None),
            P(None, FLAT, None),
            P(FLAT, None),
        ),
        out_specs=(P("gx", "gy"), P(None, FLAT, None), P(FLAT, None)),
        check_vma=False,
    )
```

```python
import jax
import jax.numpy as jnp
from jax import lax
from jax.sharding import PartitionSpec as P
from jax.experimental import pallas as pl

STEPS = 2
SWEEPS = 3


stiffness = 0.2
shear_mod = 0.6
rate_scale = 0.5
sat_level = 2.5
sat_power = 0.3
harden = 2.0

FLAT = ("gx", "gy")


def exchange(last, leading, axis):
    count = lax.axis_size(axis)
    up = [(i, i + 1) for i in range(count - 1)]
    down = [(j, i) for i, j in up]
    return lax.ppermute(last, axis, up), lax.ppermute(leading, axis, down)


def with_halo(array, sides, width):
    for axis, dim in sides:
        length = array.shape[dim]
        last = lax.slice_in_dim(array, length - width, length, axis=dim)
        leading = lax.slice_in_dim(array, 0, width, axis=dim)
        before, after = exchange(last, leading, axis)
        array = jnp.concatenate([before, array, after], axis=dim)
    return array


def thermal_step(ext, heat_rows, lateral, vertical):
    cols = jnp.pad(ext, ((0, 0), (0, 0), (1, 1)))
    center = ext[:, 1:-1]
    lap = ext[:, 2:] + ext[:, :-2] + cols[:, 1:-1, 2:] + cols[:, 1:-1, :-2] - 4.0 * center
    flux = vertical[:, None, None] * (center[1:] - center[:-1])
    vert = jnp.pad(flux, ((0, 1), (0, 0), (0, 0))) - jnp.pad(flux, ((1, 0), (0, 0), (0, 0)))
    return center + lateral[:, None, None] * lap + vert + heat_rows


def moment_of(field, weighting):
    total = weighting[0] * field[0]
    for layer in range(1, field.shape[0]):
        total = total + weighting[layer] * field[layer]
    return total


def sweep(w_pad, e_pad, load):
    center = e_pad[1:-1, 1:-1]
    e_up = 0.5 * (center + e_pad[:-2, 1:-1])
    e_down = 0.5 * (center + e_pad[2:, 1:-1])
    e_left = 0.5 * (center + e_pad[1:-1, :-2])
    e_right = 0.5 * (center + e_pad[1:-1, 2:])
    numer = (
        load
        + e_up * w_pad[:-2, 1:-1]
        + e_down * w_pad[2:, 1:-1]
        + e_left * w_pad[1:-1, :-2]
        + e_right * w_pad[1:-1, 2:]
    )
    denom = stiffness + e_up + e_down + e_left + e_right
    return numer / denom


def anand(strain, resist, recv):
    total, inelastic = (strain[0], strain[1])
    increment, theta, live = (recv[0], recv[1], recv[2])
    total_new = total + increment
    arrhen = jnp.exp(2.0 - 2.0 / (1.0 + 0.1 * theta * theta))
    hyper = jnp.sinh(shear_mod * (total_new - inelastic) / resist)
    rate = rate_scale * arrhen * hyper * jnp.abs(hyper)
    inelastic_new = inelastic + rate
    target = sat_level * jnp.power(1.0 + jnp.abs(rate) / arrhen, sat_power)
    resist_new = resist + harden * (1.0 - resist / target) * jnp.abs(rate)
    keep = live > 0.5
    strain_out = jnp.stack(
        [jnp.where(keep, total_new, total), jnp.where(keep, inelastic_new, inelastic)]
    )
    return (strain_out, jnp.where(keep, resist_new, resist))


def as_slab(piece, layers, cols):
    flat = piece.reshape(-1)
    per = layers * cols
    n = -(-flat.shape[0] // per)
    return jnp.pad(flat, (0, n * per - flat.shape[0])).reshape(n, layers, cols).transpose(1, 0, 2)


def from_slab(slab, shape):
    size = 1
    for d in shape:
        size *= d
    return slab.transpose(1, 0, 2).reshape(-1)[:size].reshape(shape)


def thermal(temp, heat, lateral, vertical, extra):
    devices = lax.axis_size(FLAT)
    t = lax.axis_index(FLAT)
    rows = temp.shape[1]
    h = STEPS + extra
    hh = h - 1
    last = jnp.concatenate([temp[:, rows - h:], heat[:, rows - hh:]], axis=1)
    leading = jnp.concatenate([temp[:, :h], heat[:, :hh]], axis=1)
    before, after = exchange(last, leading, FLAT)
    ext = jnp.concatenate([before[:, :h], temp, after[:, :h]], axis=1)
    heat_ext = jnp.concatenate([before[:, h:], heat, after[:, h:]], axis=1)
    for step in range(1, STEPS + 1):
        r = STEPS - step + extra
        heat_rows = heat_ext[:, hh - r: hh - r + rows + 2 * r]
        ext = thermal_step(ext, heat_rows, lateral, vertical)
        if step < STEPS:
            g = t * rows + jnp.arange(-r, rows + r)
            inside = (g >= 0) & (g < devices * rows)
            ext = jnp.where(inside[None, :, None], ext, 0.0)
    return ext


def relay(load, top, width, side_last, side_leading):
    n_gy = lax.axis_size("gy")
    gj = lax.axis_index("gy")
    rows, cols = load.shape
    cm = cols // n_gy
    rows = rows - 2 * width
    lp = jnp.pad(load, ((0, 0), (width, width)))
    tp = jnp.pad(top, ((width, width), (width, width)))
    both = jnp.stack([lp, tp])
    send = jnp.stack([both[:, :, k * cm: k * cm + cm + 2 * width] for k in range(n_gy)])
    depth = send.shape[2]
    got = [lax.dynamic_index_in_dim(send, gj, 0, keepdims=False)]
    side_before = side_after = None
    for shift in range(1, n_gy):
        piece = lax.dynamic_index_in_dim(send, (gj + shift) % n_gy, 0, keepdims=False)
        extras = []
        if shift == 1:
            extras.append(as_slab(side_last, 2, piece.shape[2]))
        if shift == n_gy - 1:
            extras.append(as_slab(side_leading, 2, piece.shape[2]))
        piece = jnp.concatenate([piece] + extras, axis=1)
        moved = lax.ppermute(piece, "gy", [(j, (j + shift) % n_gy) for j in range(n_gy)])
        at = depth
        if shift == 1:
            slab = as_slab(side_last, 2, piece.shape[2])
            side_before = from_slab(moved[:, at: at + slab.shape[1]], side_last.shape)
            at += slab.shape[1]
        if shift == n_gy - 1:
            slab = as_slab(side_leading, 2, piece.shape[2])
            side_after = from_slab(moved[:, at: at + slab.shape[1]], side_leading.shape)
        got.append(moved[:, :depth])
    if side_before is None:
        side_before = jnp.zeros_like(side_last)
        side_after = jnp.zeros_like(side_leading)
    side_before = jnp.where(gj > 0, side_before, 0.0)
    side_after = jnp.where(gj < n_gy - 1, side_after, 0.0)
    recv = jnp.take(jnp.stack(got), (gj - jnp.arange(n_gy)) % n_gy, axis=0)
    parts = []
    for k in range(n_gy):
        lo = 0 if k == 0 else width
        hi = rows + 2 * width if k == n_gy - 1 else rows + width
        parts.append(recv[k, 0, lo:hi])
    load_m = jnp.concatenate(parts, axis=0)
    top_m = jnp.concatenate(
        [recv[k, 1, width: rows + width, width: cm + width] for k in range(n_gy)], axis=0
    )
    return load_m, top_m, side_before, side_after


def joint_ranks(owners, devices):
    count = owners.shape[0]
    block = 128 if count % 128 == 0 else count
    nb = count // block
    onehot = (owners[:, None] == jnp.arange(devices, dtype=jnp.int32)[None, :]).astype(jnp.float32)
    oh = onehot.reshape(nb, block, devices)
    ar = jnp.arange(block)
    tri = (ar[:, None] >= ar[None, :]).astype(jnp.float32)
    within = jnp.einsum("ij,bjd->bid", tri, oh, precision=lax.Precision.HIGHEST)
    totals = within[:, -1, :]
    ab = jnp.arange(nb)
    stri = (ab[:, None] > ab[None, :]).astype(jnp.float32)
    offs = jnp.dot(stri, totals, precision=lax.Precision.HIGHEST)
    cum = (within + offs[:, None, :]).reshape(count, devices)
    return jnp.sum(cum * onehot, axis=1).astype(jnp.int32) - 1


def pick_kernel(rc_ref, parts_ref, out_ref):
    rc = rc_ref[...]
    rows = rc[:, 0:1]
    cols = rc[:, 1:2]
    block = rc.shape[0]
    _, rm, width = parts_ref.shape
    fields = out_ref.shape[1]
    cm = width // fields
    hit = rows == lax.broadcasted_iota(jnp.int32, (block, rm), 1)
    onehot = jnp.where(hit, 1.0, 0.0).astype(jnp.bfloat16)
    acc = jnp.dot(onehot, parts_ref[0], preferred_element_type=jnp.float32)
    acc = acc + jnp.dot(onehot, parts_ref[1], preferred_element_type=jnp.float32)
    acc = acc + jnp.dot(onehot, parts_ref[2], preferred_element_type=jnp.float32)
    lane = cols == lax.broadcasted_iota(jnp.int32, (block, cm), 1)
    for f in range(fields):
        seg = acc[:, f * cm: (f + 1) * cm]
        out_ref[:, f: f + 1] = jnp.sum(jnp.where(lane, seg, 0.0), axis=1, keepdims=True)


def pick_cells(fields, cells):
    count = cells.shape[0]
    nf, rm, cm = fields.shape
    wide = jnp.concatenate(list(fields), axis=1)
    hi = lax.reduce_precision(wide, exponent_bits=8, mantissa_bits=7)
    rest = wide - hi
    mid = lax.reduce_precision(rest, exponent_bits=8, mantissa_bits=7)
    lo = rest - mid
    parts = jnp.stack([hi, mid, lo]).astype(jnp.bfloat16)
    rc = jnp.stack([cells // cm, cells % cm], axis=1).astype(jnp.int32)
    block = 256 if count % 256 == 0 else count
    picked = pl.pallas_call(
        pick_kernel,
        grid=(count // block,),
        in_specs=[
            pl.BlockSpec((block, 2), lambda i: (i, 0)),
            pl.BlockSpec((3, rm, nf * cm), lambda i: (0, 0, 0)),
        ],
        out_specs=pl.BlockSpec((block, nf), lambda i: (i, 0)),
        out_shape=jax.ShapeDtypeStruct((count, nf), jnp.float32),
    )(rc, parts)
    return picked.T


def body(
    temp_start,
    heat_input,
    lateral,
    vertical,
    weighting,
    modulus,
    warp_prev,
    joint_cell,
    joint_owner,
    joint_strain,
    joint_resist,
):
    devices = lax.axis_size(FLAT)
    n_gx, n_gy = lax.axis_size("gx"), lax.axis_size("gy")
    gi, gj = lax.axis_index("gx"), lax.axis_index("gy")
    rm, cm = warp_prev.shape

    wm = jnp.stack([warp_prev, modulus])
    owners = joint_owner[:, 0]
    capacity = joint_resist.shape[1] // devices
    slots = owners * capacity + joint_ranks(owners, devices)

    extra = SWEEPS - 1
    g = SWEEPS
    wm = with_halo(wm, (("gx", 1),), g)
    temp = thermal(temp_start, heat_input, lateral, vertical, extra)
    load_t = moment_of(temp, weighting)
    load, top, left, right = relay(
        load_t, temp[-1, extra: temp.shape[1] - extra], extra, wm[:, :, cm - g:], wm[:, :, :g])
    wm = jnp.concatenate([left, wm, right], axis=2)

    warp = wm[0]
    mod_ext = wm[1]
    for step in range(1, SWEEPS + 1):
        r = SWEEPS - step
        off = SWEEPS - (r + 1)
        e_pad = mod_ext[off: off + rm + 2 * r + 2, off: off + cm + 2 * r + 2]
        lo = SWEEPS - 1 - r
        ld = load[lo: lo + rm + 2 * r, lo: lo + cm + 2 * r]
        warp = sweep(warp, e_pad, ld)
        if r > 0:
            gr = gi * rm + jnp.arange(-r, rm + r)
            gc = gj * cm + jnp.arange(-r, cm + r)
            inside = ((gr >= 0) & (gr < n_gx * rm))[:, None] & ((gc >= 0) & (gc < n_gy * cm))[None, :]
            warp = jnp.where(inside, warp, 0.0)

    picked = pick_cells(jnp.stack([warp - warp_prev, top]), joint_cell)
    values = jnp.concatenate([picked, jnp.ones_like(picked[:1])], axis=0)
    outgoing = jnp.zeros((3, devices * capacity), jnp.float32).at[:, slots].set(values)
    incoming = lax.all_to_all(outgoing, FLAT, split_axis=1, concat_axis=1, tiled=True)
    strain_next, resist_next = anand(joint_strain, joint_resist, incoming[:, None, :])
    return (warp, strain_next, resist_next)


def solution(mesh):
    return jax.shard_map(
        body,
        mesh=mesh,
        in_specs=(
            P(None, FLAT, None),
            P(None, FLAT, None),
            P(),
            P(),
            P(),
            P("gx", "gy"),
            P("gx", "gy"),
            P(FLAT),
            P(FLAT, None),
            P(None, FLAT, None),
            P(FLAT, None),
        ),
        out_specs=(P("gx", "gy"), P(None, FLAT, None), P(FLAT, None)),
        check_vma=False,
    )
```

```python
import jax
import jax.numpy as jnp
from jax import lax
from jax.sharding import PartitionSpec as P
from jax.experimental import pallas as pl

STEPS = 2
SWEEPS = 3


stiffness = 0.2
shear_mod = 0.6
rate_scale = 0.5
sat_level = 2.5
sat_power = 0.3
harden = 2.0

FLAT = ("gx", "gy")


def exchange(last, leading, axis):
    count = lax.axis_size(axis)
    up = [(i, i + 1) for i in range(count - 1)]
    down = [(j, i) for i, j in up]
    return lax.ppermute(last, axis, up), lax.ppermute(leading, axis, down)


def with_halo(array, sides, width):
    for axis, dim in sides:
        length = array.shape[dim]
        last = lax.slice_in_dim(array, length - width, length, axis=dim)
        leading = lax.slice_in_dim(array, 0, width, axis=dim)
        before, after = exchange(last, leading, axis)
        array = jnp.concatenate([before, array, after], axis=dim)
    return array


def thermal_step(ext, heat_rows, lateral, vertical):
    cols = jnp.pad(ext, ((0, 0), (0, 0), (1, 1)))
    center = ext[:, 1:-1]
    lap = ext[:, 2:] + ext[:, :-2] + cols[:, 1:-1, 2:] + cols[:, 1:-1, :-2] - 4.0 * center
    flux = vertical[:, None, None] * (center[1:] - center[:-1])
    vert = jnp.pad(flux, ((0, 1), (0, 0), (0, 0))) - jnp.pad(flux, ((1, 0), (0, 0), (0, 0)))
    return center + lateral[:, None, None] * lap + vert + heat_rows


def moment_of(field, weighting):
    total = weighting[0] * field[0]
    for layer in range(1, field.shape[0]):
        total = total + weighting[layer] * field[layer]
    return total


def sweep(w_pad, e_pad, load):
    center = e_pad[1:-1, 1:-1]
    e_up = 0.5 * (center + e_pad[:-2, 1:-1])
    e_down = 0.5 * (center + e_pad[2:, 1:-1])
    e_left = 0.5 * (center + e_pad[1:-1, :-2])
    e_right = 0.5 * (center + e_pad[1:-1, 2:])
    numer = (
        load
        + e_up * w_pad[:-2, 1:-1]
        + e_down * w_pad[2:, 1:-1]
        + e_left * w_pad[1:-1, :-2]
        + e_right * w_pad[1:-1, 2:]
    )
    denom = stiffness + e_up + e_down + e_left + e_right
    return numer / denom


def anand(strain, resist, recv):
    total, inelastic = (strain[0], strain[1])
    increment, theta, live = (recv[0], recv[1], recv[2])
    total_new = total + increment
    arrhen = jnp.exp(2.0 - 2.0 / (1.0 + 0.1 * theta * theta))
    hyper = jnp.sinh(shear_mod * (total_new - inelastic) / resist)
    rate = rate_scale * arrhen * hyper * jnp.abs(hyper)
    inelastic_new = inelastic + rate
    target = sat_level * jnp.power(1.0 + jnp.abs(rate) / arrhen, sat_power)
    resist_new = resist + harden * (1.0 - resist / target) * jnp.abs(rate)
    keep = live > 0.5
    strain_out = jnp.stack(
        [jnp.where(keep, total_new, total), jnp.where(keep, inelastic_new, inelastic)]
    )
    return (strain_out, jnp.where(keep, resist_new, resist))


def as_slab(piece, layers, cols):
    flat = piece.reshape(-1)
    per = layers * cols
    n = -(-flat.shape[0] // per)
    return jnp.pad(flat, (0, n * per - flat.shape[0])).reshape(n, layers, cols).transpose(1, 0, 2)


def from_slab(slab, shape):
    size = 1
    for d in shape:
        size *= d
    return slab.transpose(1, 0, 2).reshape(-1)[:size].reshape(shape)


def thermal(temp, heat, lateral, vertical, extra):
    devices = lax.axis_size(FLAT)
    t = lax.axis_index(FLAT)
    rows = temp.shape[1]
    h = STEPS + extra
    hh = h - 1
    last = jnp.concatenate([temp[:, rows - h:], heat[:, rows - hh:]], axis=1)
    leading = jnp.concatenate([temp[:, :h], heat[:, :hh]], axis=1)
    before, after = exchange(last, leading, FLAT)
    ext = jnp.concatenate([before[:, :h], temp, after[:, :h]], axis=1)
    heat_ext = jnp.concatenate([before[:, h:], heat, after[:, h:]], axis=1)
    for step in range(1, STEPS + 1):
        r = STEPS - step + extra
        heat_rows = heat_ext[:, hh - r: hh - r + rows + 2 * r]
        ext = thermal_step(ext, heat_rows, lateral, vertical)
        if step < STEPS:
            g = t * rows + jnp.arange(-r, rows + r)
            inside = (g >= 0) & (g < devices * rows)
            ext = jnp.where(inside[None, :, None], ext, 0.0)
    return ext


def relay(load, top, width, side_last, side_leading):
    n_gy = lax.axis_size("gy")
    gj = lax.axis_index("gy")
    rows, cols = load.shape
    cm = cols // n_gy
    rows = rows - 2 * width
    lp = jnp.pad(load, ((0, 0), (width, width)))
    tp = jnp.pad(top, ((width, width), (width, width)))
    both = jnp.stack([lp, tp])
    send = jnp.stack([both[:, :, k * cm: k * cm + cm + 2 * width] for k in range(n_gy)])
    depth = send.shape[2]
    got = [lax.dynamic_index_in_dim(send, gj, 0, keepdims=False)]
    side_before = side_after = None
    for shift in range(1, n_gy):
        piece = lax.dynamic_index_in_dim(send, (gj + shift) % n_gy, 0, keepdims=False)
        extras = []
        if shift == 1:
            extras.append(as_slab(side_last, 2, piece.shape[2]))
        if shift == n_gy - 1:
            extras.append(as_slab(side_leading, 2, piece.shape[2]))
        piece = jnp.concatenate([piece] + extras, axis=1)
        moved = lax.ppermute(piece, "gy", [(j, (j + shift) % n_gy) for j in range(n_gy)])
        at = depth
        if shift == 1:
            slab = as_slab(side_last, 2, piece.shape[2])
            side_before = from_slab(moved[:, at: at + slab.shape[1]], side_last.shape)
            at += slab.shape[1]
        if shift == n_gy - 1:
            slab = as_slab(side_leading, 2, piece.shape[2])
            side_after = from_slab(moved[:, at: at + slab.shape[1]], side_leading.shape)
        got.append(moved[:, :depth])
    if side_before is None:
        side_before = jnp.zeros_like(side_last)
        side_after = jnp.zeros_like(side_leading)
    side_before = jnp.where(gj > 0, side_before, 0.0)
    side_after = jnp.where(gj < n_gy - 1, side_after, 0.0)
    recv = jnp.take(jnp.stack(got), (gj - jnp.arange(n_gy)) % n_gy, axis=0)
    parts = []
    for k in range(n_gy):
        lo = 0 if k == 0 else width
        hi = rows + 2 * width if k == n_gy - 1 else rows + width
        parts.append(recv[k, 0, lo:hi])
    load_m = jnp.concatenate(parts, axis=0)
    top_m = jnp.concatenate(
        [recv[k, 1, width: rows + width, width: cm + width] for k in range(n_gy)], axis=0
    )
    return load_m, top_m, side_before, side_after


def joint_ranks(owners, devices):
    count = owners.shape[0]
    block = 128 if count % 128 == 0 else count
    nb = count // block
    onehot = (owners[:, None] == jnp.arange(devices, dtype=jnp.int32)[None, :]).astype(jnp.float32)
    oh = onehot.reshape(nb, block, devices)
    ar = jnp.arange(block)
    tri = (ar[:, None] >= ar[None, :]).astype(jnp.float32)
    within = jnp.einsum("ij,bjd->bid", tri, oh, precision=lax.Precision.HIGHEST)
    totals = within[:, -1, :]
    ab = jnp.arange(nb)
    stri = (ab[:, None] > ab[None, :]).astype(jnp.float32)
    offs = jnp.dot(stri, totals, precision=lax.Precision.HIGHEST)
    cum = (within + offs[:, None, :]).reshape(count, devices)
    return jnp.sum(cum * onehot, axis=1).astype(jnp.int32) - 1


def pick_kernel(rows_ref, cols_ref, parts_ref, out_ref):
    rows = rows_ref[...]
    cols = cols_ref[...]
    block = rows.shape[1]
    _, fields, rm, cm = parts_ref.shape
    hit = lax.broadcasted_iota(jnp.int32, (cm, block), 0) == cols
    onehot = jnp.where(hit, 1.0, 0.0).astype(jnp.bfloat16)
    sel = lax.broadcasted_iota(jnp.int32, (rm, block), 0) == rows
    for f in range(fields):
        acc = jnp.dot(parts_ref[0, f], onehot, preferred_element_type=jnp.float32)
        acc = acc + jnp.dot(parts_ref[1, f], onehot, preferred_element_type=jnp.float32)
        acc = acc + jnp.dot(parts_ref[2, f], onehot, preferred_element_type=jnp.float32)
        out_ref[f: f + 1, :] = jnp.sum(jnp.where(sel, acc, 0.0), axis=0, keepdims=True)


def pick_cells(fields, cells):
    count = cells.shape[0]
    nf, rm, cm = fields.shape
    hi = lax.reduce_precision(fields, exponent_bits=8, mantissa_bits=7)
    rest = fields - hi
    mid = lax.reduce_precision(rest, exponent_bits=8, mantissa_bits=7)
    lo = rest - mid
    parts = jnp.stack([hi, mid, lo]).astype(jnp.bfloat16)
    rows = (cells // cm).astype(jnp.int32)[None, :]
    cols = (cells % cm).astype(jnp.int32)[None, :]
    block = 512 if count % 512 == 0 else count
    return pl.pallas_call(
        pick_kernel,
        grid=(count // block,),
        in_specs=[
            pl.BlockSpec((1, block), lambda i: (0, i)),
            pl.BlockSpec((1, block), lambda i: (0, i)),
            pl.BlockSpec((3, nf, rm, cm), lambda i: (0, 0, 0, 0)),
        ],
        out_specs=pl.BlockSpec((nf, block), lambda i: (0, i)),
        out_shape=jax.ShapeDtypeStruct((nf, count), jnp.float32),
    )(rows, cols, parts)


def body(
    temp_start,
    heat_input,
    lateral,
    vertical,
    weighting,
    modulus,
    warp_prev,
    joint_cell,
    joint_owner,
    joint_strain,
    joint_resist,
):
    devices = lax.axis_size(FLAT)
    n_gx, n_gy = lax.axis_size("gx"), lax.axis_size("gy")
    gi, gj = lax.axis_index("gx"), lax.axis_index("gy")
    rm, cm = warp_prev.shape

    wm = jnp.stack([warp_prev, modulus])
    owners = joint_owner[:, 0]
    capacity = joint_resist.shape[1] // devices
    slots = owners * capacity + joint_ranks(owners, devices)

    extra = SWEEPS - 1
    g = SWEEPS
    wm = with_halo(wm, (("gx", 1),), g)
    temp = thermal(temp_start, heat_input, lateral, vertical, extra)
    load_t = moment_of(temp, weighting)
    load, top, left, right = relay(
        load_t, temp[-1, extra: temp.shape[1] - extra], extra, wm[:, :, cm - g:], wm[:, :, :g])
    wm = jnp.concatenate([left, wm, right], axis=2)

    warp = wm[0]
    mod_ext = wm[1]
    for step in range(1, SWEEPS + 1):
        r = SWEEPS - step
        off = SWEEPS - (r + 1)
        e_pad = mod_ext[off: off + rm + 2 * r + 2, off: off + cm + 2 * r + 2]
        lo = SWEEPS - 1 - r
        ld = load[lo: lo + rm + 2 * r, lo: lo + cm + 2 * r]
        warp = sweep(warp, e_pad, ld)
        if r > 0:
            gr = gi * rm + jnp.arange(-r, rm + r)
            gc = gj * cm + jnp.arange(-r, cm + r)
            inside = ((gr >= 0) & (gr < n_gx * rm))[:, None] & ((gc >= 0) & (gc < n_gy * cm))[None, :]
            warp = jnp.where(inside, warp, 0.0)

    picked = pick_cells(jnp.stack([warp - warp_prev, top]), joint_cell)
    values = jnp.concatenate([picked, jnp.ones_like(picked[:1])], axis=0)
    outgoing = jnp.zeros((3, devices * capacity), jnp.float32).at[:, slots].set(values)
    incoming = lax.all_to_all(outgoing, FLAT, split_axis=1, concat_axis=1, tiled=True)
    strain_next, resist_next = anand(joint_strain, joint_resist, incoming[:, None, :])
    return (warp, strain_next, resist_next)


def solution(mesh):
    return jax.shard_map(
        body,
        mesh=mesh,
        in_specs=(
            P(None, FLAT, None),
            P(None, FLAT, None),
            P(),
            P(),
            P(),
            P("gx", "gy"),
            P("gx", "gy"),
            P(FLAT),
            P(FLAT, None),
            P(None, FLAT, None),
            P(FLAT, None),
        ),
        out_specs=(P("gx", "gy"), P(None, FLAT, None), P(FLAT, None)),
        check_vma=False,
    )
```

```python
import jax
import jax.numpy as jnp
from jax import lax
from jax.sharding import PartitionSpec as P
from jax.experimental import pallas as pl

STEPS = 2
SWEEPS = 3


stiffness = 0.2
shear_mod = 0.6
rate_scale = 0.5
sat_level = 2.5
sat_power = 0.3
harden = 2.0

FLAT = ("gx", "gy")


def exchange(last, leading, axis):
    count = lax.axis_size(axis)
    up = [(i, i + 1) for i in range(count - 1)]
    down = [(j, i) for i, j in up]
    return lax.ppermute(last, axis, up), lax.ppermute(leading, axis, down)


def with_halo(array, sides, width):
    for axis, dim in sides:
        length = array.shape[dim]
        last = lax.slice_in_dim(array, length - width, length, axis=dim)
        leading = lax.slice_in_dim(array, 0, width, axis=dim)
        before, after = exchange(last, leading, axis)
        array = jnp.concatenate([before, array, after], axis=dim)
    return array


def thermal_step(ext, heat_rows, lateral, vertical):
    cols = jnp.pad(ext, ((0, 0), (0, 0), (1, 1)))
    center = ext[:, 1:-1]
    lap = ext[:, 2:] + ext[:, :-2] + cols[:, 1:-1, 2:] + cols[:, 1:-1, :-2] - 4.0 * center
    flux = vertical[:, None, None] * (center[1:] - center[:-1])
    vert = jnp.pad(flux, ((0, 1), (0, 0), (0, 0))) - jnp.pad(flux, ((1, 0), (0, 0), (0, 0)))
    return center + lateral[:, None, None] * lap + vert + heat_rows


def moment_of(field, weighting):
    total = weighting[0] * field[0]
    for layer in range(1, field.shape[0]):
        total = total + weighting[layer] * field[layer]
    return total


def sweep(w_pad, e_pad, load):
    center = e_pad[1:-1, 1:-1]
    e_up = 0.5 * (center + e_pad[:-2, 1:-1])
    e_down = 0.5 * (center + e_pad[2:, 1:-1])
    e_left = 0.5 * (center + e_pad[1:-1, :-2])
    e_right = 0.5 * (center + e_pad[1:-1, 2:])
    numer = (
        load
        + e_up * w_pad[:-2, 1:-1]
        + e_down * w_pad[2:, 1:-1]
        + e_left * w_pad[1:-1, :-2]
        + e_right * w_pad[1:-1, 2:]
    )
    denom = stiffness + e_up + e_down + e_left + e_right
    return numer / denom


def anand(strain, resist, recv):
    total, inelastic = (strain[0], strain[1])
    increment, theta, live = (recv[0], recv[1], recv[2])
    total_new = total + increment
    arrhen = jnp.exp(2.0 - 2.0 / (1.0 + 0.1 * theta * theta))
    hyper = jnp.sinh(shear_mod * (total_new - inelastic) / resist)
    rate = rate_scale * arrhen * hyper * jnp.abs(hyper)
    inelastic_new = inelastic + rate
    target = sat_level * jnp.power(1.0 + jnp.abs(rate) / arrhen, sat_power)
    resist_new = resist + harden * (1.0 - resist / target) * jnp.abs(rate)
    keep = live > 0.5
    strain_out = jnp.stack(
        [jnp.where(keep, total_new, total), jnp.where(keep, inelastic_new, inelastic)]
    )
    return (strain_out, jnp.where(keep, resist_new, resist))


def as_slab(piece, layers, cols):
    flat = piece.reshape(-1)
    per = layers * cols
    n = -(-flat.shape[0] // per)
    return jnp.pad(flat, (0, n * per - flat.shape[0])).reshape(n, layers, cols).transpose(1, 0, 2)


def from_slab(slab, shape):
    size = 1
    for d in shape:
        size *= d
    return slab.transpose(1, 0, 2).reshape(-1)[:size].reshape(shape)


def thermal(temp, heat, lateral, vertical, extra):
    devices = lax.axis_size(FLAT)
    t = lax.axis_index(FLAT)
    rows = temp.shape[1]
    h = STEPS + extra
    hh = h - 1
    last = jnp.concatenate([temp[:, rows - h:], heat[:, rows - hh:]], axis=1)
    leading = jnp.concatenate([temp[:, :h], heat[:, :hh]], axis=1)
    before, after = exchange(last, leading, FLAT)
    ext = jnp.concatenate([before[:, :h], temp, after[:, :h]], axis=1)
    heat_ext = jnp.concatenate([before[:, h:], heat, after[:, h:]], axis=1)
    for step in range(1, STEPS + 1):
        r = STEPS - step + extra
        heat_rows = heat_ext[:, hh - r: hh - r + rows + 2 * r]
        ext = thermal_step(ext, heat_rows, lateral, vertical)
        if step < STEPS:
            g = t * rows + jnp.arange(-r, rows + r)
            inside = (g >= 0) & (g < devices * rows)
            ext = jnp.where(inside[None, :, None], ext, 0.0)
    return ext


def relay(load, top, width, side_last, side_leading):
    n_gy = lax.axis_size("gy")
    gj = lax.axis_index("gy")
    rows, cols = load.shape
    cm = cols // n_gy
    rows = rows - 2 * width
    lp = jnp.pad(load, ((0, 0), (width, width)))
    tp = jnp.pad(top, ((width, width), (width, width)))
    both = jnp.stack([lp, tp])
    send = jnp.stack([both[:, :, k * cm: k * cm + cm + 2 * width] for k in range(n_gy)])
    depth = send.shape[2]
    got = [lax.dynamic_index_in_dim(send, gj, 0, keepdims=False)]
    side_before = side_after = None
    for shift in range(1, n_gy):
        piece = lax.dynamic_index_in_dim(send, (gj + shift) % n_gy, 0, keepdims=False)
        extras = []
        if shift == 1:
            extras.append(as_slab(side_last, 2, piece.shape[2]))
        if shift == n_gy - 1:
            extras.append(as_slab(side_leading, 2, piece.shape[2]))
        piece = jnp.concatenate([piece] + extras, axis=1)
        moved = lax.ppermute(piece, "gy", [(j, (j + shift) % n_gy) for j in range(n_gy)])
        at = depth
        if shift == 1:
            slab = as_slab(side_last, 2, piece.shape[2])
            side_before = from_slab(moved[:, at: at + slab.shape[1]], side_last.shape)
            at += slab.shape[1]
        if shift == n_gy - 1:
            slab = as_slab(side_leading, 2, piece.shape[2])
            side_after = from_slab(moved[:, at: at + slab.shape[1]], side_leading.shape)
        got.append(moved[:, :depth])
    if side_before is None:
        side_before = jnp.zeros_like(side_last)
        side_after = jnp.zeros_like(side_leading)
    side_before = jnp.where(gj > 0, side_before, 0.0)
    side_after = jnp.where(gj < n_gy - 1, side_after, 0.0)
    recv = jnp.take(jnp.stack(got), (gj - jnp.arange(n_gy)) % n_gy, axis=0)
    parts = []
    for k in range(n_gy):
        lo = 0 if k == 0 else width
        hi = rows + 2 * width if k == n_gy - 1 else rows + width
        parts.append(recv[k, 0, lo:hi])
    load_m = jnp.concatenate(parts, axis=0)
    top_m = jnp.concatenate(
        [recv[k, 1, width: rows + width, width: cm + width] for k in range(n_gy)], axis=0
    )
    return load_m, top_m, side_before, side_after


def joint_ranks(owners, devices):
    count = owners.shape[0]
    block = 128 if count % 128 == 0 else count
    nb = count // block
    onehot = (owners[:, None] == jnp.arange(devices, dtype=jnp.int32)[None, :]).astype(jnp.float32)
    oh = onehot.reshape(nb, block, devices)
    ar = jnp.arange(block)
    tri = (ar[:, None] >= ar[None, :]).astype(jnp.float32)
    within = jnp.einsum("ij,bjd->bid", tri, oh, precision=lax.Precision.HIGHEST)
    totals = within[:, -1, :]
    ab = jnp.arange(nb)
    stri = (ab[:, None] > ab[None, :]).astype(jnp.float32)
    offs = jnp.dot(stri, totals, precision=lax.Precision.HIGHEST)
    cum = (within + offs[:, None, :]).reshape(count, devices)
    return jnp.sum(cum * onehot, axis=1).astype(jnp.int32) - 1


def pick_kernel(rows_ref, cols_ref, parts_ref, out_ref):
    rows = rows_ref[...]
    cols = cols_ref[...]
    block = rows.shape[1]
    _, fields, rm, cm = parts_ref.shape
    hit = lax.broadcasted_iota(jnp.int32, (cm, block), 0) == cols
    onehot = jnp.where(hit, 1.0, 0.0).astype(jnp.bfloat16)
    sel = lax.broadcasted_iota(jnp.int32, (rm, block), 0) == rows
    for f in range(fields):
        acc = jnp.dot(parts_ref[0, f], onehot, preferred_element_type=jnp.float32)
        acc = acc + jnp.dot(parts_ref[1, f], onehot, preferred_element_type=jnp.float32)
        acc = acc + jnp.dot(parts_ref[2, f], onehot, preferred_element_type=jnp.float32)
        out_ref[f: f + 1, :] = jnp.sum(jnp.where(sel, acc, 0.0), axis=0, keepdims=True)


def pick_cells(fields, cells):
    count = cells.shape[0]
    nf, rm, cm = fields.shape
    hi = lax.reduce_precision(fields, exponent_bits=8, mantissa_bits=7)
    rest = fields - hi
    mid = lax.reduce_precision(rest, exponent_bits=8, mantissa_bits=7)
    lo = rest - mid
    parts = jnp.stack([hi, mid, lo]).astype(jnp.bfloat16)
    rows = (cells // cm).astype(jnp.int32)[None, :]
    cols = (cells % cm).astype(jnp.int32)[None, :]
    block = 512 if count % 512 == 0 else count
    return pl.pallas_call(
        pick_kernel,
        grid=(count // block,),
        in_specs=[
            pl.BlockSpec((1, block), lambda i: (0, i)),
            pl.BlockSpec((1, block), lambda i: (0, i)),
            pl.BlockSpec((3, nf, rm, cm), lambda i: (0, 0, 0, 0)),
        ],
        out_specs=pl.BlockSpec((nf, block), lambda i: (0, i)),
        out_shape=jax.ShapeDtypeStruct((nf, count), jnp.float32),
    )(rows, cols, parts)


def place_kernel(owners_ref, ranks_ref, parts_ref, out_ref):
    owners = owners_ref[...]
    ranks = ranks_ref[...]
    _, fields, count = parts_ref.shape
    devices, cap = out_ref.shape[1:]
    mine = lax.broadcasted_iota(jnp.int32, (devices, count), 0) == owners
    slot = lax.broadcasted_iota(jnp.int32, (count, cap), 1) == ranks
    at = jnp.where(slot, 1.0, 0.0).astype(jnp.bfloat16)
    for f in range(fields):
        acc = None
        for p in range(3):
            spread = jnp.where(mine, parts_ref[p, f: f + 1, :], 0.0).astype(jnp.bfloat16)
            term = jnp.dot(spread, at, preferred_element_type=jnp.float32)
            acc = term if acc is None else acc + term
        out_ref[f] = acc
    live = jnp.where(mine, 1.0, 0.0).astype(jnp.bfloat16)
    out_ref[fields] = jnp.dot(live, at, preferred_element_type=jnp.float32)


def place_joints(values, owners, ranks, devices, cap):
    nf, count = values.shape
    hi = lax.reduce_precision(values, exponent_bits=8, mantissa_bits=7)
    rest = values - hi
    mid = lax.reduce_precision(rest, exponent_bits=8, mantissa_bits=7)
    lo = rest - mid
    parts = jnp.stack([hi, mid, lo]).astype(jnp.float32)
    return pl.pallas_call(
        place_kernel,
        out_shape=jax.ShapeDtypeStruct((nf + 1, devices, cap), jnp.float32),
    )(owners[None, :].astype(jnp.int32), ranks[:, None].astype(jnp.int32), parts)


def body(
    temp_start,
    heat_input,
    lateral,
    vertical,
    weighting,
    modulus,
    warp_prev,
    joint_cell,
    joint_owner,
    joint_strain,
    joint_resist,
):
    devices = lax.axis_size(FLAT)
    n_gx, n_gy = lax.axis_size("gx"), lax.axis_size("gy")
    gi, gj = lax.axis_index("gx"), lax.axis_index("gy")
    rm, cm = warp_prev.shape

    wm = jnp.stack([warp_prev, modulus])
    owners = joint_owner[:, 0]
    capacity = joint_resist.shape[1] // devices
    ranks = joint_ranks(owners, devices)

    extra = SWEEPS - 1
    g = SWEEPS
    wm = with_halo(wm, (("gx", 1),), g)
    temp = thermal(temp_start, heat_input, lateral, vertical, extra)
    load_t = moment_of(temp, weighting)
    load, top, left, right = relay(
        load_t, temp[-1, extra: temp.shape[1] - extra], extra, wm[:, :, cm - g:], wm[:, :, :g])
    wm = jnp.concatenate([left, wm, right], axis=2)

    warp = wm[0]
    mod_ext = wm[1]
    for step in range(1, SWEEPS + 1):
        r = SWEEPS - step
        off = SWEEPS - (r + 1)
        e_pad = mod_ext[off: off + rm + 2 * r + 2, off: off + cm + 2 * r + 2]
        lo = SWEEPS - 1 - r
        ld = load[lo: lo + rm + 2 * r, lo: lo + cm + 2 * r]
        warp = sweep(warp, e_pad, ld)
        if r > 0:
            gr = gi * rm + jnp.arange(-r, rm + r)
            gc = gj * cm + jnp.arange(-r, cm + r)
            inside = ((gr >= 0) & (gr < n_gx * rm))[:, None] & ((gc >= 0) & (gc < n_gy * cm))[None, :]
            warp = jnp.where(inside, warp, 0.0)

    picked = pick_cells(jnp.stack([warp - warp_prev, top]), joint_cell)
    outgoing = place_joints(picked, owners, ranks, devices, capacity)
    incoming = lax.all_to_all(outgoing, FLAT, split_axis=1, concat_axis=1, tiled=True)
    incoming = incoming.reshape(incoming.shape[0], devices * capacity)
    strain_next, resist_next = anand(joint_strain, joint_resist, incoming[:, None, :])
    return (warp, strain_next, resist_next)


def solution(mesh):
    return jax.shard_map(
        body,
        mesh=mesh,
        in_specs=(
            P(None, FLAT, None),
            P(None, FLAT, None),
            P(),
            P(),
            P(),
            P("gx", "gy"),
            P("gx", "gy"),
            P(FLAT),
            P(FLAT, None),
            P(None, FLAT, None),
            P(FLAT, None),
        ),
        out_specs=(P("gx", "gy"), P(None, FLAT, None), P(FLAT, None)),
        check_vma=False,
    )
```

```python
import jax
import jax.numpy as jnp
from jax import lax
from jax.sharding import PartitionSpec as P
from jax.experimental import pallas as pl

STEPS = 2
SWEEPS = 3


stiffness = 0.2
shear_mod = 0.6
rate_scale = 0.5
sat_level = 2.5
sat_power = 0.3
harden = 2.0

FLAT = ("gx", "gy")


def exchange(last, leading, axis):
    count = lax.axis_size(axis)
    up = [(i, i + 1) for i in range(count - 1)]
    down = [(j, i) for i, j in up]
    return lax.ppermute(last, axis, up), lax.ppermute(leading, axis, down)


def with_halo(array, sides, width):
    for axis, dim in sides:
        length = array.shape[dim]
        last = lax.slice_in_dim(array, length - width, length, axis=dim)
        leading = lax.slice_in_dim(array, 0, width, axis=dim)
        before, after = exchange(last, leading, axis)
        array = jnp.concatenate([before, array, after], axis=dim)
    return array


def thermal_step(ext, heat_rows, lateral, vertical):
    cols = jnp.pad(ext, ((0, 0), (0, 0), (1, 1)))
    center = ext[:, 1:-1]
    lap = ext[:, 2:] + ext[:, :-2] + cols[:, 1:-1, 2:] + cols[:, 1:-1, :-2] - 4.0 * center
    flux = vertical[:, None, None] * (center[1:] - center[:-1])
    vert = jnp.pad(flux, ((0, 1), (0, 0), (0, 0))) - jnp.pad(flux, ((1, 0), (0, 0), (0, 0)))
    return center + lateral[:, None, None] * lap + vert + heat_rows


def moment_of(field, weighting):
    total = weighting[0] * field[0]
    for layer in range(1, field.shape[0]):
        total = total + weighting[layer] * field[layer]
    return total


def sweep(w_pad, e_pad, load):
    center = e_pad[1:-1, 1:-1]
    e_up = 0.5 * (center + e_pad[:-2, 1:-1])
    e_down = 0.5 * (center + e_pad[2:, 1:-1])
    e_left = 0.5 * (center + e_pad[1:-1, :-2])
    e_right = 0.5 * (center + e_pad[1:-1, 2:])
    numer = (
        load
        + e_up * w_pad[:-2, 1:-1]
        + e_down * w_pad[2:, 1:-1]
        + e_left * w_pad[1:-1, :-2]
        + e_right * w_pad[1:-1, 2:]
    )
    denom = stiffness + e_up + e_down + e_left + e_right
    return numer / denom


def anand(strain, resist, recv):
    total, inelastic = (strain[0], strain[1])
    increment, theta, live = (recv[0], recv[1], recv[2])
    total_new = total + increment
    arrhen = jnp.exp(2.0 - 2.0 / (1.0 + 0.1 * theta * theta))
    hyper = jnp.sinh(shear_mod * (total_new - inelastic) / resist)
    rate = rate_scale * arrhen * hyper * jnp.abs(hyper)
    inelastic_new = inelastic + rate
    target = sat_level * jnp.power(1.0 + jnp.abs(rate) / arrhen, sat_power)
    resist_new = resist + harden * (1.0 - resist / target) * jnp.abs(rate)
    keep = live > 0.5
    strain_out = jnp.stack(
        [jnp.where(keep, total_new, total), jnp.where(keep, inelastic_new, inelastic)]
    )
    return (strain_out, jnp.where(keep, resist_new, resist))


def as_slab(piece, layers, cols):
    flat = piece.reshape(-1)
    per = layers * cols
    n = -(-flat.shape[0] // per)
    return jnp.pad(flat, (0, n * per - flat.shape[0])).reshape(n, layers, cols).transpose(1, 0, 2)


def from_slab(slab, shape):
    size = 1
    for d in shape:
        size *= d
    return slab.transpose(1, 0, 2).reshape(-1)[:size].reshape(shape)


def thermal(temp, heat, lateral, vertical, extra):
    devices = lax.axis_size(FLAT)
    t = lax.axis_index(FLAT)
    rows = temp.shape[1]
    h = STEPS + extra
    hh = h - 1
    last = jnp.concatenate([temp[:, rows - h:], heat[:, rows - hh:]], axis=1)
    leading = jnp.concatenate([temp[:, :h], heat[:, :hh]], axis=1)
    half = last.shape[0] // 2
    lo_b, lo_a = exchange(last[:half], leading[:half], FLAT)
    hi_b, hi_a = exchange(last[half:], leading[half:], FLAT)
    before = jnp.concatenate([lo_b, hi_b], axis=0)
    after = jnp.concatenate([lo_a, hi_a], axis=0)
    ext = jnp.concatenate([before[:, :h], temp, after[:, :h]], axis=1)
    heat_ext = jnp.concatenate([before[:, h:], heat, after[:, h:]], axis=1)
    for step in range(1, STEPS + 1):
        r = STEPS - step + extra
        heat_rows = heat_ext[:, hh - r: hh - r + rows + 2 * r]
        ext = thermal_step(ext, heat_rows, lateral, vertical)
        if step < STEPS:
            g = t * rows + jnp.arange(-r, rows + r)
            inside = (g >= 0) & (g < devices * rows)
            ext = jnp.where(inside[None, :, None], ext, 0.0)
    return ext


def relay(load, top, width, side_last, side_leading):
    n_gy = lax.axis_size("gy")
    gj = lax.axis_index("gy")
    rows, cols = load.shape
    cm = cols // n_gy
    rows = rows - 2 * width
    lp = jnp.pad(load, ((0, 0), (width, width)))
    tp = jnp.pad(top, ((width, width), (width, width)))
    both = jnp.stack([lp, tp])
    send = jnp.stack([both[:, :, k * cm: k * cm + cm + 2 * width] for k in range(n_gy)])
    depth = send.shape[2]
    got = [lax.dynamic_index_in_dim(send, gj, 0, keepdims=False)]
    side_before = side_after = None
    for shift in range(1, n_gy):
        piece = lax.dynamic_index_in_dim(send, (gj + shift) % n_gy, 0, keepdims=False)
        extras = []
        if shift == 1:
            extras.append(as_slab(side_last, 2, piece.shape[2]))
        if shift == n_gy - 1:
            extras.append(as_slab(side_leading, 2, piece.shape[2]))
        piece = jnp.concatenate([piece] + extras, axis=1)
        moved = lax.ppermute(piece, "gy", [(j, (j + shift) % n_gy) for j in range(n_gy)])
        at = depth
        if shift == 1:
            slab = as_slab(side_last, 2, piece.shape[2])
            side_before = from_slab(moved[:, at: at + slab.shape[1]], side_last.shape)
            at += slab.shape[1]
        if shift == n_gy - 1:
            slab = as_slab(side_leading, 2, piece.shape[2])
            side_after = from_slab(moved[:, at: at + slab.shape[1]], side_leading.shape)
        got.append(moved[:, :depth])
    if side_before is None:
        side_before = jnp.zeros_like(side_last)
        side_after = jnp.zeros_like(side_leading)
    side_before = jnp.where(gj > 0, side_before, 0.0)
    side_after = jnp.where(gj < n_gy - 1, side_after, 0.0)
    recv = jnp.take(jnp.stack(got), (gj - jnp.arange(n_gy)) % n_gy, axis=0)
    parts = []
    for k in range(n_gy):
        lo = 0 if k == 0 else width
        hi = rows + 2 * width if k == n_gy - 1 else rows + width
        parts.append(recv[k, 0, lo:hi])
    load_m = jnp.concatenate(parts, axis=0)
    top_m = jnp.concatenate(
        [recv[k, 1, width: rows + width, width: cm + width] for k in range(n_gy)], axis=0
    )
    return load_m, top_m, side_before, side_after


def joint_ranks(owners, devices):
    count = owners.shape[0]
    block = 128 if count % 128 == 0 else count
    nb = count // block
    onehot = (owners[:, None] == jnp.arange(devices, dtype=jnp.int32)[None, :]).astype(jnp.float32)
    oh = onehot.reshape(nb, block, devices)
    ar = jnp.arange(block)
    tri = (ar[:, None] >= ar[None, :]).astype(jnp.float32)
    within = jnp.einsum("ij,bjd->bid", tri, oh, precision=lax.Precision.HIGHEST)
    totals = within[:, -1, :]
    ab = jnp.arange(nb)
    stri = (ab[:, None] > ab[None, :]).astype(jnp.float32)
    offs = jnp.dot(stri, totals, precision=lax.Precision.HIGHEST)
    cum = (within + offs[:, None, :]).reshape(count, devices)
    return jnp.sum(cum * onehot, axis=1).astype(jnp.int32) - 1


def pick_kernel(rows_ref, cols_ref, parts_ref, out_ref):
    rows = rows_ref[...]
    cols = cols_ref[...]
    block = rows.shape[1]
    _, fields, rm, cm = parts_ref.shape
    hit = lax.broadcasted_iota(jnp.int32, (cm, block), 0) == cols
    onehot = jnp.where(hit, 1.0, 0.0).astype(jnp.bfloat16)
    sel = lax.broadcasted_iota(jnp.int32, (rm, block), 0) == rows
    for f in range(fields):
        acc = jnp.dot(parts_ref[0, f], onehot, preferred_element_type=jnp.float32)
        acc = acc + jnp.dot(parts_ref[1, f], onehot, preferred_element_type=jnp.float32)
        acc = acc + jnp.dot(parts_ref[2, f], onehot, preferred_element_type=jnp.float32)
        out_ref[f: f + 1, :] = jnp.sum(jnp.where(sel, acc, 0.0), axis=0, keepdims=True)


def pick_cells(fields, cells):
    count = cells.shape[0]
    nf, rm, cm = fields.shape
    hi = lax.reduce_precision(fields, exponent_bits=8, mantissa_bits=7)
    rest = fields - hi
    mid = lax.reduce_precision(rest, exponent_bits=8, mantissa_bits=7)
    lo = rest - mid
    parts = jnp.stack([hi, mid, lo]).astype(jnp.bfloat16)
    rows = (cells // cm).astype(jnp.int32)[None, :]
    cols = (cells % cm).astype(jnp.int32)[None, :]
    block = 512 if count % 512 == 0 else count
    return pl.pallas_call(
        pick_kernel,
        grid=(count // block,),
        in_specs=[
            pl.BlockSpec((1, block), lambda i: (0, i)),
            pl.BlockSpec((1, block), lambda i: (0, i)),
            pl.BlockSpec((3, nf, rm, cm), lambda i: (0, 0, 0, 0)),
        ],
        out_specs=pl.BlockSpec((nf, block), lambda i: (0, i)),
        out_shape=jax.ShapeDtypeStruct((nf, count), jnp.float32),
    )(rows, cols, parts)


def place_kernel(owners_ref, ranks_ref, parts_ref, out_ref):
    owners = owners_ref[...]
    ranks = ranks_ref[...]
    _, fields, count = parts_ref.shape
    devices, cap = out_ref.shape[1:]
    mine = lax.broadcasted_iota(jnp.int32, (devices, count), 0) == owners
    slot = lax.broadcasted_iota(jnp.int32, (count, cap), 1) == ranks
    at = jnp.where(slot, 1.0, 0.0).astype(jnp.bfloat16)
    for f in range(fields):
        acc = None
        for p in range(3):
            spread = jnp.where(mine, parts_ref[p, f: f + 1, :], 0.0).astype(jnp.bfloat16)
            term = jnp.dot(spread, at, preferred_element_type=jnp.float32)
            acc = term if acc is None else acc + term
        out_ref[f] = acc
    live = jnp.where(mine, 1.0, 0.0).astype(jnp.bfloat16)
    out_ref[fields] = jnp.dot(live, at, preferred_element_type=jnp.float32)


def place_joints(values, owners, ranks, devices, cap):
    nf, count = values.shape
    hi = lax.reduce_precision(values, exponent_bits=8, mantissa_bits=7)
    rest = values - hi
    mid = lax.reduce_precision(rest, exponent_bits=8, mantissa_bits=7)
    lo = rest - mid
    parts = jnp.stack([hi, mid, lo]).astype(jnp.float32)
    return pl.pallas_call(
        place_kernel,
        out_shape=jax.ShapeDtypeStruct((nf + 1, devices, cap), jnp.float32),
    )(owners[None, :].astype(jnp.int32), ranks[:, None].astype(jnp.int32), parts)


def body(
    temp_start,
    heat_input,
    lateral,
    vertical,
    weighting,
    modulus,
    warp_prev,
    joint_cell,
    joint_owner,
    joint_strain,
    joint_resist,
):
    devices = lax.axis_size(FLAT)
    n_gx, n_gy = lax.axis_size("gx"), lax.axis_size("gy")
    gi, gj = lax.axis_index("gx"), lax.axis_index("gy")
    rm, cm = warp_prev.shape

    wm = jnp.stack([warp_prev, modulus])
    owners = joint_owner[:, 0]
    capacity = joint_resist.shape[1] // devices
    ranks = joint_ranks(owners, devices)

    extra = SWEEPS - 1
    g = SWEEPS
    wm = with_halo(wm, (("gx", 1),), g)
    temp = thermal(temp_start, heat_input, lateral, vertical, extra)
    load_t = moment_of(temp, weighting)
    load, top, left, right = relay(
        load_t, temp[-1, extra: temp.shape[1] - extra], extra, wm[:, :, cm - g:], wm[:, :, :g])
    wm = jnp.concatenate([left, wm, right], axis=2)

    warp = wm[0]
    mod_ext = wm[1]
    for step in range(1, SWEEPS + 1):
        r = SWEEPS - step
        off = SWEEPS - (r + 1)
        e_pad = mod_ext[off: off + rm + 2 * r + 2, off: off + cm + 2 * r + 2]
        lo = SWEEPS - 1 - r
        ld = load[lo: lo + rm + 2 * r, lo: lo + cm + 2 * r]
        warp = sweep(warp, e_pad, ld)
        if r > 0:
            gr = gi * rm + jnp.arange(-r, rm + r)
            gc = gj * cm + jnp.arange(-r, cm + r)
            inside = ((gr >= 0) & (gr < n_gx * rm))[:, None] & ((gc >= 0) & (gc < n_gy * cm))[None, :]
            warp = jnp.where(inside, warp, 0.0)

    picked = pick_cells(jnp.stack([warp - warp_prev, top]), joint_cell)
    outgoing = place_joints(picked, owners, ranks, devices, capacity)
    incoming = lax.all_to_all(outgoing, FLAT, split_axis=1, concat_axis=1, tiled=True)
    incoming = incoming.reshape(incoming.shape[0], devices * capacity)
    strain_next, resist_next = anand(joint_strain, joint_resist, incoming[:, None, :])
    return (warp, strain_next, resist_next)


def solution(mesh):
    return jax.shard_map(
        body,
        mesh=mesh,
        in_specs=(
            P(None, FLAT, None),
            P(None, FLAT, None),
            P(),
            P(),
            P(),
            P("gx", "gy"),
            P("gx", "gy"),
            P(FLAT),
            P(FLAT, None),
            P(None, FLAT, None),
            P(FLAT, None),
        ),
        out_specs=(P("gx", "gy"), P(None, FLAT, None), P(FLAT, None)),
        check_vma=False,
    )
```

```python
import jax
import jax.numpy as jnp
from jax import lax
from jax.sharding import PartitionSpec as P
from jax.experimental import pallas as pl

STEPS = 2
SWEEPS = 3


stiffness = 0.2
shear_mod = 0.6
rate_scale = 0.5
sat_level = 2.5
sat_power = 0.3
harden = 2.0

FLAT = ("gx", "gy")


def exchange(last, leading, axis):
    count = lax.axis_size(axis)
    up = [(i, i + 1) for i in range(count - 1)]
    down = [(j, i) for i, j in up]
    return lax.ppermute(last, axis, up), lax.ppermute(leading, axis, down)


def with_halo(array, sides, width):
    for axis, dim in sides:
        length = array.shape[dim]
        last = lax.slice_in_dim(array, length - width, length, axis=dim)
        leading = lax.slice_in_dim(array, 0, width, axis=dim)
        before, after = exchange(last, leading, axis)
        array = jnp.concatenate([before, array, after], axis=dim)
    return array


def thermal_step(ext, heat_rows, lateral, vertical):
    cols = jnp.pad(ext, ((0, 0), (0, 0), (1, 1)))
    center = ext[:, 1:-1]
    lap = ext[:, 2:] + ext[:, :-2] + cols[:, 1:-1, 2:] + cols[:, 1:-1, :-2] - 4.0 * center
    flux = vertical[:, None, None] * (center[1:] - center[:-1])
    vert = jnp.pad(flux, ((0, 1), (0, 0), (0, 0))) - jnp.pad(flux, ((1, 0), (0, 0), (0, 0)))
    return center + lateral[:, None, None] * lap + vert + heat_rows


def moment_of(field, weighting):
    total = weighting[0] * field[0]
    for layer in range(1, field.shape[0]):
        total = total + weighting[layer] * field[layer]
    return total


def sweep(w_pad, e_pad, load):
    center = e_pad[1:-1, 1:-1]
    e_up = 0.5 * (center + e_pad[:-2, 1:-1])
    e_down = 0.5 * (center + e_pad[2:, 1:-1])
    e_left = 0.5 * (center + e_pad[1:-1, :-2])
    e_right = 0.5 * (center + e_pad[1:-1, 2:])
    numer = (
        load
        + e_up * w_pad[:-2, 1:-1]
        + e_down * w_pad[2:, 1:-1]
        + e_left * w_pad[1:-1, :-2]
        + e_right * w_pad[1:-1, 2:]
    )
    denom = stiffness + e_up + e_down + e_left + e_right
    return numer / denom


def anand(strain, resist, recv):
    total, inelastic = (strain[0], strain[1])
    increment, theta, live = (recv[0], recv[1], recv[2])
    total_new = total + increment
    arrhen = jnp.exp(2.0 - 2.0 / (1.0 + 0.1 * theta * theta))
    hyper = jnp.sinh(shear_mod * (total_new - inelastic) / resist)
    rate = rate_scale * arrhen * hyper * jnp.abs(hyper)
    inelastic_new = inelastic + rate
    target = sat_level * jnp.power(1.0 + jnp.abs(rate) / arrhen, sat_power)
    resist_new = resist + harden * (1.0 - resist / target) * jnp.abs(rate)
    keep = live > 0.5
    strain_out = jnp.stack(
        [jnp.where(keep, total_new, total), jnp.where(keep, inelastic_new, inelastic)]
    )
    return (strain_out, jnp.where(keep, resist_new, resist))


def as_slab(piece, layers, cols):
    flat = piece.reshape(-1)
    per = layers * cols
    n = -(-flat.shape[0] // per)
    return jnp.pad(flat, (0, n * per - flat.shape[0])).reshape(n, layers, cols).transpose(1, 0, 2)


def from_slab(slab, shape):
    size = 1
    for d in shape:
        size *= d
    return slab.transpose(1, 0, 2).reshape(-1)[:size].reshape(shape)


def thermal(temp, heat, lateral, vertical, extra):
    devices = lax.axis_size(FLAT)
    t = lax.axis_index(FLAT)
    rows = temp.shape[1]
    h = STEPS + extra
    hh = h - 1
    n_gx, n_gy = lax.axis_size("gx"), lax.axis_size("gy")
    bt, bh = STEPS, STEPS - 1
    last = jnp.concatenate([temp[:, rows - bt:], heat[:, rows - bh:]], axis=1)
    leading = jnp.concatenate([temp[:, :bt], heat[:, :bh]], axis=1)
    before, after = exchange(last, leading, FLAT)
    far_last = jnp.concatenate([temp[:, rows - h: rows - bt], heat[:, rows - hh: rows - bh]], axis=1)
    far_leading = jnp.concatenate([temp[:, bt:h], heat[:, bh:hh]], axis=1)
    up = [(i * n_gy + n_gy - 1, (i + 1) * n_gy) for i in range(n_gx - 1)]
    far_before = lax.ppermute(far_last, FLAT, up)
    far_after = lax.ppermute(far_leading, FLAT, [(b, a) for a, b in up])
    before = jnp.concatenate(
        [far_before[:, :extra], before[:, :bt], far_before[:, extra:], before[:, bt:]], axis=1)
    after = jnp.concatenate(
        [after[:, :bt], far_after[:, :extra], after[:, bt:], far_after[:, extra:]], axis=1)
    before, after = lax.optimization_barrier((before, after))
    ext = jnp.concatenate([before[:, :h], temp, after[:, :h]], axis=1)
    heat_ext = jnp.concatenate([before[:, h:], heat, after[:, h:]], axis=1)
    for step in range(1, STEPS + 1):
        r = STEPS - step + extra
        heat_rows = heat_ext[:, hh - r: hh - r + rows + 2 * r]
        ext = thermal_step(ext, heat_rows, lateral, vertical)
        if step < STEPS:
            g = t * rows + jnp.arange(-r, rows + r)
            inside = (g >= 0) & (g < devices * rows)
            ext = jnp.where(inside[None, :, None], ext, 0.0)
    return ext


def relay(load, top, width, side_last, side_leading):
    n_gy = lax.axis_size("gy")
    gj = lax.axis_index("gy")
    rows, cols = load.shape
    cm = cols // n_gy
    rows = rows - 2 * width
    lp = jnp.pad(load, ((0, 0), (width, width)))
    tp = jnp.pad(top, ((width, width), (width, width)))
    both = jnp.stack([lp, tp])
    send = jnp.stack([both[:, :, k * cm: k * cm + cm + 2 * width] for k in range(n_gy)])
    depth = send.shape[2]
    got = [lax.dynamic_index_in_dim(send, gj, 0, keepdims=False)]
    side_before = side_after = None
    for shift in range(1, n_gy):
        piece = lax.dynamic_index_in_dim(send, (gj + shift) % n_gy, 0, keepdims=False)
        extras = []
        if shift == 1:
            extras.append(as_slab(side_last, 2, piece.shape[2]))
        if shift == n_gy - 1:
            extras.append(as_slab(side_leading, 2, piece.shape[2]))
        piece = jnp.concatenate([piece] + extras, axis=1)
        moved = lax.ppermute(piece, "gy", [(j, (j + shift) % n_gy) for j in range(n_gy)])
        at = depth
        if shift == 1:
            slab = as_slab(side_last, 2, piece.shape[2])
            side_before = from_slab(moved[:, at: at + slab.shape[1]], side_last.shape)
            at += slab.shape[1]
        if shift == n_gy - 1:
            slab = as_slab(side_leading, 2, piece.shape[2])
            side_after = from_slab(moved[:, at: at + slab.shape[1]], side_leading.shape)
        got.append(moved[:, :depth])
    if side_before is None:
        side_before = jnp.zeros_like(side_last)
        side_after = jnp.zeros_like(side_leading)
    side_before = jnp.where(gj > 0, side_before, 0.0)
    side_after = jnp.where(gj < n_gy - 1, side_after, 0.0)
    recv = jnp.take(jnp.stack(got), (gj - jnp.arange(n_gy)) % n_gy, axis=0)
    parts = []
    for k in range(n_gy):
        lo = 0 if k == 0 else width
        hi = rows + 2 * width if k == n_gy - 1 else rows + width
        parts.append(recv[k, 0, lo:hi])
    load_m = jnp.concatenate(parts, axis=0)
    top_m = jnp.concatenate(
        [recv[k, 1, width: rows + width, width: cm + width] for k in range(n_gy)], axis=0
    )
    return load_m, top_m, side_before, side_after


def joint_ranks(owners, devices):
    count = owners.shape[0]
    block = 128 if count % 128 == 0 else count
    nb = count // block
    onehot = (owners[:, None] == jnp.arange(devices, dtype=jnp.int32)[None, :]).astype(jnp.float32)
    oh = onehot.reshape(nb, block, devices)
    ar = jnp.arange(block)
    tri = (ar[:, None] >= ar[None, :]).astype(jnp.float32)
    within = jnp.einsum("ij,bjd->bid", tri, oh, precision=lax.Precision.HIGHEST)
    totals = within[:, -1, :]
    ab = jnp.arange(nb)
    stri = (ab[:, None] > ab[None, :]).astype(jnp.float32)
    offs = jnp.dot(stri, totals, precision=lax.Precision.HIGHEST)
    cum = (within + offs[:, None, :]).reshape(count, devices)
    return jnp.sum(cum * onehot, axis=1).astype(jnp.int32) - 1


def pick_kernel(rows_ref, cols_ref, parts_ref, out_ref):
    rows = rows_ref[...]
    cols = cols_ref[...]
    block = rows.shape[1]
    _, fields, rm, cm = parts_ref.shape
    hit = lax.broadcasted_iota(jnp.int32, (cm, block), 0) == cols
    onehot = jnp.where(hit, 1.0, 0.0).astype(jnp.bfloat16)
    sel = lax.broadcasted_iota(jnp.int32, (rm, block), 0) == rows
    for f in range(fields):
        acc = jnp.dot(parts_ref[0, f], onehot, preferred_element_type=jnp.float32)
        acc = acc + jnp.dot(parts_ref[1, f], onehot, preferred_element_type=jnp.float32)
        acc = acc + jnp.dot(parts_ref[2, f], onehot, preferred_element_type=jnp.float32)
        out_ref[f: f + 1, :] = jnp.sum(jnp.where(sel, acc, 0.0), axis=0, keepdims=True)


def pick_cells(fields, cells):
    count = cells.shape[0]
    nf, rm, cm = fields.shape
    hi = lax.reduce_precision(fields, exponent_bits=8, mantissa_bits=7)
    rest = fields - hi
    mid = lax.reduce_precision(rest, exponent_bits=8, mantissa_bits=7)
    lo = rest - mid
    parts = jnp.stack([hi, mid, lo]).astype(jnp.bfloat16)
    rows = (cells // cm).astype(jnp.int32)[None, :]
    cols = (cells % cm).astype(jnp.int32)[None, :]
    block = 512 if count % 512 == 0 else count
    return pl.pallas_call(
        pick_kernel,
        grid=(count // block,),
        in_specs=[
            pl.BlockSpec((1, block), lambda i: (0, i)),
            pl.BlockSpec((1, block), lambda i: (0, i)),
            pl.BlockSpec((3, nf, rm, cm), lambda i: (0, 0, 0, 0)),
        ],
        out_specs=pl.BlockSpec((nf, block), lambda i: (0, i)),
        out_shape=jax.ShapeDtypeStruct((nf, count), jnp.float32),
    )(rows, cols, parts)


def place_kernel(owners_ref, ranks_ref, parts_ref, out_ref):
    owners = owners_ref[...]
    ranks = ranks_ref[...]
    _, fields, count = parts_ref.shape
    devices, cap = out_ref.shape[1:]
    mine = lax.broadcasted_iota(jnp.int32, (devices, count), 0) == owners
    slot = lax.broadcasted_iota(jnp.int32, (count, cap), 1) == ranks
    at = jnp.where(slot, 1.0, 0.0).astype(jnp.bfloat16)
    for f in range(fields):
        acc = None
        for p in range(3):
            spread = jnp.where(mine, parts_ref[p, f: f + 1, :], 0.0).astype(jnp.bfloat16)
            term = jnp.dot(spread, at, preferred_element_type=jnp.float32)
            acc = term if acc is None else acc + term
        out_ref[f] = acc
    live = jnp.where(mine, 1.0, 0.0).astype(jnp.bfloat16)
    out_ref[fields] = jnp.dot(live, at, preferred_element_type=jnp.float32)


def place_joints(values, owners, ranks, devices, cap):
    nf, count = values.shape
    hi = lax.reduce_precision(values, exponent_bits=8, mantissa_bits=7)
    rest = values - hi
    mid = lax.reduce_precision(rest, exponent_bits=8, mantissa_bits=7)
    lo = rest - mid
    parts = jnp.stack([hi, mid, lo]).astype(jnp.float32)
    return pl.pallas_call(
        place_kernel,
        out_shape=jax.ShapeDtypeStruct((nf + 1, devices, cap), jnp.float32),
    )(owners[None, :].astype(jnp.int32), ranks[:, None].astype(jnp.int32), parts)


def body(
    temp_start,
    heat_input,
    lateral,
    vertical,
    weighting,
    modulus,
    warp_prev,
    joint_cell,
    joint_owner,
    joint_strain,
    joint_resist,
):
    devices = lax.axis_size(FLAT)
    n_gx, n_gy = lax.axis_size("gx"), lax.axis_size("gy")
    gi, gj = lax.axis_index("gx"), lax.axis_index("gy")
    rm, cm = warp_prev.shape

    wm = jnp.stack([warp_prev, modulus])
    owners = joint_owner[:, 0]
    capacity = joint_resist.shape[1] // devices
    ranks = joint_ranks(owners, devices)

    extra = SWEEPS - 1
    g = SWEEPS
    wm = with_halo(wm, (("gx", 1),), g)
    temp = thermal(temp_start, heat_input, lateral, vertical, extra)
    load_t = moment_of(temp, weighting)
    load, top, left, right = relay(
        load_t, temp[-1, extra: temp.shape[1] - extra], extra, wm[:, :, cm - g:], wm[:, :, :g])
    wm = jnp.concatenate([left, wm, right], axis=2)

    warp = wm[0]
    mod_ext = wm[1]
    for step in range(1, SWEEPS + 1):
        r = SWEEPS - step
        off = SWEEPS - (r + 1)
        e_pad = mod_ext[off: off + rm + 2 * r + 2, off: off + cm + 2 * r + 2]
        lo = SWEEPS - 1 - r
        ld = load[lo: lo + rm + 2 * r, lo: lo + cm + 2 * r]
        warp = sweep(warp, e_pad, ld)
        if r > 0:
            gr = gi * rm + jnp.arange(-r, rm + r)
            gc = gj * cm + jnp.arange(-r, cm + r)
            inside = ((gr >= 0) & (gr < n_gx * rm))[:, None] & ((gc >= 0) & (gc < n_gy * cm))[None, :]
            warp = jnp.where(inside, warp, 0.0)

    picked = pick_cells(jnp.stack([warp - warp_prev, top]), joint_cell)
    outgoing = place_joints(picked, owners, ranks, devices, capacity)
    incoming = lax.all_to_all(outgoing, FLAT, split_axis=1, concat_axis=1, tiled=True)
    incoming = incoming.reshape(incoming.shape[0], devices * capacity)
    strain_next, resist_next = anand(joint_strain, joint_resist, incoming[:, None, :])
    return (warp, strain_next, resist_next)


def solution(mesh):
    return jax.shard_map(
        body,
        mesh=mesh,
        in_specs=(
            P(None, FLAT, None),
            P(None, FLAT, None),
            P(),
            P(),
            P(),
            P("gx", "gy"),
            P("gx", "gy"),
            P(FLAT),
            P(FLAT, None),
            P(None, FLAT, None),
            P(FLAT, None),
        ),
        out_specs=(P("gx", "gy"), P(None, FLAT, None), P(FLAT, None)),
        check_vma=False,
    )
```

```python
import jax
import jax.numpy as jnp
from jax import lax
from jax.sharding import PartitionSpec as P
from jax.experimental import pallas as pl

STEPS = 2
SWEEPS = 3


stiffness = 0.2
shear_mod = 0.6
rate_scale = 0.5
sat_level = 2.5
sat_power = 0.3
harden = 2.0

FLAT = ("gx", "gy")


def exchange(last, leading, axis):
    count = lax.axis_size(axis)
    up = [(i, i + 1) for i in range(count - 1)]
    down = [(j, i) for i, j in up]
    return lax.ppermute(last, axis, up), lax.ppermute(leading, axis, down)


def with_halo(array, sides, width):
    for axis, dim in sides:
        length = array.shape[dim]
        last = lax.slice_in_dim(array, length - width, length, axis=dim)
        leading = lax.slice_in_dim(array, 0, width, axis=dim)
        before, after = exchange(last, leading, axis)
        array = jnp.concatenate([before, array, after], axis=dim)
    return array


def thermal_step(ext, heat_rows, lateral, vertical):
    cols = jnp.pad(ext, ((0, 0), (0, 0), (1, 1)))
    center = ext[:, 1:-1]
    lap = ext[:, 2:] + ext[:, :-2] + cols[:, 1:-1, 2:] + cols[:, 1:-1, :-2] - 4.0 * center
    flux = vertical[:, None, None] * (center[1:] - center[:-1])
    vert = jnp.pad(flux, ((0, 1), (0, 0), (0, 0))) - jnp.pad(flux, ((1, 0), (0, 0), (0, 0)))
    return center + lateral[:, None, None] * lap + vert + heat_rows


def moment_of(field, weighting):
    total = weighting[0] * field[0]
    for layer in range(1, field.shape[0]):
        total = total + weighting[layer] * field[layer]
    return total


def sweep(w_pad, e_pad, load):
    center = e_pad[1:-1, 1:-1]
    e_up = 0.5 * (center + e_pad[:-2, 1:-1])
    e_down = 0.5 * (center + e_pad[2:, 1:-1])
    e_left = 0.5 * (center + e_pad[1:-1, :-2])
    e_right = 0.5 * (center + e_pad[1:-1, 2:])
    numer = (
        load
        + e_up * w_pad[:-2, 1:-1]
        + e_down * w_pad[2:, 1:-1]
        + e_left * w_pad[1:-1, :-2]
        + e_right * w_pad[1:-1, 2:]
    )
    denom = stiffness + e_up + e_down + e_left + e_right
    return numer / denom


def anand(strain, resist, recv):
    total, inelastic = (strain[0], strain[1])
    increment, theta, live = (recv[0], recv[1], recv[2])
    total_new = total + increment
    arrhen = jnp.exp(2.0 - 2.0 / (1.0 + 0.1 * theta * theta))
    hyper = jnp.sinh(shear_mod * (total_new - inelastic) / resist)
    rate = rate_scale * arrhen * hyper * jnp.abs(hyper)
    inelastic_new = inelastic + rate
    target = sat_level * jnp.power(1.0 + jnp.abs(rate) / arrhen, sat_power)
    resist_new = resist + harden * (1.0 - resist / target) * jnp.abs(rate)
    keep = live > 0.5
    strain_out = jnp.stack(
        [jnp.where(keep, total_new, total), jnp.where(keep, inelastic_new, inelastic)]
    )
    return (strain_out, jnp.where(keep, resist_new, resist))


def as_slab(piece, layers, cols):
    flat = piece.reshape(-1)
    per = layers * cols
    n = -(-flat.shape[0] // per)
    return jnp.pad(flat, (0, n * per - flat.shape[0])).reshape(n, layers, cols).transpose(1, 0, 2)


def from_slab(slab, shape):
    size = 1
    for d in shape:
        size *= d
    return slab.transpose(1, 0, 2).reshape(-1)[:size].reshape(shape)


def thermal(temp, heat, lateral, vertical, extra):
    devices = lax.axis_size(FLAT)
    t = lax.axis_index(FLAT)
    rows = temp.shape[1]
    h = STEPS + extra
    hh = h - 1
    last = jnp.concatenate([temp[:, rows - h:], heat[:, rows - hh:]], axis=1)
    leading = jnp.concatenate([temp[:, :h], heat[:, :hh]], axis=1)
    before, after = exchange(last, leading, FLAT)
    ext = jnp.concatenate([before[:, :h], temp, after[:, :h]], axis=1)
    heat_ext = jnp.concatenate([before[:, h:], heat, after[:, h:]], axis=1)
    for step in range(1, STEPS + 1):
        r = STEPS - step + extra
        heat_rows = heat_ext[:, hh - r: hh - r + rows + 2 * r]
        ext = thermal_step(ext, heat_rows, lateral, vertical)
        if step < STEPS:
            g = t * rows + jnp.arange(-r, rows + r)
            inside = (g >= 0) & (g < devices * rows)
            ext = jnp.where(inside[None, :, None], ext, 0.0)
    return ext


def relay(load, top, width, side_last, side_leading):
    n_gy = lax.axis_size("gy")
    gj = lax.axis_index("gy")
    rows, cols = load.shape
    cm = cols // n_gy
    rows = rows - 2 * width
    lp = jnp.pad(load, ((0, 0), (width, width)))
    tp = jnp.pad(top, ((width, width), (width, width)))
    both = jnp.stack([lp, tp])
    send = jnp.stack([both[:, :, k * cm: k * cm + cm + 2 * width] for k in range(n_gy)])
    depth = send.shape[2]
    got = [lax.dynamic_index_in_dim(send, gj, 0, keepdims=False)]
    side_before = side_after = None
    for shift in range(1, n_gy):
        piece = lax.dynamic_index_in_dim(send, (gj + shift) % n_gy, 0, keepdims=False)
        extras = []
        if shift == 1:
            extras.append(as_slab(side_last, 2, piece.shape[2]))
        if shift == n_gy - 1:
            extras.append(as_slab(side_leading, 2, piece.shape[2]))
        piece = jnp.concatenate([piece] + extras, axis=1)
        moved = lax.ppermute(piece, "gy", [(j, (j + shift) % n_gy) for j in range(n_gy)])
        at = depth
        if shift == 1:
            slab = as_slab(side_last, 2, piece.shape[2])
            side_before = from_slab(moved[:, at: at + slab.shape[1]], side_last.shape)
            at += slab.shape[1]
        if shift == n_gy - 1:
            slab = as_slab(side_leading, 2, piece.shape[2])
            side_after = from_slab(moved[:, at: at + slab.shape[1]], side_leading.shape)
        got.append(moved[:, :depth])
    if side_before is None:
        side_before = jnp.zeros_like(side_last)
        side_after = jnp.zeros_like(side_leading)
    side_before = jnp.where(gj > 0, side_before, 0.0)
    side_after = jnp.where(gj < n_gy - 1, side_after, 0.0)
    recv = jnp.take(jnp.stack(got), (gj - jnp.arange(n_gy)) % n_gy, axis=0)
    parts = []
    for k in range(n_gy):
        lo = 0 if k == 0 else width
        hi = rows + 2 * width if k == n_gy - 1 else rows + width
        parts.append(recv[k, 0, lo:hi])
    load_m = jnp.concatenate(parts, axis=0)
    top_m = jnp.concatenate(
        [recv[k, 1, width: rows + width, width: cm + width] for k in range(n_gy)], axis=0
    )
    return load_m, top_m, side_before, side_after


def joint_ranks(owners, devices):
    count = owners.shape[0]
    block = 128 if count % 128 == 0 else count
    nb = count // block
    onehot = (owners[:, None] == jnp.arange(devices, dtype=jnp.int32)[None, :]).astype(jnp.float32)
    oh = onehot.reshape(nb, block, devices)
    ar = jnp.arange(block)
    tri = (ar[:, None] >= ar[None, :]).astype(jnp.float32)
    within = jnp.einsum("ij,bjd->bid", tri, oh, precision=lax.Precision.HIGHEST)
    totals = within[:, -1, :]
    ab = jnp.arange(nb)
    stri = (ab[:, None] > ab[None, :]).astype(jnp.float32)
    offs = jnp.dot(stri, totals, precision=lax.Precision.HIGHEST)
    cum = (within + offs[:, None, :]).reshape(count, devices)
    return jnp.sum(cum * onehot, axis=1).astype(jnp.int32) - 1


def split3(x):
    hi = x.astype(jnp.bfloat16).astype(jnp.float32)
    rest = x - hi
    mid = rest.astype(jnp.bfloat16).astype(jnp.float32)
    return hi, mid, rest - mid


def joints_kernel(rows_ref, cols_ref, parts_ref, owners_ref, ranks_ref, out_ref):
    _, fields, rm, cm = parts_ref.shape
    count = rows_ref.shape[1]
    devices, cap = out_ref.shape[1:]
    block = 512 if count % 512 == 0 else count
    picked = []
    for b in range(count // block):
        rows = rows_ref[:, b * block: (b + 1) * block]
        cols = cols_ref[:, b * block: (b + 1) * block]
        hit = lax.broadcasted_iota(jnp.int32, (cm, block), 0) == cols
        onehot = jnp.where(hit, 1.0, 0.0).astype(jnp.bfloat16)
        sel = lax.broadcasted_iota(jnp.int32, (rm, block), 0) == rows
        got = []
        for f in range(fields):
            acc = jnp.dot(parts_ref[0, f], onehot, preferred_element_type=jnp.float32)
            acc = acc + jnp.dot(parts_ref[1, f], onehot, preferred_element_type=jnp.float32)
            acc = acc + jnp.dot(parts_ref[2, f], onehot, preferred_element_type=jnp.float32)
            got.append(jnp.sum(jnp.where(sel, acc, 0.0), axis=0, keepdims=True))
        picked.append(jnp.concatenate(got, axis=0))
    values = jnp.concatenate(picked, axis=1)
    mine = lax.broadcasted_iota(jnp.int32, (devices, count), 0) == owners_ref[...]
    slot = lax.broadcasted_iota(jnp.int32, (count, cap), 1) == ranks_ref[...]
    at = jnp.where(slot, 1.0, 0.0).astype(jnp.bfloat16)
    split = split3(values)
    for f in range(fields):
        acc = None
        for part in split:
            spread = jnp.where(mine, part[f: f + 1, :], 0.0).astype(jnp.bfloat16)
            term = jnp.dot(spread, at, preferred_element_type=jnp.float32)
            acc = term if acc is None else acc + term
        out_ref[f] = acc
    live = jnp.where(mine, 1.0, 0.0).astype(jnp.bfloat16)
    out_ref[fields] = jnp.dot(live, at, preferred_element_type=jnp.float32)


def route_joints(fields, cells, owners, ranks, devices, cap):
    nf, rm, cm = fields.shape
    hi = lax.reduce_precision(fields, exponent_bits=8, mantissa_bits=7)
    rest = fields - hi
    mid = lax.reduce_precision(rest, exponent_bits=8, mantissa_bits=7)
    lo = rest - mid
    parts = jnp.stack([hi, mid, lo]).astype(jnp.bfloat16)
    return pl.pallas_call(
        joints_kernel,
        out_shape=jax.ShapeDtypeStruct((nf + 1, devices, cap), jnp.float32),
    )(
        (cells // cm).astype(jnp.int32)[None, :],
        (cells % cm).astype(jnp.int32)[None, :],
        parts,
        owners[None, :].astype(jnp.int32),
        ranks[:, None].astype(jnp.int32),
    )


def body(
    temp_start,
    heat_input,
    lateral,
    vertical,
    weighting,
    modulus,
    warp_prev,
    joint_cell,
    joint_owner,
    joint_strain,
    joint_resist,
):
    devices = lax.axis_size(FLAT)
    n_gx, n_gy = lax.axis_size("gx"), lax.axis_size("gy")
    gi, gj = lax.axis_index("gx"), lax.axis_index("gy")
    rm, cm = warp_prev.shape

    wm = jnp.stack([warp_prev, modulus])
    owners = joint_owner[:, 0]
    capacity = joint_resist.shape[1] // devices
    ranks = joint_ranks(owners, devices)

    extra = SWEEPS - 1
    g = SWEEPS
    wm = with_halo(wm, (("gx", 1),), g)
    temp = thermal(temp_start, heat_input, lateral, vertical, extra)
    load_t = moment_of(temp, weighting)
    load, top, left, right = relay(
        load_t, temp[-1, extra: temp.shape[1] - extra], extra, wm[:, :, cm - g:], wm[:, :, :g])
    wm = jnp.concatenate([left, wm, right], axis=2)

    warp = wm[0]
    mod_ext = wm[1]
    for step in range(1, SWEEPS + 1):
        r = SWEEPS - step
        off = SWEEPS - (r + 1)
        e_pad = mod_ext[off: off + rm + 2 * r + 2, off: off + cm + 2 * r + 2]
        lo = SWEEPS - 1 - r
        ld = load[lo: lo + rm + 2 * r, lo: lo + cm + 2 * r]
        warp = sweep(warp, e_pad, ld)
        if r > 0:
            gr = gi * rm + jnp.arange(-r, rm + r)
            gc = gj * cm + jnp.arange(-r, cm + r)
            inside = ((gr >= 0) & (gr < n_gx * rm))[:, None] & ((gc >= 0) & (gc < n_gy * cm))[None, :]
            warp = jnp.where(inside, warp, 0.0)

    outgoing = route_joints(
        jnp.stack([warp - warp_prev, top]), joint_cell, owners, ranks, devices, capacity)
    incoming = lax.all_to_all(outgoing, FLAT, split_axis=1, concat_axis=1, tiled=True)
    incoming = incoming.reshape(incoming.shape[0], devices * capacity)
    strain_next, resist_next = anand(joint_strain, joint_resist, incoming[:, None, :])
    return (warp, strain_next, resist_next)


def solution(mesh):
    return jax.shard_map(
        body,
        mesh=mesh,
        in_specs=(
            P(None, FLAT, None),
            P(None, FLAT, None),
            P(),
            P(),
            P(),
            P("gx", "gy"),
            P("gx", "gy"),
            P(FLAT),
            P(FLAT, None),
            P(None, FLAT, None),
            P(FLAT, None),
        ),
        out_specs=(P("gx", "gy"), P(None, FLAT, None), P(FLAT, None)),
        check_vma=False,
    )
```

```python
import jax
import jax.numpy as jnp
from jax import lax
from jax.sharding import PartitionSpec as P
from jax.experimental import pallas as pl

STEPS = 2
SWEEPS = 3


stiffness = 0.2
shear_mod = 0.6
rate_scale = 0.5
sat_level = 2.5
sat_power = 0.3
harden = 2.0

FLAT = ("gx", "gy")


def exchange(last, leading, axis):
    count = lax.axis_size(axis)
    up = [(i, i + 1) for i in range(count - 1)]
    down = [(j, i) for i, j in up]
    return lax.ppermute(last, axis, up), lax.ppermute(leading, axis, down)


def with_halo(array, sides, width):
    for axis, dim in sides:
        length = array.shape[dim]
        last = lax.slice_in_dim(array, length - width, length, axis=dim)
        leading = lax.slice_in_dim(array, 0, width, axis=dim)
        before, after = exchange(last, leading, axis)
        array = jnp.concatenate([before, array, after], axis=dim)
    return array


def thermal_step(ext, heat_rows, lateral, vertical):
    cols = jnp.pad(ext, ((0, 0), (0, 0), (1, 1)))
    center = ext[:, 1:-1]
    lap = ext[:, 2:] + ext[:, :-2] + cols[:, 1:-1, 2:] + cols[:, 1:-1, :-2] - 4.0 * center
    flux = vertical[:, None, None] * (center[1:] - center[:-1])
    vert = jnp.pad(flux, ((0, 1), (0, 0), (0, 0))) - jnp.pad(flux, ((1, 0), (0, 0), (0, 0)))
    return center + lateral[:, None, None] * lap + vert + heat_rows


def moment_of(field, weighting):
    total = weighting[0] * field[0]
    for layer in range(1, field.shape[0]):
        total = total + weighting[layer] * field[layer]
    return total


def sweep(w_pad, e_pad, load):
    center = e_pad[1:-1, 1:-1]
    e_up = 0.5 * (center + e_pad[:-2, 1:-1])
    e_down = 0.5 * (center + e_pad[2:, 1:-1])
    e_left = 0.5 * (center + e_pad[1:-1, :-2])
    e_right = 0.5 * (center + e_pad[1:-1, 2:])
    numer = (
        load
        + e_up * w_pad[:-2, 1:-1]
        + e_down * w_pad[2:, 1:-1]
        + e_left * w_pad[1:-1, :-2]
        + e_right * w_pad[1:-1, 2:]
    )
    denom = stiffness + e_up + e_down + e_left + e_right
    return numer / denom


def anand(strain, resist, recv):
    total, inelastic = (strain[0], strain[1])
    increment, theta, live = (recv[0], recv[1], recv[2])
    total_new = total + increment
    arrhen = jnp.exp(2.0 - 2.0 / (1.0 + 0.1 * theta * theta))
    hyper = jnp.sinh(shear_mod * (total_new - inelastic) / resist)
    rate = rate_scale * arrhen * hyper * jnp.abs(hyper)
    inelastic_new = inelastic + rate
    target = sat_level * jnp.power(1.0 + jnp.abs(rate) / arrhen, sat_power)
    resist_new = resist + harden * (1.0 - resist / target) * jnp.abs(rate)
    keep = live > 0.5
    strain_out = jnp.stack(
        [jnp.where(keep, total_new, total), jnp.where(keep, inelastic_new, inelastic)]
    )
    return (strain_out, jnp.where(keep, resist_new, resist))


def as_slab(piece, layers, cols):
    flat = piece.reshape(-1)
    per = layers * cols
    n = -(-flat.shape[0] // per)
    return jnp.pad(flat, (0, n * per - flat.shape[0])).reshape(n, layers, cols).transpose(1, 0, 2)


def from_slab(slab, shape):
    size = 1
    for d in shape:
        size *= d
    return slab.transpose(1, 0, 2).reshape(-1)[:size].reshape(shape)


def thermal(temp, heat, lateral, vertical, extra):
    devices = lax.axis_size(FLAT)
    t = lax.axis_index(FLAT)
    rows = temp.shape[1]
    h = STEPS + extra
    hh = h - 1
    last = jnp.concatenate([temp[:, rows - h:], heat[:, rows - hh:]], axis=1)
    leading = jnp.concatenate([temp[:, :h], heat[:, :hh]], axis=1)
    before, after = exchange(last, leading, FLAT)
    ext = jnp.concatenate([before[:, :h], temp, after[:, :h]], axis=1)
    heat_ext = jnp.concatenate([before[:, h:], heat, after[:, h:]], axis=1)
    for step in range(1, STEPS + 1):
        r = STEPS - step + extra
        heat_rows = heat_ext[:, hh - r: hh - r + rows + 2 * r]
        ext = thermal_step(ext, heat_rows, lateral, vertical)
        if step < STEPS:
            g = t * rows + jnp.arange(-r, rows + r)
            inside = (g >= 0) & (g < devices * rows)
            ext = jnp.where(inside[None, :, None], ext, 0.0)
    return ext


def relay(load, top, width, side_last, side_leading):
    n_gy = lax.axis_size("gy")
    gj = lax.axis_index("gy")
    rows, cols = load.shape
    cm = cols // n_gy
    rows = rows - 2 * width
    lp = jnp.pad(load, ((0, 0), (width, width)))
    tp = jnp.pad(top, ((width, width), (width, width)))
    both = jnp.stack([lp, tp])
    send = jnp.stack([both[:, :, k * cm: k * cm + cm + 2 * width] for k in range(n_gy)])
    depth = send.shape[2]
    got = [lax.dynamic_index_in_dim(send, gj, 0, keepdims=False)]
    side_before = side_after = None
    for shift in range(1, n_gy):
        piece = lax.dynamic_index_in_dim(send, (gj + shift) % n_gy, 0, keepdims=False)
        extras = []
        if shift == 1:
            extras.append(as_slab(side_last, 2, piece.shape[2]))
        if shift == n_gy - 1:
            extras.append(as_slab(side_leading, 2, piece.shape[2]))
        piece = jnp.concatenate([piece] + extras, axis=1)
        moved = lax.ppermute(piece, "gy", [(j, (j + shift) % n_gy) for j in range(n_gy)])
        at = depth
        if shift == 1:
            slab = as_slab(side_last, 2, piece.shape[2])
            side_before = from_slab(moved[:, at: at + slab.shape[1]], side_last.shape)
            at += slab.shape[1]
        if shift == n_gy - 1:
            slab = as_slab(side_leading, 2, piece.shape[2])
            side_after = from_slab(moved[:, at: at + slab.shape[1]], side_leading.shape)
        got.append(moved[:, :depth])
    if side_before is None:
        side_before = jnp.zeros_like(side_last)
        side_after = jnp.zeros_like(side_leading)
    side_before = jnp.where(gj > 0, side_before, 0.0)
    side_after = jnp.where(gj < n_gy - 1, side_after, 0.0)
    recv = jnp.take(jnp.stack(got), (gj - jnp.arange(n_gy)) % n_gy, axis=0)
    parts = []
    for k in range(n_gy):
        lo = 0 if k == 0 else width
        hi = rows + 2 * width if k == n_gy - 1 else rows + width
        parts.append(recv[k, 0, lo:hi])
    load_m = jnp.concatenate(parts, axis=0)
    top_m = jnp.concatenate(
        [recv[k, 1, width: rows + width, width: cm + width] for k in range(n_gy)], axis=0
    )
    return load_m, top_m, side_before, side_after


def joint_ranks(owners, devices):
    count = owners.shape[0]
    block = 128 if count % 128 == 0 else count
    nb = count // block
    onehot = (owners[:, None] == jnp.arange(devices, dtype=jnp.int32)[None, :]).astype(jnp.float32)
    oh = onehot.reshape(nb, block, devices)
    ar = jnp.arange(block)
    tri = (ar[:, None] >= ar[None, :]).astype(jnp.float32)
    within = jnp.einsum("ij,bjd->bid", tri, oh, precision=lax.Precision.HIGHEST)
    totals = within[:, -1, :]
    ab = jnp.arange(nb)
    stri = (ab[:, None] > ab[None, :]).astype(jnp.float32)
    offs = jnp.dot(stri, totals, precision=lax.Precision.HIGHEST)
    cum = (within + offs[:, None, :]).reshape(count, devices)
    return jnp.sum(cum * onehot, axis=1).astype(jnp.int32) - 1


def split3(x):
    hi = x.astype(jnp.bfloat16).astype(jnp.float32)
    rest = x - hi
    mid = rest.astype(jnp.bfloat16).astype(jnp.float32)
    return hi, mid, rest - mid


def joints_kernel(rows_ref, cols_ref, parts_ref, owners_ref, ranks_ref, out_ref):
    _, fields, rm, cm = parts_ref.shape
    count = rows_ref.shape[1]
    devices, cap = out_ref.shape[1:]
    block = 512 if count % 512 == 0 else count
    picked = []
    for b in range(count // block):
        rows = rows_ref[:, b * block: (b + 1) * block]
        cols = cols_ref[:, b * block: (b + 1) * block]
        hit = lax.broadcasted_iota(jnp.int32, (cm, block), 0) == cols
        onehot = jnp.where(hit, 1.0, 0.0).astype(jnp.bfloat16)
        sel = lax.broadcasted_iota(jnp.int32, (rm, block), 0) == rows
        got = []
        for f in range(fields):
            acc = jnp.dot(parts_ref[0, f], onehot, preferred_element_type=jnp.float32)
            acc = acc + jnp.dot(parts_ref[1, f], onehot, preferred_element_type=jnp.float32)
            acc = acc + jnp.dot(parts_ref[2, f], onehot, preferred_element_type=jnp.float32)
            got.append(jnp.sum(jnp.where(sel, acc, 0.0), axis=0, keepdims=True))
        picked.append(jnp.concatenate(got, axis=0))
    values = jnp.concatenate(picked, axis=1)
    mine = lax.broadcasted_iota(jnp.int32, (devices, count), 0) == owners_ref[...]
    slot = lax.broadcasted_iota(jnp.int32, (cap, count), 0) == ranks_ref[...]
    at = jnp.where(slot, 1.0, 0.0).astype(jnp.bfloat16)
    over_joints = (((1,), (1,)), ((), ()))
    split = split3(values)
    for f in range(fields):
        acc = None
        for part in split:
            spread = jnp.where(mine, part[f: f + 1, :], 0.0).astype(jnp.bfloat16)
            term = lax.dot_general(spread, at, over_joints, preferred_element_type=jnp.float32)
            acc = term if acc is None else acc + term
        out_ref[f] = acc
    live = jnp.where(mine, 1.0, 0.0).astype(jnp.bfloat16)
    out_ref[fields] = lax.dot_general(live, at, over_joints, preferred_element_type=jnp.float32)


def route_joints(fields, cells, owners, ranks, devices, cap):
    nf, rm, cm = fields.shape
    hi = lax.reduce_precision(fields, exponent_bits=8, mantissa_bits=7)
    rest = fields - hi
    mid = lax.reduce_precision(rest, exponent_bits=8, mantissa_bits=7)
    lo = rest - mid
    parts = jnp.stack([hi, mid, lo]).astype(jnp.bfloat16)
    return pl.pallas_call(
        joints_kernel,
        out_shape=jax.ShapeDtypeStruct((nf + 1, devices, cap), jnp.float32),
    )(
        (cells // cm).astype(jnp.int32)[None, :],
        (cells % cm).astype(jnp.int32)[None, :],
        parts,
        owners[None, :].astype(jnp.int32),
        ranks[None, :].astype(jnp.int32),
    )


def body(
    temp_start,
    heat_input,
    lateral,
    vertical,
    weighting,
    modulus,
    warp_prev,
    joint_cell,
    joint_owner,
    joint_strain,
    joint_resist,
):
    devices = lax.axis_size(FLAT)
    n_gx, n_gy = lax.axis_size("gx"), lax.axis_size("gy")
    gi, gj = lax.axis_index("gx"), lax.axis_index("gy")
    rm, cm = warp_prev.shape

    wm = jnp.stack([warp_prev, modulus])
    owners = joint_owner[:, 0]
    capacity = joint_resist.shape[1] // devices
    ranks = joint_ranks(owners, devices)

    extra = SWEEPS - 1
    g = SWEEPS
    wm = with_halo(wm, (("gx", 1),), g)
    temp = thermal(temp_start, heat_input, lateral, vertical, extra)
    load_t = moment_of(temp, weighting)
    load, top, left, right = relay(
        load_t, temp[-1, extra: temp.shape[1] - extra], extra, wm[:, :, cm - g:], wm[:, :, :g])
    wm = jnp.concatenate([left, wm, right], axis=2)

    warp = wm[0]
    mod_ext = wm[1]
    for step in range(1, SWEEPS + 1):
        r = SWEEPS - step
        off = SWEEPS - (r + 1)
        e_pad = mod_ext[off: off + rm + 2 * r + 2, off: off + cm + 2 * r + 2]
        lo = SWEEPS - 1 - r
        ld = load[lo: lo + rm + 2 * r, lo: lo + cm + 2 * r]
        warp = sweep(warp, e_pad, ld)
        if r > 0:
            gr = gi * rm + jnp.arange(-r, rm + r)
            gc = gj * cm + jnp.arange(-r, cm + r)
            inside = ((gr >= 0) & (gr < n_gx * rm))[:, None] & ((gc >= 0) & (gc < n_gy * cm))[None, :]
            warp = jnp.where(inside, warp, 0.0)

    outgoing = route_joints(
        jnp.stack([warp - warp_prev, top]), joint_cell, owners, ranks, devices, capacity)
    incoming = lax.all_to_all(outgoing, FLAT, split_axis=1, concat_axis=1, tiled=True)
    incoming = incoming.reshape(incoming.shape[0], devices * capacity)
    strain_next, resist_next = anand(joint_strain, joint_resist, incoming[:, None, :])
    return (warp, strain_next, resist_next)


def solution(mesh):
    return jax.shard_map(
        body,
        mesh=mesh,
        in_specs=(
            P(None, FLAT, None),
            P(None, FLAT, None),
            P(),
            P(),
            P(),
            P("gx", "gy"),
            P("gx", "gy"),
            P(FLAT),
            P(FLAT, None),
            P(None, FLAT, None),
            P(FLAT, None),
        ),
        out_specs=(P("gx", "gy"), P(None, FLAT, None), P(FLAT, None)),
        check_vma=False,
    )
```

```python
import jax
import jax.numpy as jnp
from jax import lax
from jax.sharding import PartitionSpec as P
from jax.experimental import pallas as pl

STEPS = 2
SWEEPS = 3


stiffness = 0.2
shear_mod = 0.6
rate_scale = 0.5
sat_level = 2.5
sat_power = 0.3
harden = 2.0

FLAT = ("gx", "gy")


def exchange(last, leading, axis):
    count = lax.axis_size(axis)
    up = [(i, i + 1) for i in range(count - 1)]
    down = [(j, i) for i, j in up]
    return lax.ppermute(last, axis, up), lax.ppermute(leading, axis, down)


def with_halo(array, sides, width):
    for axis, dim in sides:
        length = array.shape[dim]
        last = lax.slice_in_dim(array, length - width, length, axis=dim)
        leading = lax.slice_in_dim(array, 0, width, axis=dim)
        before, after = exchange(last, leading, axis)
        array = jnp.concatenate([before, array, after], axis=dim)
    return array


def thermal_step(ext, heat_rows, lateral, vertical):
    cols = jnp.pad(ext, ((0, 0), (0, 0), (1, 1)))
    center = ext[:, 1:-1]
    lap = ext[:, 2:] + ext[:, :-2] + cols[:, 1:-1, 2:] + cols[:, 1:-1, :-2] - 4.0 * center
    flux = vertical[:, None, None] * (center[1:] - center[:-1])
    vert = jnp.pad(flux, ((0, 1), (0, 0), (0, 0))) - jnp.pad(flux, ((1, 0), (0, 0), (0, 0)))
    return center + lateral[:, None, None] * lap + vert + heat_rows


def moment_of(field, weighting):
    total = weighting[0] * field[0]
    for layer in range(1, field.shape[0]):
        total = total + weighting[layer] * field[layer]
    return total


def sweep(w_pad, e_pad, load):
    center = e_pad[1:-1, 1:-1]
    e_up = 0.5 * (center + e_pad[:-2, 1:-1])
    e_down = 0.5 * (center + e_pad[2:, 1:-1])
    e_left = 0.5 * (center + e_pad[1:-1, :-2])
    e_right = 0.5 * (center + e_pad[1:-1, 2:])
    numer = (
        load
        + e_up * w_pad[:-2, 1:-1]
        + e_down * w_pad[2:, 1:-1]
        + e_left * w_pad[1:-1, :-2]
        + e_right * w_pad[1:-1, 2:]
    )
    denom = stiffness + e_up + e_down + e_left + e_right
    return numer / denom


def anand(strain, resist, recv):
    total, inelastic = (strain[0], strain[1])
    increment, theta, live = (recv[0], recv[1], recv[2])
    total_new = total + increment
    arrhen = jnp.exp(2.0 - 2.0 / (1.0 + 0.1 * theta * theta))
    hyper = jnp.sinh(shear_mod * (total_new - inelastic) / resist)
    rate = rate_scale * arrhen * hyper * jnp.abs(hyper)
    inelastic_new = inelastic + rate
    target = sat_level * jnp.power(1.0 + jnp.abs(rate) / arrhen, sat_power)
    resist_new = resist + harden * (1.0 - resist / target) * jnp.abs(rate)
    keep = live > 0.5
    strain_out = jnp.stack(
        [jnp.where(keep, total_new, total), jnp.where(keep, inelastic_new, inelastic)]
    )
    return (strain_out, jnp.where(keep, resist_new, resist))


def as_slab(piece, layers, cols):
    flat = piece.reshape(-1)
    per = layers * cols
    n = -(-flat.shape[0] // per)
    return jnp.pad(flat, (0, n * per - flat.shape[0])).reshape(n, layers, cols).transpose(1, 0, 2)


def from_slab(slab, shape):
    size = 1
    for d in shape:
        size *= d
    return slab.transpose(1, 0, 2).reshape(-1)[:size].reshape(shape)


def thermal(temp, heat, lateral, vertical, extra):
    devices = lax.axis_size(FLAT)
    t = lax.axis_index(FLAT)
    rows = temp.shape[1]
    h = STEPS + extra
    hh = h - 1
    last = jnp.concatenate([temp[:, rows - h:], heat[:, rows - hh:]], axis=1)
    leading = jnp.concatenate([temp[:, :h], heat[:, :hh]], axis=1)
    before, after = exchange(last, leading, FLAT)
    ext = jnp.concatenate([before[:, :h], temp, after[:, :h]], axis=1)
    heat_ext = jnp.concatenate([before[:, h:], heat, after[:, h:]], axis=1)
    for step in range(1, STEPS + 1):
        r = STEPS - step + extra
        heat_rows = heat_ext[:, hh - r: hh - r + rows + 2 * r]
        ext = thermal_step(ext, heat_rows, lateral, vertical)
        if step < STEPS:
            g = t * rows + jnp.arange(-r, rows + r)
            inside = (g >= 0) & (g < devices * rows)
            ext = jnp.where(inside[None, :, None], ext, 0.0)
    return ext


def relay(load, top, width, side_last, side_leading):
    n_gy = lax.axis_size("gy")
    gj = lax.axis_index("gy")
    rows, cols = load.shape
    cm = cols // n_gy
    rows = rows - 2 * width
    lp = jnp.pad(load, ((0, 0), (width, width)))
    tp = jnp.pad(top, ((width, width), (0, 0)))
    send = []
    for k in range(n_gy):
        main = jnp.stack([load[:, k * cm: (k + 1) * cm], tp[:, k * cm: (k + 1) * cm]])
        halo = jnp.concatenate(
            [lp[:, k * cm: k * cm + width], lp[:, (k + 1) * cm + width: (k + 1) * cm + 2 * width]],
            axis=1)
        send.append(jnp.concatenate([main, as_slab(halo, 2, cm)], axis=1))
    send = jnp.stack(send)
    depth = send.shape[2]
    full = load.shape[0]
    got = [lax.dynamic_index_in_dim(send, gj, 0, keepdims=False)]
    side_before = side_after = None
    for shift in range(1, n_gy):
        piece = lax.dynamic_index_in_dim(send, (gj + shift) % n_gy, 0, keepdims=False)
        extras = []
        if shift == 1:
            extras.append(as_slab(side_last, 2, piece.shape[2]))
        if shift == n_gy - 1:
            extras.append(as_slab(side_leading, 2, piece.shape[2]))
        piece = jnp.concatenate([piece] + extras, axis=1)
        moved = lax.ppermute(piece, "gy", [(j, (j + shift) % n_gy) for j in range(n_gy)])
        at = depth
        if shift == 1:
            slab = as_slab(side_last, 2, piece.shape[2])
            side_before = from_slab(moved[:, at: at + slab.shape[1]], side_last.shape)
            at += slab.shape[1]
        if shift == n_gy - 1:
            slab = as_slab(side_leading, 2, piece.shape[2])
            side_after = from_slab(moved[:, at: at + slab.shape[1]], side_leading.shape)
        got.append(moved[:, :depth])
    if side_before is None:
        side_before = jnp.zeros_like(side_last)
        side_after = jnp.zeros_like(side_leading)
    side_before = jnp.where(gj > 0, side_before, 0.0)
    side_after = jnp.where(gj < n_gy - 1, side_after, 0.0)
    recv = jnp.take(jnp.stack(got), (gj - jnp.arange(n_gy)) % n_gy, axis=0)
    parts = []
    for k in range(n_gy):
        halo = from_slab(recv[k, :, full:], (full, 2 * width))
        window = jnp.concatenate([halo[:, :width], recv[k, 0, :full], halo[:, width:]], axis=1)
        lo = 0 if k == 0 else width
        hi = rows + 2 * width if k == n_gy - 1 else rows + width
        parts.append(window[lo:hi])
    load_m = jnp.concatenate(parts, axis=0)
    top_m = jnp.concatenate([recv[k, 1, width: rows + width] for k in range(n_gy)], axis=0)
    return load_m, top_m, side_before, side_after


def joint_ranks(owners, devices):
    count = owners.shape[0]
    block = 128 if count % 128 == 0 else count
    nb = count // block
    onehot = (owners[:, None] == jnp.arange(devices, dtype=jnp.int32)[None, :]).astype(jnp.float32)
    oh = onehot.reshape(nb, block, devices)
    ar = jnp.arange(block)
    tri = (ar[:, None] >= ar[None, :]).astype(jnp.float32)
    within = jnp.einsum("ij,bjd->bid", tri, oh, precision=lax.Precision.HIGHEST)
    totals = within[:, -1, :]
    ab = jnp.arange(nb)
    stri = (ab[:, None] > ab[None, :]).astype(jnp.float32)
    offs = jnp.dot(stri, totals, precision=lax.Precision.HIGHEST)
    cum = (within + offs[:, None, :]).reshape(count, devices)
    return jnp.sum(cum * onehot, axis=1).astype(jnp.int32) - 1


def split3(x):
    hi = x.astype(jnp.bfloat16).astype(jnp.float32)
    rest = x - hi
    mid = rest.astype(jnp.bfloat16).astype(jnp.float32)
    return hi, mid, rest - mid


def joints_kernel(rows_ref, cols_ref, parts_ref, owners_ref, ranks_ref, out_ref):
    _, fields, rm, cm = parts_ref.shape
    count = rows_ref.shape[1]
    devices, cap = out_ref.shape[1:]
    block = 512 if count % 512 == 0 else count
    picked = []
    for b in range(count // block):
        rows = rows_ref[:, b * block: (b + 1) * block]
        cols = cols_ref[:, b * block: (b + 1) * block]
        hit = lax.broadcasted_iota(jnp.int32, (cm, block), 0) == cols
        onehot = jnp.where(hit, 1.0, 0.0).astype(jnp.bfloat16)
        sel = lax.broadcasted_iota(jnp.int32, (rm, block), 0) == rows
        got = []
        for f in range(fields):
            acc = jnp.dot(parts_ref[0, f], onehot, preferred_element_type=jnp.float32)
            acc = acc + jnp.dot(parts_ref[1, f], onehot, preferred_element_type=jnp.float32)
            acc = acc + jnp.dot(parts_ref[2, f], onehot, preferred_element_type=jnp.float32)
            got.append(jnp.sum(jnp.where(sel, acc, 0.0), axis=0, keepdims=True))
        picked.append(jnp.concatenate(got, axis=0))
    values = jnp.concatenate(picked, axis=1)
    mine = lax.broadcasted_iota(jnp.int32, (devices, count), 0) == owners_ref[...]
    slot = lax.broadcasted_iota(jnp.int32, (cap, count), 0) == ranks_ref[...]
    at = jnp.where(slot, 1.0, 0.0).astype(jnp.bfloat16)
    over_joints = (((1,), (1,)), ((), ()))
    split = split3(values)
    for f in range(fields):
        acc = None
        for part in split:
            spread = jnp.where(mine, part[f: f + 1, :], 0.0).astype(jnp.bfloat16)
            term = lax.dot_general(spread, at, over_joints, preferred_element_type=jnp.float32)
            acc = term if acc is None else acc + term
        out_ref[f] = acc
    live = jnp.where(mine, 1.0, 0.0).astype(jnp.bfloat16)
    out_ref[fields] = lax.dot_general(live, at, over_joints, preferred_element_type=jnp.float32)


def route_joints(fields, cells, owners, ranks, devices, cap):
    nf, rm, cm = fields.shape
    hi = lax.reduce_precision(fields, exponent_bits=8, mantissa_bits=7)
    rest = fields - hi
    mid = lax.reduce_precision(rest, exponent_bits=8, mantissa_bits=7)
    lo = rest - mid
    parts = jnp.stack([hi, mid, lo]).astype(jnp.bfloat16)
    return pl.pallas_call(
        joints_kernel,
        out_shape=jax.ShapeDtypeStruct((nf + 1, devices, cap), jnp.float32),
    )(
        (cells // cm).astype(jnp.int32)[None, :],
        (cells % cm).astype(jnp.int32)[None, :],
        parts,
        owners[None, :].astype(jnp.int32),
        ranks[None, :].astype(jnp.int32),
    )


def body(
    temp_start,
    heat_input,
    lateral,
    vertical,
    weighting,
    modulus,
    warp_prev,
    joint_cell,
    joint_owner,
    joint_strain,
    joint_resist,
):
    devices = lax.axis_size(FLAT)
    n_gx, n_gy = lax.axis_size("gx"), lax.axis_size("gy")
    gi, gj = lax.axis_index("gx"), lax.axis_index("gy")
    rm, cm = warp_prev.shape

    wm = jnp.stack([warp_prev, modulus])
    owners = joint_owner[:, 0]
    capacity = joint_resist.shape[1] // devices
    ranks = joint_ranks(owners, devices)

    extra = SWEEPS - 1
    g = SWEEPS
    wm = with_halo(wm, (("gx", 1),), g)
    temp = thermal(temp_start, heat_input, lateral, vertical, extra)
    load_t = moment_of(temp, weighting)
    load, top, left, right = relay(
        load_t, temp[-1, extra: temp.shape[1] - extra], extra, wm[:, :, cm - g:], wm[:, :, :g])
    wm = jnp.concatenate([left, wm, right], axis=2)

    warp = wm[0]
    mod_ext = wm[1]
    for step in range(1, SWEEPS + 1):
        r = SWEEPS - step
        off = SWEEPS - (r + 1)
        e_pad = mod_ext[off: off + rm + 2 * r + 2, off: off + cm + 2 * r + 2]
        lo = SWEEPS - 1 - r
        ld = load[lo: lo + rm + 2 * r, lo: lo + cm + 2 * r]
        warp = sweep(warp, e_pad, ld)
        if r > 0:
            gr = gi * rm + jnp.arange(-r, rm + r)
            gc = gj * cm + jnp.arange(-r, cm + r)
            inside = ((gr >= 0) & (gr < n_gx * rm))[:, None] & ((gc >= 0) & (gc < n_gy * cm))[None, :]
            warp = jnp.where(inside, warp, 0.0)

    outgoing = route_joints(
        jnp.stack([warp - warp_prev, top]), joint_cell, owners, ranks, devices, capacity)
    incoming = lax.all_to_all(outgoing, FLAT, split_axis=1, concat_axis=1, tiled=True)
    incoming = incoming.reshape(incoming.shape[0], devices * capacity)
    strain_next, resist_next = anand(joint_strain, joint_resist, incoming[:, None, :])
    return (warp, strain_next, resist_next)


def solution(mesh):
    return jax.shard_map(
        body,
        mesh=mesh,
        in_specs=(
            P(None, FLAT, None),
            P(None, FLAT, None),
            P(),
            P(),
            P(),
            P("gx", "gy"),
            P("gx", "gy"),
            P(FLAT),
            P(FLAT, None),
            P(None, FLAT, None),
            P(FLAT, None),
        ),
        out_specs=(P("gx", "gy"), P(None, FLAT, None), P(FLAT, None)),
        check_vma=False,
    )
```

```python
import jax
import jax.numpy as jnp
from jax import lax
from jax.sharding import PartitionSpec as P
from jax.experimental import pallas as pl

STEPS = 2
SWEEPS = 3


stiffness = 0.2
shear_mod = 0.6
rate_scale = 0.5
sat_level = 2.5
sat_power = 0.3
harden = 2.0

FLAT = ("gx", "gy")


def exchange(last, leading, axis):
    count = lax.axis_size(axis)
    up = [(i, i + 1) for i in range(count - 1)]
    down = [(j, i) for i, j in up]
    return lax.ppermute(last, axis, up), lax.ppermute(leading, axis, down)


def with_halo(array, sides, width):
    for axis, dim in sides:
        length = array.shape[dim]
        last = lax.slice_in_dim(array, length - width, length, axis=dim)
        leading = lax.slice_in_dim(array, 0, width, axis=dim)
        before, after = exchange(last, leading, axis)
        array = jnp.concatenate([before, array, after], axis=dim)
    return array


def thermal_step(ext, heat_rows, lateral, vertical):
    cols = jnp.pad(ext, ((0, 0), (0, 0), (1, 1)))
    center = ext[:, 1:-1]
    lap = ext[:, 2:] + ext[:, :-2] + cols[:, 1:-1, 2:] + cols[:, 1:-1, :-2] - 4.0 * center
    flux = vertical[:, None, None] * (center[1:] - center[:-1])
    vert = jnp.pad(flux, ((0, 1), (0, 0), (0, 0))) - jnp.pad(flux, ((1, 0), (0, 0), (0, 0)))
    return center + lateral[:, None, None] * lap + vert + heat_rows


def moment_of(field, weighting):
    total = weighting[0] * field[0]
    for layer in range(1, field.shape[0]):
        total = total + weighting[layer] * field[layer]
    return total


def sweep(w_pad, e_pad, load):
    center = e_pad[1:-1, 1:-1]
    e_up = 0.5 * (center + e_pad[:-2, 1:-1])
    e_down = 0.5 * (center + e_pad[2:, 1:-1])
    e_left = 0.5 * (center + e_pad[1:-1, :-2])
    e_right = 0.5 * (center + e_pad[1:-1, 2:])
    numer = (
        load
        + e_up * w_pad[:-2, 1:-1]
        + e_down * w_pad[2:, 1:-1]
        + e_left * w_pad[1:-1, :-2]
        + e_right * w_pad[1:-1, 2:]
    )
    denom = stiffness + e_up + e_down + e_left + e_right
    return numer / denom


def anand(strain, resist, recv):
    total, inelastic = (strain[0], strain[1])
    increment, theta, live = (recv[0], recv[1], recv[2])
    total_new = total + increment
    arrhen = jnp.exp(2.0 - 2.0 / (1.0 + 0.1 * theta * theta))
    hyper = jnp.sinh(shear_mod * (total_new - inelastic) / resist)
    rate = rate_scale * arrhen * hyper * jnp.abs(hyper)
    inelastic_new = inelastic + rate
    target = sat_level * jnp.power(1.0 + jnp.abs(rate) / arrhen, sat_power)
    resist_new = resist + harden * (1.0 - resist / target) * jnp.abs(rate)
    keep = live > 0.5
    strain_out = jnp.stack(
        [jnp.where(keep, total_new, total), jnp.where(keep, inelastic_new, inelastic)]
    )
    return (strain_out, jnp.where(keep, resist_new, resist))


def as_slab(piece, layers, cols):
    flat = piece.reshape(-1)
    per = layers * cols
    n = -(-flat.shape[0] // per)
    return jnp.pad(flat, (0, n * per - flat.shape[0])).reshape(n, layers, cols).transpose(1, 0, 2)


def from_slab(slab, shape):
    size = 1
    for d in shape:
        size *= d
    return slab.transpose(1, 0, 2).reshape(-1)[:size].reshape(shape)


def thermal(temp, heat, lateral, vertical, extra):
    devices = lax.axis_size(FLAT)
    t = lax.axis_index(FLAT)
    rows = temp.shape[1]
    h = STEPS + extra
    hh = h - 1
    last = jnp.concatenate([temp[:, rows - h:], heat[:, rows - hh:]], axis=1)
    leading = jnp.concatenate([temp[:, :h], heat[:, :hh]], axis=1)
    before, after = exchange(last.transpose(1, 0, 2), leading.transpose(1, 0, 2), FLAT)
    before, after = before.transpose(1, 0, 2), after.transpose(1, 0, 2)
    ext = jnp.concatenate([before[:, :h], temp, after[:, :h]], axis=1)
    heat_ext = jnp.concatenate([before[:, h:], heat, after[:, h:]], axis=1)
    for step in range(1, STEPS + 1):
        r = STEPS - step + extra
        heat_rows = heat_ext[:, hh - r: hh - r + rows + 2 * r]
        ext = thermal_step(ext, heat_rows, lateral, vertical)
        if step < STEPS:
            g = t * rows + jnp.arange(-r, rows + r)
            inside = (g >= 0) & (g < devices * rows)
            ext = jnp.where(inside[None, :, None], ext, 0.0)
    return ext


def relay(load, top, width, side_last, side_leading):
    n_gy = lax.axis_size("gy")
    gj = lax.axis_index("gy")
    rows, cols = load.shape
    cm = cols // n_gy
    rows = rows - 2 * width
    lp = jnp.pad(load, ((0, 0), (width, width)))
    tp = jnp.pad(top, ((width, width), (0, 0)))
    send = []
    for k in range(n_gy):
        main = jnp.stack([load[:, k * cm: (k + 1) * cm], tp[:, k * cm: (k + 1) * cm]])
        halo = jnp.concatenate(
            [lp[:, k * cm: k * cm + width], lp[:, (k + 1) * cm + width: (k + 1) * cm + 2 * width]],
            axis=1)
        send.append(jnp.concatenate([main, as_slab(halo, 2, cm)], axis=1))
    send = jnp.stack(send)
    depth = send.shape[2]
    full = load.shape[0]
    got = [lax.dynamic_index_in_dim(send, gj, 0, keepdims=False)]
    side_before = side_after = None
    for shift in range(1, n_gy):
        piece = lax.dynamic_index_in_dim(send, (gj + shift) % n_gy, 0, keepdims=False)
        extras = []
        if shift == 1:
            extras.append(as_slab(side_last, 2, piece.shape[2]))
        if shift == n_gy - 1:
            extras.append(as_slab(side_leading, 2, piece.shape[2]))
        piece = jnp.concatenate([piece] + extras, axis=1)
        moved = lax.ppermute(piece, "gy", [(j, (j + shift) % n_gy) for j in range(n_gy)])
        at = depth
        if shift == 1:
            slab = as_slab(side_last, 2, piece.shape[2])
            side_before = from_slab(moved[:, at: at + slab.shape[1]], side_last.shape)
            at += slab.shape[1]
        if shift == n_gy - 1:
            slab = as_slab(side_leading, 2, piece.shape[2])
            side_after = from_slab(moved[:, at: at + slab.shape[1]], side_leading.shape)
        got.append(moved[:, :depth])
    if side_before is None:
        side_before = jnp.zeros_like(side_last)
        side_after = jnp.zeros_like(side_leading)
    side_before = jnp.where(gj > 0, side_before, 0.0)
    side_after = jnp.where(gj < n_gy - 1, side_after, 0.0)
    recv = jnp.take(jnp.stack(got), (gj - jnp.arange(n_gy)) % n_gy, axis=0)
    parts = []
    for k in range(n_gy):
        halo = from_slab(recv[k, :, full:], (full, 2 * width))
        window = jnp.concatenate([halo[:, :width], recv[k, 0, :full], halo[:, width:]], axis=1)
        lo = 0 if k == 0 else width
        hi = rows + 2 * width if k == n_gy - 1 else rows + width
        parts.append(window[lo:hi])
    load_m = jnp.concatenate(parts, axis=0)
    top_m = jnp.concatenate([recv[k, 1, width: rows + width] for k in range(n_gy)], axis=0)
    return load_m, top_m, side_before, side_after


def joint_ranks(owners, devices):
    count = owners.shape[0]
    block = 128 if count % 128 == 0 else count
    nb = count // block
    onehot = (owners[:, None] == jnp.arange(devices, dtype=jnp.int32)[None, :]).astype(jnp.float32)
    oh = onehot.reshape(nb, block, devices)
    ar = jnp.arange(block)
    tri = (ar[:, None] >= ar[None, :]).astype(jnp.float32)
    within = jnp.einsum("ij,bjd->bid", tri, oh, precision=lax.Precision.HIGHEST)
    totals = within[:, -1, :]
    ab = jnp.arange(nb)
    stri = (ab[:, None] > ab[None, :]).astype(jnp.float32)
    offs = jnp.dot(stri, totals, precision=lax.Precision.HIGHEST)
    cum = (within + offs[:, None, :]).reshape(count, devices)
    return jnp.sum(cum * onehot, axis=1).astype(jnp.int32) - 1


def split3(x):
    hi = x.astype(jnp.bfloat16).astype(jnp.float32)
    rest = x - hi
    mid = rest.astype(jnp.bfloat16).astype(jnp.float32)
    return hi, mid, rest - mid


def joints_kernel(rows_ref, cols_ref, parts_ref, owners_ref, ranks_ref, out_ref):
    _, fields, rm, cm = parts_ref.shape
    count = rows_ref.shape[1]
    devices, cap = out_ref.shape[1:]
    block = 512 if count % 512 == 0 else count
    picked = []
    for b in range(count // block):
        rows = rows_ref[:, b * block: (b + 1) * block]
        cols = cols_ref[:, b * block: (b + 1) * block]
        hit = lax.broadcasted_iota(jnp.int32, (cm, block), 0) == cols
        onehot = jnp.where(hit, 1.0, 0.0).astype(jnp.bfloat16)
        sel = lax.broadcasted_iota(jnp.int32, (rm, block), 0) == rows
        got = []
        for f in range(fields):
            acc = jnp.dot(parts_ref[0, f], onehot, preferred_element_type=jnp.float32)
            acc = acc + jnp.dot(parts_ref[1, f], onehot, preferred_element_type=jnp.float32)
            acc = acc + jnp.dot(parts_ref[2, f], onehot, preferred_element_type=jnp.float32)
            got.append(jnp.sum(jnp.where(sel, acc, 0.0), axis=0, keepdims=True))
        picked.append(jnp.concatenate(got, axis=0))
    values = jnp.concatenate(picked, axis=1)
    mine = lax.broadcasted_iota(jnp.int32, (devices, count), 0) == owners_ref[...]
    slot = lax.broadcasted_iota(jnp.int32, (cap, count), 0) == ranks_ref[...]
    at = jnp.where(slot, 1.0, 0.0).astype(jnp.bfloat16)
    over_joints = (((1,), (1,)), ((), ()))
    split = split3(values)
    for f in range(fields):
        acc = None
        for part in split:
            spread = jnp.where(mine, part[f: f + 1, :], 0.0).astype(jnp.bfloat16)
            term = lax.dot_general(spread, at, over_joints, preferred_element_type=jnp.float32)
            acc = term if acc is None else acc + term
        out_ref[f] = acc
    live = jnp.where(mine, 1.0, 0.0).astype(jnp.bfloat16)
    out_ref[fields] = lax.dot_general(live, at, over_joints, preferred_element_type=jnp.float32)


def route_joints(fields, cells, owners, ranks, devices, cap):
    nf, rm, cm = fields.shape
    hi = lax.reduce_precision(fields, exponent_bits=8, mantissa_bits=7)
    rest = fields - hi
    mid = lax.reduce_precision(rest, exponent_bits=8, mantissa_bits=7)
    lo = rest - mid
    parts = jnp.stack([hi, mid, lo]).astype(jnp.bfloat16)
    return pl.pallas_call(
        joints_kernel,
        out_shape=jax.ShapeDtypeStruct((nf + 1, devices, cap), jnp.float32),
    )(
        (cells // cm).astype(jnp.int32)[None, :],
        (cells % cm).astype(jnp.int32)[None, :],
        parts,
        owners[None, :].astype(jnp.int32),
        ranks[None, :].astype(jnp.int32),
    )


def body(
    temp_start,
    heat_input,
    lateral,
    vertical,
    weighting,
    modulus,
    warp_prev,
    joint_cell,
    joint_owner,
    joint_strain,
    joint_resist,
):
    devices = lax.axis_size(FLAT)
    n_gx, n_gy = lax.axis_size("gx"), lax.axis_size("gy")
    gi, gj = lax.axis_index("gx"), lax.axis_index("gy")
    rm, cm = warp_prev.shape

    wm = jnp.stack([warp_prev, modulus])
    owners = joint_owner[:, 0]
    capacity = joint_resist.shape[1] // devices
    ranks = joint_ranks(owners, devices)

    extra = SWEEPS - 1
    g = SWEEPS
    wm = with_halo(wm, (("gx", 1),), g)
    temp = thermal(temp_start, heat_input, lateral, vertical, extra)
    load_t = moment_of(temp, weighting)
    load, top, left, right = relay(
        load_t, temp[-1, extra: temp.shape[1] - extra], extra, wm[:, :, cm - g:], wm[:, :, :g])
    wm = jnp.concatenate([left, wm, right], axis=2)

    warp = wm[0]
    mod_ext = wm[1]
    for step in range(1, SWEEPS + 1):
        r = SWEEPS - step
        off = SWEEPS - (r + 1)
        e_pad = mod_ext[off: off + rm + 2 * r + 2, off: off + cm + 2 * r + 2]
        lo = SWEEPS - 1 - r
        ld = load[lo: lo + rm + 2 * r, lo: lo + cm + 2 * r]
        warp = sweep(warp, e_pad, ld)
        if r > 0:
            gr = gi * rm + jnp.arange(-r, rm + r)
            gc = gj * cm + jnp.arange(-r, cm + r)
            inside = ((gr >= 0) & (gr < n_gx * rm))[:, None] & ((gc >= 0) & (gc < n_gy * cm))[None, :]
            warp = jnp.where(inside, warp, 0.0)

    outgoing = route_joints(
        jnp.stack([warp - warp_prev, top]), joint_cell, owners, ranks, devices, capacity)
    incoming = lax.all_to_all(outgoing, FLAT, split_axis=1, concat_axis=1, tiled=True)
    incoming = incoming.reshape(incoming.shape[0], devices * capacity)
    strain_next, resist_next = anand(joint_strain, joint_resist, incoming[:, None, :])
    return (warp, strain_next, resist_next)


def solution(mesh):
    return jax.shard_map(
        body,
        mesh=mesh,
        in_specs=(
            P(None, FLAT, None),
            P(None, FLAT, None),
            P(),
            P(),
            P(),
            P("gx", "gy"),
            P("gx", "gy"),
            P(FLAT),
            P(FLAT, None),
            P(None, FLAT, None),
            P(FLAT, None),
        ),
        out_specs=(P("gx", "gy"), P(None, FLAT, None), P(FLAT, None)),
        check_vma=False,
    )
```

```python
import jax
import jax.numpy as jnp
from jax import lax
from jax.sharding import PartitionSpec as P
from jax.experimental import pallas as pl

STEPS = 2
SWEEPS = 3


stiffness = 0.2
shear_mod = 0.6
rate_scale = 0.5
sat_level = 2.5
sat_power = 0.3
harden = 2.0

FLAT = ("gx", "gy")


def exchange(last, leading, axis):
    count = lax.axis_size(axis)
    up = [(i, i + 1) for i in range(count - 1)]
    down = [(j, i) for i, j in up]
    return lax.ppermute(last, axis, up), lax.ppermute(leading, axis, down)


def with_halo(array, sides, width):
    for axis, dim in sides:
        length = array.shape[dim]
        last = lax.slice_in_dim(array, length - width, length, axis=dim)
        leading = lax.slice_in_dim(array, 0, width, axis=dim)
        before, after = exchange(last, leading, axis)
        array = jnp.concatenate([before, array, after], axis=dim)
    return array


def thermal_step(ext, heat_rows, lateral, vertical):
    cols = jnp.pad(ext, ((0, 0), (0, 0), (1, 1)))
    center = ext[:, 1:-1]
    lap = ext[:, 2:] + ext[:, :-2] + cols[:, 1:-1, 2:] + cols[:, 1:-1, :-2] - 4.0 * center
    flux = vertical[:, None, None] * (center[1:] - center[:-1])
    vert = jnp.pad(flux, ((0, 1), (0, 0), (0, 0))) - jnp.pad(flux, ((1, 0), (0, 0), (0, 0)))
    return center + lateral[:, None, None] * lap + vert + heat_rows


def moment_of(field, weighting):
    total = weighting[0] * field[0]
    for layer in range(1, field.shape[0]):
        total = total + weighting[layer] * field[layer]
    return total


def sweep(w_pad, e_pad, load):
    center = e_pad[1:-1, 1:-1]
    e_up = 0.5 * (center + e_pad[:-2, 1:-1])
    e_down = 0.5 * (center + e_pad[2:, 1:-1])
    e_left = 0.5 * (center + e_pad[1:-1, :-2])
    e_right = 0.5 * (center + e_pad[1:-1, 2:])
    numer = (
        load
        + e_up * w_pad[:-2, 1:-1]
        + e_down * w_pad[2:, 1:-1]
        + e_left * w_pad[1:-1, :-2]
        + e_right * w_pad[1:-1, 2:]
    )
    denom = stiffness + e_up + e_down + e_left + e_right
    return numer / denom


def anand(strain, resist, recv):
    total, inelastic = (strain[0], strain[1])
    increment, theta, live = (recv[0], recv[1], recv[2])
    total_new = total + increment
    arrhen = jnp.exp(2.0 - 2.0 / (1.0 + 0.1 * theta * theta))
    hyper = jnp.sinh(shear_mod * (total_new - inelastic) / resist)
    rate = rate_scale * arrhen * hyper * jnp.abs(hyper)
    inelastic_new = inelastic + rate
    target = sat_level * jnp.power(1.0 + jnp.abs(rate) / arrhen, sat_power)
    resist_new = resist + harden * (1.0 - resist / target) * jnp.abs(rate)
    keep = live > 0.5
    strain_out = jnp.stack(
        [jnp.where(keep, total_new, total), jnp.where(keep, inelastic_new, inelastic)]
    )
    return (strain_out, jnp.where(keep, resist_new, resist))


def as_slab(piece, layers, cols):
    flat = piece.reshape(-1)
    per = layers * cols
    n = -(-flat.shape[0] // per)
    return jnp.pad(flat, (0, n * per - flat.shape[0])).reshape(n, layers, cols).transpose(1, 0, 2)


def from_slab(slab, shape):
    size = 1
    for d in shape:
        size *= d
    return slab.transpose(1, 0, 2).reshape(-1)[:size].reshape(shape)


def thermal(temp, heat, lateral, vertical, extra):
    devices = lax.axis_size(FLAT)
    t = lax.axis_index(FLAT)
    rows = temp.shape[1]
    h = STEPS + extra
    hh = h - 1
    last = jnp.concatenate([temp[:, rows - h:], heat[:, rows - hh:]], axis=1)
    leading = jnp.concatenate([temp[:, :h], heat[:, :hh]], axis=1)
    before, after = exchange(last, leading, FLAT)
    ext = jnp.concatenate([before[:, :h], temp, after[:, :h]], axis=1)
    heat_ext = jnp.concatenate([before[:, h:], heat, after[:, h:]], axis=1)
    for step in range(1, STEPS + 1):
        r = STEPS - step + extra
        heat_rows = heat_ext[:, hh - r: hh - r + rows + 2 * r]
        ext = thermal_step(ext, heat_rows, lateral, vertical)
        if step < STEPS:
            g = t * rows + jnp.arange(-r, rows + r)
            inside = (g >= 0) & (g < devices * rows)
            ext = jnp.where(inside[None, :, None], ext, 0.0)
    return ext


def relay(load, top, width, side_last, side_leading):
    n_gy = lax.axis_size("gy")
    gj = lax.axis_index("gy")
    rows, cols = load.shape
    cm = cols // n_gy
    rows = rows - 2 * width
    lp = jnp.pad(load, ((0, 0), (width, width)))
    full = load.shape[0]
    send = []
    for k in range(n_gy):
        halo = jnp.concatenate(
            [lp[:, k * cm: k * cm + width], lp[:, (k + 1) * cm + width: (k + 1) * cm + 2 * width]],
            axis=1)
        send.append(jnp.concatenate(
            [load[:, k * cm: (k + 1) * cm], top[:, k * cm: (k + 1) * cm], as_slab(halo, 1, cm)[0]],
            axis=0))
    send = jnp.stack(send)
    depth = send.shape[1]
    got = [lax.dynamic_index_in_dim(send, gj, 0, keepdims=False)]
    side_before = side_after = None
    for shift in range(1, n_gy):
        piece = lax.dynamic_index_in_dim(send, (gj + shift) % n_gy, 0, keepdims=False)
        extras = []
        if shift == 1:
            extras.append(as_slab(side_last, 1, cm)[0])
        if shift == n_gy - 1:
            extras.append(as_slab(side_leading, 1, cm)[0])
        piece = jnp.concatenate([piece] + extras, axis=0)
        moved = lax.ppermute(piece, "gy", [(j, (j + shift) % n_gy) for j in range(n_gy)])
        at = depth
        if shift == 1:
            n = as_slab(side_last, 1, cm).shape[1]
            side_before = from_slab(moved[None, at: at + n], side_last.shape)
            at += n
        if shift == n_gy - 1:
            n = as_slab(side_leading, 1, cm).shape[1]
            side_after = from_slab(moved[None, at: at + n], side_leading.shape)
        got.append(moved[:depth])
    if side_before is None:
        side_before = jnp.zeros_like(side_last)
        side_after = jnp.zeros_like(side_leading)
    side_before = jnp.where(gj > 0, side_before, 0.0)
    side_after = jnp.where(gj < n_gy - 1, side_after, 0.0)
    recv = jnp.take(jnp.stack(got), (gj - jnp.arange(n_gy)) % n_gy, axis=0)
    parts = []
    for k in range(n_gy):
        halo = from_slab(recv[k, None, full + rows:], (full, 2 * width))
        window = jnp.concatenate([halo[:, :width], recv[k, :full], halo[:, width:]], axis=1)
        lo = 0 if k == 0 else width
        hi = rows + 2 * width if k == n_gy - 1 else rows + width
        parts.append(window[lo:hi])
    load_m = jnp.concatenate(parts, axis=0)
    top_m = jnp.concatenate([recv[k, full: full + rows] for k in range(n_gy)], axis=0)
    return load_m, top_m, side_before, side_after


def joint_ranks(owners, devices):
    count = owners.shape[0]
    block = 128 if count % 128 == 0 else count
    nb = count // block
    onehot = (owners[:, None] == jnp.arange(devices, dtype=jnp.int32)[None, :]).astype(jnp.float32)
    oh = onehot.reshape(nb, block, devices)
    ar = jnp.arange(block)
    tri = (ar[:, None] >= ar[None, :]).astype(jnp.float32)
    within = jnp.einsum("ij,bjd->bid", tri, oh, precision=lax.Precision.HIGHEST)
    totals = within[:, -1, :]
    ab = jnp.arange(nb)
    stri = (ab[:, None] > ab[None, :]).astype(jnp.float32)
    offs = jnp.dot(stri, totals, precision=lax.Precision.HIGHEST)
    cum = (within + offs[:, None, :]).reshape(count, devices)
    return jnp.sum(cum * onehot, axis=1).astype(jnp.int32) - 1


def split3(x):
    hi = x.astype(jnp.bfloat16).astype(jnp.float32)
    rest = x - hi
    mid = rest.astype(jnp.bfloat16).astype(jnp.float32)
    return hi, mid, rest - mid


def joints_kernel(rows_ref, cols_ref, parts_ref, owners_ref, ranks_ref, out_ref):
    _, fields, rm, cm = parts_ref.shape
    count = rows_ref.shape[1]
    devices, cap = out_ref.shape[1:]
    block = 512 if count % 512 == 0 else count
    picked = []
    for b in range(count // block):
        rows = rows_ref[:, b * block: (b + 1) * block]
        cols = cols_ref[:, b * block: (b + 1) * block]
        hit = lax.broadcasted_iota(jnp.int32, (cm, block), 0) == cols
        onehot = jnp.where(hit, 1.0, 0.0).astype(jnp.bfloat16)
        sel = lax.broadcasted_iota(jnp.int32, (rm, block), 0) == rows
        got = []
        for f in range(fields):
            acc = jnp.dot(parts_ref[0, f], onehot, preferred_element_type=jnp.float32)
            acc = acc + jnp.dot(parts_ref[1, f], onehot, preferred_element_type=jnp.float32)
            acc = acc + jnp.dot(parts_ref[2, f], onehot, preferred_element_type=jnp.float32)
            got.append(jnp.sum(jnp.where(sel, acc, 0.0), axis=0, keepdims=True))
        picked.append(jnp.concatenate(got, axis=0))
    values = jnp.concatenate(picked, axis=1)
    mine = lax.broadcasted_iota(jnp.int32, (devices, count), 0) == owners_ref[...]
    slot = lax.broadcasted_iota(jnp.int32, (cap, count), 0) == ranks_ref[...]
    at = jnp.where(slot, 1.0, 0.0).astype(jnp.bfloat16)
    over_joints = (((1,), (1,)), ((), ()))
    split = split3(values)
    for f in range(fields):
        acc = None
        for part in split:
            spread = jnp.where(mine, part[f: f + 1, :], 0.0).astype(jnp.bfloat16)
            term = lax.dot_general(spread, at, over_joints, preferred_element_type=jnp.float32)
            acc = term if acc is None else acc + term
        out_ref[f] = acc
    live = jnp.where(mine, 1.0, 0.0).astype(jnp.bfloat16)
    out_ref[fields] = lax.dot_general(live, at, over_joints, preferred_element_type=jnp.float32)


def route_joints(fields, cells, owners, ranks, devices, cap):
    nf, rm, cm = fields.shape
    hi = lax.reduce_precision(fields, exponent_bits=8, mantissa_bits=7)
    rest = fields - hi
    mid = lax.reduce_precision(rest, exponent_bits=8, mantissa_bits=7)
    lo = rest - mid
    parts = jnp.stack([hi, mid, lo]).astype(jnp.bfloat16)
    return pl.pallas_call(
        joints_kernel,
        out_shape=jax.ShapeDtypeStruct((nf + 1, devices, cap), jnp.float32),
    )(
        (cells // cm).astype(jnp.int32)[None, :],
        (cells % cm).astype(jnp.int32)[None, :],
        parts,
        owners[None, :].astype(jnp.int32),
        ranks[None, :].astype(jnp.int32),
    )


def body(
    temp_start,
    heat_input,
    lateral,
    vertical,
    weighting,
    modulus,
    warp_prev,
    joint_cell,
    joint_owner,
    joint_strain,
    joint_resist,
):
    devices = lax.axis_size(FLAT)
    n_gx, n_gy = lax.axis_size("gx"), lax.axis_size("gy")
    gi, gj = lax.axis_index("gx"), lax.axis_index("gy")
    rm, cm = warp_prev.shape

    wm = jnp.stack([warp_prev, modulus])
    owners = joint_owner[:, 0]
    capacity = joint_resist.shape[1] // devices
    ranks = joint_ranks(owners, devices)

    extra = SWEEPS - 1
    g = SWEEPS
    wm = with_halo(wm, (("gx", 1),), g)
    temp = thermal(temp_start, heat_input, lateral, vertical, extra)
    load_t = moment_of(temp, weighting)
    load, top, left, right = relay(
        load_t, temp[-1, extra: temp.shape[1] - extra], extra, wm[:, :, cm - g:], wm[:, :, :g])
    wm = jnp.concatenate([left, wm, right], axis=2)

    warp = wm[0]
    mod_ext = wm[1]
    for step in range(1, SWEEPS + 1):
        r = SWEEPS - step
        off = SWEEPS - (r + 1)
        e_pad = mod_ext[off: off + rm + 2 * r + 2, off: off + cm + 2 * r + 2]
        lo = SWEEPS - 1 - r
        ld = load[lo: lo + rm + 2 * r, lo: lo + cm + 2 * r]
        warp = sweep(warp, e_pad, ld)
        if r > 0:
            gr = gi * rm + jnp.arange(-r, rm + r)
            gc = gj * cm + jnp.arange(-r, cm + r)
            inside = ((gr >= 0) & (gr < n_gx * rm))[:, None] & ((gc >= 0) & (gc < n_gy * cm))[None, :]
            warp = jnp.where(inside, warp, 0.0)

    outgoing = route_joints(
        jnp.stack([warp - warp_prev, top]), joint_cell, owners, ranks, devices, capacity)
    incoming = lax.all_to_all(outgoing, FLAT, split_axis=1, concat_axis=1, tiled=True)
    incoming = incoming.reshape(incoming.shape[0], devices * capacity)
    strain_next, resist_next = anand(joint_strain, joint_resist, incoming[:, None, :])
    return (warp, strain_next, resist_next)


def solution(mesh):
    return jax.shard_map(
        body,
        mesh=mesh,
        in_specs=(
            P(None, FLAT, None),
            P(None, FLAT, None),
            P(),
            P(),
            P(),
            P("gx", "gy"),
            P("gx", "gy"),
            P(FLAT),
            P(FLAT, None),
            P(None, FLAT, None),
            P(FLAT, None),
        ),
        out_specs=(P("gx", "gy"), P(None, FLAT, None), P(FLAT, None)),
        check_vma=False,
    )
```
